32 devices in a mesh: groups: 2 (over x), dp: 4 (over y, core), tensor: 4 (over z).
Axes of the slice: x: 2, y: 2, z: 4, core: 2. Of those that a mesh axis runs over, the one named last changes fastest.
Arguments:
- queries: bfloat16 [64, 64, 8192], P(('groups', 'dp'), None, 'tensor'), parts along dimension 0, may hold values from -5 to 5
- suffix_kv: bfloat16 [64, 2, 64, 1024], P(('groups', 'dp'), None, None, 'tensor'), parts along dimension 0, may hold values from -5 to 5
- out_grad: bfloat16 [64, 64, 8192], P(('groups', 'dp'), None, 'tensor'), parts along dimension 0, may hold values from -12 to 12
- prefix_kv: bfloat16 [8, 2, 448, 1024], P(('groups', 'dp'), None, None, 'tensor'), parts along dimension 0, may hold values from -5 to 5
- logratio: float32 [64], P(('groups', 'dp')), parts along dimension 0, may hold values from -8 to 8
- pair_slots: int32 [32, 2], P(('groups', 'dp')), parts along dimension 0, may hold values from 0 to 7, as said below
- pair_goal: int32 [32, 1], P(('groups', 'dp')), parts along dimension 0, may hold values from 0 to 3, as said below
- prefix_len: int32 [8], P('groups'), parts along dimension 0, may hold values from 1 to 448, 896 in all
Outputs:
- query_grad: bfloat16 [64, 64, 8192], P(('groups', 'dp'), None, 'tensor'), parts along dimension 0
- suffix_kv_grad: bfloat16 [64, 2, 64, 1024], P(('groups', 'dp'), None, None, 'tensor'), parts along dimension 0
- prefix_kv_grad: bfloat16 [8, 2, 448, 1024], P(('groups', 'dp'), None, None, 'tensor'), parts along dimension 0
The draws below stay inside these ranges and needn't reach their ends.
There are 2 independent parts, one for each index of `groups`. The reference program is written for one: setup_inputs(seed, part) draws one part's arguments, and reference() takes and returns one part's arrays. A program takes and returns all parts, laid end to end along the dimension named above; each array names one. Nothing has to cross between parts.
Inputs may be any that keep to these rules, and one draw needn't show every extreme that they name: `pair_slots`: within the 4 rows of one owner, the two columns together name each of that owner's 8 suffixes exactly once. `pair_goal`: within the 4 rows of one owner no goal appears twice; in every draw one goal receives exactly one pair from every owner. `prefix_len`: the lengths sum to 896.
All inputs are finite; a program needn't handle non-finite values.
Results may differ from the reference program's by a relative error of at most 0.007.
Values may be sent and summed in bfloat16 or wider, within the bound.
No kernel may reach another device: no remote copies, remote signals or barrier semaphores. Data moves between devices by JAX's collectives and lax.ppermute only.
A program may use at most 128 MiB of HBM per device.

```python
import math
import jax
import jax.numpy as jnp
import numpy as np
from jax import lax

H = 64
KVH = 8
HD = 128
SLEN = 64
PMAX = 448
PAIRS_DEV = 4
SUF_DEV = 8
CAP_P = 1
GOALS = 4
PAIRS = 16
SUFFIXES = 32


def draw_queries(key, part):
    shape = (SUFFIXES, SLEN, H, HD)
    drawn = jnp.clip(jax.random.normal(jax.random.fold_in(key, 13), shape, jnp.float32), -5.0, 5.0)
    return drawn.reshape(SUFFIXES, SLEN, H * HD).astype(jnp.bfloat16)


def draw_suffix_kv(key, part):
    shape = (SUFFIXES, 2, SLEN, KVH * HD)
    drawn = jnp.clip(jax.random.normal(jax.random.fold_in(key, 22), shape, jnp.float32), -5.0, 5.0)
    return drawn.astype(jnp.bfloat16)


def draw_pair_slots(key, part):
    owner_keys = jax.random.split(jax.random.fold_in(key, 31), PAIRS // PAIRS_DEV)
    shuffled = jax.vmap(lambda owner_key: jax.random.permutation(owner_key, SUF_DEV))(owner_keys)
    return shuffled.reshape(PAIRS, 2).astype(jnp.int32)


def draw_pair_goal(key, part):
    heavy_key, block_key = jax.random.split(jax.random.fold_in(key, 41))
    heavy = jax.random.randint(heavy_key, (), 0, GOALS)
    others = (heavy + 1 + jnp.arange((GOALS - 1) * CAP_P) // CAP_P) % GOALS

    def owner_rows(owner_key):
        first_key, second_key = jax.random.split(owner_key)
        mixed = jax.random.permutation(first_key, others)
        rows_all = jnp.concatenate([jnp.full((CAP_P,), heavy, jnp.int32), mixed[:PAIRS_DEV - CAP_P].astype(jnp.int32)])
        return jax.random.permutation(second_key, rows_all)
    blocks = jax.vmap(owner_rows)(jax.random.split(block_key, PAIRS // PAIRS_DEV))
    return blocks.reshape(PAIRS, 1).astype(jnp.int32)


def level_of(stream_key, extent, shards, smallest, largest):
    factor_of, own = 1.0, jax.random.fold_in(stream_key, 6)
    for position, shards_of in shards:
        heights = jnp.exp(jax.random.uniform(jax.random.fold_in(own, position), (shards_of,), jnp.float32, smallest / len(shards), largest / len(shards)))
        factor_of = factor_of * jnp.repeat(heights, extent[position] // shards_of).reshape([-1 if axis == position else 1 for axis in range(len(extent))])
    return factor_of


def profile(amount, total, most, lean):
    weights = [(1 << 20) // math.isqrt(rank ** lean) + 1 for rank in range(2, amount + 1)]
    rest, holding = total - most - (amount - 1), [1] * (amount - 1)
    while rest > 0:
        candidates = [i for i in range(amount - 1) if holding[i] < most]
        whole, budget = sum([weights[i] for i in candidates]), rest
        for i in candidates:
            extra = min(most - holding[i], max(1, budget * weights[i] // whole), rest)
            holding[i] = holding[i] + extra
            rest = rest - extra
    return np.array([most] + holding)


def ragged(own_key, amount, total, bound, slope):
    if amount == 2:
        one = jax.random.randint(own_key, (), max(1, total - bound), min(bound, total - 1) + 1)
        return jnp.stack([one, total - one])
    sizes = jnp.asarray(profile(amount, total, bound, slope), jnp.int32)
    twos = (amount - 1) // 2
    giver, sink = sizes[1:1 + 2 * twos:2], sizes[2:2 + 2 * twos:2]
    room = jnp.minimum(giver - 1, bound - sink)
    passed = jax.random.randint(jax.random.fold_in(own_key, 1), (twos,), 0, 1 << 20) % (room + 1)
    sizes = sizes.at[1:1 + 2 * twos:2].set(giver - passed).at[2:2 + 2 * twos:2].set(sink + passed)
    return sizes[jax.random.permutation(jax.random.fold_in(own_key, 2), amount)]


def centred(own_key, dims, width, limit, cuts=(), kind=jnp.bfloat16):
    result = width * jax.random.normal(own_key, dims, jnp.float32)
    if cuts:
        result = result * level_of(own_key, dims, cuts, -0.22, 0.18)
    return jnp.clip(result, -limit, limit).astype(kind)


def setup_inputs(seed: int = 0, part: int = 0) -> dict:
    seeds = jax.random.split(jax.random.key(seed), 9)
    part_keys = jax.random.split(jax.random.fold_in(seeds[8], part), 9)
    return {
        "queries": draw_queries(jax.random.fold_in(jax.random.fold_in(seeds[8], part), 71), part),
        "suffix_kv": draw_suffix_kv(jax.random.fold_in(jax.random.fold_in(seeds[8], part), 71), part),
        "out_grad": centred(part_keys[2], (SUFFIXES, SLEN, H * HD), 2.0, 12.0, ((0, 4), (2, 4))),
        "prefix_kv": centred(part_keys[3], (GOALS, 2, PMAX, KVH * HD), 1.0, 5.0, ((0, 4), (3, 4))),
        "logratio": centred(part_keys[4], (SUFFIXES,), 2.0, 8.0, ((0, 4),), jnp.float32),
        "pair_slots": draw_pair_slots(jax.random.fold_in(jax.random.fold_in(seeds[8], part), 71), part),
        "pair_goal": draw_pair_goal(jax.random.fold_in(jax.random.fold_in(seeds[8], part), 71), part),
        "prefix_len": ragged(part_keys[7], GOALS, GOALS * PMAX // 2, PMAX, 2).astype(jnp.int32),
    }


dpo_beta = 0.5


def attend(query, keys_own, values_own, cotangent, keys_pre, values_pre, length, score_scale):
    all_keys = jnp.concatenate([keys_pre, keys_own], 0).astype(jnp.float32)
    all_values = jnp.concatenate([values_pre, values_own], 0).astype(jnp.float32)
    query_f = query.astype(jnp.float32)
    scores = jnp.einsum("tkgd,skd->kgts", query_f, all_keys) * score_scale
    prefix_rows = keys_pre.shape[0]
    key_index = jnp.arange(all_keys.shape[0])[None, :]
    query_index = jnp.arange(query.shape[0])[:, None]
    allowed = jnp.where(key_index < prefix_rows, key_index < length, key_index - prefix_rows <= query_index)
    scores = jnp.where(allowed, scores, -1e30)
    row_max = jnp.max(scores, -1, keepdims=True)
    raised = jnp.exp(scores - row_max)
    probability = raised / jnp.sum(raised, -1, keepdims=True)
    probability_low = lax.optimization_barrier(probability.astype(jnp.bfloat16)).astype(jnp.float32)
    output = jnp.einsum("kgts,skd->tkgd", probability_low, all_values)
    cotangent_f = lax.optimization_barrier(cotangent).astype(jnp.float32)
    row_dot = jnp.einsum("tkgd,tkgd->kgt", cotangent_f, output)
    grad_prob = jnp.einsum("tkgd,skd->kgts", cotangent_f, all_values)
    grad_score = (probability * (grad_prob - row_dot[..., None])).astype(jnp.bfloat16)
    grad_score_f = lax.optimization_barrier(grad_score).astype(jnp.float32)
    grad_query = (score_scale * jnp.einsum("kgts,skd->tkgd", grad_score_f, all_keys)).astype(jnp.bfloat16)
    grad_keys = score_scale * jnp.einsum("kgts,tkgd->skd", grad_score_f, query_f)
    grad_values = jnp.einsum("kgts,tkgd->skd", probability_low, cotangent_f)
    return grad_query, grad_keys, grad_values


def reference(queries, suffix_kv, out_grad, prefix_kv, logratio, pair_slots, pair_goal, prefix_len):
    group_size = H // KVH
    score_scale = HD ** -0.5
    owner_base = (jnp.arange(PAIRS) // PAIRS_DEV * SUF_DEV).astype(jnp.int32)
    chosen = (pair_slots[:, 0] + owner_base).astype(jnp.int32)
    rejected = (pair_slots[:, 1] + owner_base).astype(jnp.int32)
    pair_goals = pair_goal[:, 0].astype(jnp.int32)
    suffix_goal = jnp.zeros((SUFFIXES,), jnp.int32).at[chosen].set(pair_goals).at[rejected].set(pair_goals)
    weight = dpo_beta * jax.nn.sigmoid(-dpo_beta * (logratio[chosen] - logratio[rejected]))
    coefficient = jnp.zeros((SUFFIXES,), jnp.float32).at[chosen].set(-weight).at[rejected].set(weight)
    cotangent = (coefficient[:, None, None] * out_grad.astype(jnp.float32)).astype(jnp.bfloat16)

    def per_suffix(carry, index):
        goal = suffix_goal[index]
        goal_kv = lax.dynamic_index_in_dim(prefix_kv, goal, 0, keepdims=False)
        one_query = queries[index].reshape(SLEN, KVH, group_size, HD)
        one_kv = suffix_kv[index]
        one_cot = cotangent[index].reshape(SLEN, KVH, group_size, HD)
        grad_query, grad_keys, grad_values = attend(
            one_query, one_kv[0].reshape(SLEN, KVH, HD), one_kv[1].reshape(SLEN, KVH, HD), one_cot,
            goal_kv[0].reshape(PMAX, KVH, HD), goal_kv[1].reshape(PMAX, KVH, HD), prefix_len[goal], score_scale)
        prefix_part = jnp.stack([grad_keys[:PMAX], grad_values[:PMAX]], 0).reshape(2, PMAX, KVH * HD)
        own_part = jnp.stack([grad_keys[PMAX:], grad_values[PMAX:]], 0).astype(jnp.bfloat16).reshape(2, SLEN, KVH * HD)
        current = lax.dynamic_index_in_dim(carry, goal, 0, keepdims=False)
        carry = lax.dynamic_update_index_in_dim(carry, current + prefix_part, goal, 0)
        return carry, (grad_query.reshape(SLEN, H * HD), own_part)

    initial = jnp.zeros((GOALS, 2, PMAX, KVH * HD), jnp.float32)
    prefix_sum, (query_grad, kv_grad) = lax.scan(per_suffix, initial, jnp.arange(SUFFIXES, dtype=jnp.int32))
    return query_grad, kv_grad, prefix_sum.astype(jnp.bfloat16)
```

```python
import functools

import jax
import jax.numpy as jnp
from jax import lax
from jax.experimental import pallas as pl
from jax.experimental.pallas import tpu as pltpu
from jax.sharding import PartitionSpec as P

HD = 128

dpo_beta = 0.5


def attend_kernel(slots_ref, goal_ref, len_ref, coef_ref,
                  q_ref, og_ref, skv_ref, pkv_ref,
                  dq_ref, dkv_ref, dpre_ref, *, group, seq, prefix_rows):
    p = pl.program_id(0)
    member = pl.program_id(2)
    s = slots_ref[2 * p + member]
    goal = goal_ref[p]
    length = len_ref[goal]
    coef = coef_ref[s]
    scale = HD ** (-0.5)
    keys_all = prefix_rows + seq
    rows = group * seq

    q_blk = q_ref[0]
    og_blk = og_ref[0]
    cot_blk = (coef * og_blk.astype(jnp.float32)).astype(jnp.bfloat16)
    q_rows = jnp.concatenate([q_blk[:, g * HD:(g + 1) * HD] for g in range(group)], 0)
    c_rows = jnp.concatenate([cot_blk[:, g * HD:(g + 1) * HD] for g in range(group)], 0)
    keys = jnp.concatenate([pkv_ref[0, 0], skv_ref[0, 0]], 0)
    values = jnp.concatenate([pkv_ref[0, 1], skv_ref[0, 1]], 0)

    nt = (((1,), (1,)), ((), ()))
    tn = (((0,), (0,)), ((), ()))
    scores = lax.dot_general(q_rows, keys, nt, preferred_element_type=jnp.float32) * scale
    key_index = lax.broadcasted_iota(jnp.int32, (rows, keys_all), 1)
    tok_index = lax.broadcasted_iota(jnp.int32, (rows, keys_all), 0) % seq
    in_prefix = key_index < prefix_rows
    allowed = (in_prefix & (key_index < length)) | (
        jnp.logical_not(in_prefix) & (key_index - prefix_rows <= tok_index))
    scores = jnp.where(allowed, scores, -1e30)
    row_max = jnp.max(scores, -1, keepdims=True)
    raised = jnp.exp(scores - row_max)
    prob = raised / jnp.sum(raised, -1, keepdims=True)
    prob_low = prob.astype(jnp.bfloat16)
    output = jnp.dot(prob_low, values, preferred_element_type=jnp.float32)
    row_dot = jnp.sum(c_rows.astype(jnp.float32) * output, -1, keepdims=True)
    grad_prob = lax.dot_general(c_rows, values, nt, preferred_element_type=jnp.float32)
    grad_score = (prob * (grad_prob - row_dot)).astype(jnp.bfloat16)
    grad_q = (scale * jnp.dot(grad_score, keys, preferred_element_type=jnp.float32)).astype(jnp.bfloat16)
    grad_k = scale * lax.dot_general(grad_score, q_rows, tn, preferred_element_type=jnp.float32)
    grad_v = lax.dot_general(prob_low, c_rows, tn, preferred_element_type=jnp.float32)

    for g in range(group):
        dq_ref[0, :, g * HD:(g + 1) * HD] = grad_q[g * seq:(g + 1) * seq]
    dkv_ref[0, 0] = grad_k[prefix_rows:].astype(jnp.bfloat16)
    dkv_ref[0, 1] = grad_v[prefix_rows:].astype(jnp.bfloat16)

    @pl.when(member == 0)
    def _():
        dpre_ref[0, 0] = grad_k[:prefix_rows]
        dpre_ref[0, 1] = grad_v[:prefix_rows]

    @pl.when(member != 0)
    def _():
        dpre_ref[0, 0] += grad_k[:prefix_rows]
        dpre_ref[0, 1] += grad_v[:prefix_rows]


def attend_all(slots, goals, lengths, coef, queries, out_grad, suffix_kv, prefix_all):
    suffix_count, seq, qwidth = queries.shape
    kv_width = suffix_kv.shape[-1]
    kv_local = kv_width // HD
    group = qwidth // kv_width
    goal_count, _, prefix_rows, _ = prefix_all.shape
    pair_count = goals.shape[0]
    qb = group * HD

    def q_map(p, k, m, slots_ref, goal_ref, len_ref):
        return (slots_ref[2 * p + m], 0, k)

    def skv_map(p, k, m, slots_ref, goal_ref, len_ref):
        return (slots_ref[2 * p + m], 0, 0, k)

    def pkv_map(p, k, m, slots_ref, goal_ref, len_ref):
        return (goal_ref[p], 0, 0, k)

    kernel = functools.partial(attend_kernel, group=group, seq=seq, prefix_rows=prefix_rows)
    out_shape = (
        jax.ShapeDtypeStruct((suffix_count, seq, qwidth), jnp.bfloat16),
        jax.ShapeDtypeStruct((suffix_count, 2, seq, kv_width), jnp.bfloat16),
        jax.ShapeDtypeStruct((goal_count, 2, prefix_rows, kv_width), jnp.float32),
    )
    in_specs = [
        pl.BlockSpec(memory_space=pltpu.SMEM),
        pl.BlockSpec((1, seq, qb), q_map),
        pl.BlockSpec((1, seq, qb), q_map),
        pl.BlockSpec((1, 2, seq, HD), skv_map),
        pl.BlockSpec((1, 2, prefix_rows, HD), pkv_map),
    ]
    operands = [coef, queries, out_grad, suffix_kv, prefix_all]
    aliases = {}
    if pair_count < goal_count:
        in_specs.append(pl.BlockSpec(memory_space=pl.ANY))
        operands.append(jnp.zeros(out_shape[2].shape, jnp.float32))
        aliases = {3 + len(operands) - 1: 2}

        def kernel_with_zero(*refs):
            return kernel(*refs[:8], *refs[9:])
        body = kernel_with_zero
    else:
        body = kernel
    grid_spec = pltpu.PrefetchScalarGridSpec(
        num_scalar_prefetch=3,
        grid=(pair_count, kv_local, 2),
        in_specs=in_specs,
        out_specs=[
            pl.BlockSpec((1, seq, qb), q_map),
            pl.BlockSpec((1, 2, seq, HD), skv_map),
            pl.BlockSpec((1, 2, prefix_rows, HD), pkv_map),
        ],
    )
    return pl.pallas_call(
        body,
        grid_spec=grid_spec,
        out_shape=out_shape,
        input_output_aliases=aliases,
        compiler_params=pltpu.CompilerParams(
            dimension_semantics=("arbitrary", "arbitrary", "arbitrary")),
    )(slots, goals, lengths, *operands)


def shards(queries, suffix_kv, out_grad, prefix_kv, logratio, pair_slots, pair_goal, prefix_len):
    suffix_count = queries.shape[0]
    chosen = pair_slots[:, 0]
    rejected = pair_slots[:, 1]
    positions = jnp.arange(suffix_count)
    pick_chosen = chosen[:, None] == positions[None, :]
    pick_rejected = rejected[:, None] == positions[None, :]
    ratio_chosen = jnp.sum(jnp.where(pick_chosen, logratio[None, :], 0.0), 1)
    ratio_rejected = jnp.sum(jnp.where(pick_rejected, logratio[None, :], 0.0), 1)
    weight = dpo_beta * jax.nn.sigmoid(-dpo_beta * (ratio_chosen - ratio_rejected))
    coefficient = jnp.sum(
        jnp.where(pick_rejected, weight[:, None], 0.0)
        - jnp.where(pick_chosen, weight[:, None], 0.0),
        0,
    )
    slots = pair_slots.reshape(-1).astype(jnp.int32)
    goals = pair_goal[:, 0].astype(jnp.int32)
    prefix_all = lax.all_gather(prefix_kv, "dp", axis=0, tiled=True)
    grad_q, grad_kv, partial = attend_all(
        slots, goals, prefix_len.astype(jnp.int32), coefficient,
        queries, out_grad, suffix_kv, prefix_all)
    prefix_grad = lax.psum_scatter(partial, "dp", scatter_dimension=0, tiled=True)
    return grad_q, grad_kv, prefix_grad.astype(jnp.bfloat16)


def solution(mesh):
    return jax.shard_map(
        shards,
        mesh=mesh,
        in_specs=(
            P(("groups", "dp"), None, "tensor"),
            P(("groups", "dp"), None, None, "tensor"),
            P(("groups", "dp"), None, "tensor"),
            P(("groups", "dp"), None, None, "tensor"),
            P(("groups", "dp")),
            P(("groups", "dp"), None),
            P(("groups", "dp"), None),
            P("groups"),
        ),
        out_specs=(
            P(("groups", "dp"), None, "tensor"),
            P(("groups", "dp"), None, None, "tensor"),
            P(("groups", "dp"), None, None, "tensor"),
        ),
        check_vma=False,
    )
```

```python
import functools

import jax
import jax.numpy as jnp
from jax import lax
from jax.experimental import pallas as pl
from jax.experimental.pallas import tpu as pltpu
from jax.sharding import PartitionSpec as P

HD = 128

dpo_beta = 0.5


def attend_math(q_blk, og_blk, keys_pre, values_pre, keys_own, values_own, length, coef,
                *, group, seq, prefix_rows):
    scale = HD ** (-0.5)
    keys_all = prefix_rows + seq
    rows = group * seq
    cot_blk = (coef * og_blk.astype(jnp.float32)).astype(jnp.bfloat16)
    q_rows = jnp.concatenate([q_blk[:, g * HD:(g + 1) * HD] for g in range(group)], 0)
    c_rows = jnp.concatenate([cot_blk[:, g * HD:(g + 1) * HD] for g in range(group)], 0)
    keys = jnp.concatenate([keys_pre, keys_own], 0)
    values = jnp.concatenate([values_pre, values_own], 0)

    nt = (((1,), (1,)), ((), ()))
    tn = (((0,), (0,)), ((), ()))
    scores = lax.dot_general(q_rows, keys, nt, preferred_element_type=jnp.float32) * scale
    key_index = lax.broadcasted_iota(jnp.int32, (rows, keys_all), 1)
    tok_index = lax.broadcasted_iota(jnp.int32, (rows, keys_all), 0) % seq
    in_prefix = key_index < prefix_rows
    allowed = (in_prefix & (key_index < length)) | (
        jnp.logical_not(in_prefix) & (key_index - prefix_rows <= tok_index))
    scores = jnp.where(allowed, scores, -1e30)
    row_max = jnp.max(scores, -1, keepdims=True)
    raised = jnp.exp(scores - row_max)
    prob = raised / jnp.sum(raised, -1, keepdims=True)
    prob_low = prob.astype(jnp.bfloat16)
    output = jnp.dot(prob_low, values, preferred_element_type=jnp.float32)
    row_dot = jnp.sum(c_rows.astype(jnp.float32) * output, -1, keepdims=True)
    grad_prob = lax.dot_general(c_rows, values, nt, preferred_element_type=jnp.float32)
    grad_score = (prob * (grad_prob - row_dot)).astype(jnp.bfloat16)
    grad_q = (scale * jnp.dot(grad_score, keys, preferred_element_type=jnp.float32)).astype(jnp.bfloat16)
    grad_k = scale * lax.dot_general(grad_score, q_rows, tn, preferred_element_type=jnp.float32)
    grad_v = lax.dot_general(prob_low, c_rows, tn, preferred_element_type=jnp.float32)
    return grad_q, grad_k, grad_v


def store_grads(grad_q, grad_k, grad_v, member, dq_ref, dkv_ref, dpre_ref, *, group, seq, prefix_rows):
    for g in range(group):
        dq_ref[0, :, g * HD:(g + 1) * HD] = grad_q[g * seq:(g + 1) * seq]
    dkv_ref[0, 0] = grad_k[prefix_rows:].astype(jnp.bfloat16)
    dkv_ref[0, 1] = grad_v[prefix_rows:].astype(jnp.bfloat16)

    @pl.when(member == 0)
    def _():
        dpre_ref[0, 0] = grad_k[:prefix_rows]
        dpre_ref[0, 1] = grad_v[:prefix_rows]

    @pl.when(member != 0)
    def _():
        dpre_ref[0, 0] += grad_k[:prefix_rows]
        dpre_ref[0, 1] += grad_v[:prefix_rows]


def attend_kernel(slots_ref, goal_ref, len_ref, coef_ref,
                  q_ref, og_ref, skv_ref, pkv_ref,
                  dq_ref, dkv_ref, dpre_ref, *, group, seq, prefix_rows):
    p = pl.program_id(0)
    member = pl.program_id(2)
    s = slots_ref[2 * p + member]
    length = len_ref[goal_ref[p]]
    dims = dict(group=group, seq=seq, prefix_rows=prefix_rows)
    grads = attend_math(q_ref[0], og_ref[0], pkv_ref[0, 0], pkv_ref[0, 1], skv_ref[0, 0], skv_ref[0, 1],
                        length, coef_ref[s], **dims)
    store_grads(*grads, member, dq_ref, dkv_ref, dpre_ref, **dims)


def slot_kernel(sidx_ref, len_ref, coef_ref, q_ref, og_ref, skv_ref, pkv_ref, *rest,
                group, seq, prefix_rows, chained):
    if chained:
        rest = rest[2:]
    dq_ref, dkv_ref, dpre_ref = rest
    member = pl.program_id(1)
    dims = dict(group=group, seq=seq, prefix_rows=prefix_rows)
    grads = attend_math(q_ref[0], og_ref[0], pkv_ref[0, 0], pkv_ref[0, 1], skv_ref[0, 0], skv_ref[0, 1],
                        len_ref[0], coef_ref[member], **dims)
    store_grads(*grads, member, dq_ref, dkv_ref, dpre_ref, **dims)


def attend_slot(sidx, length, coef, queries, out_grad, suffix_kv, prefix_one, chain):
    suffix_count, seq, qwidth = queries.shape
    kv_width = suffix_kv.shape[-1]
    kv_local = kv_width // HD
    group = qwidth // kv_width
    prefix_rows = prefix_one.shape[2]
    qb = group * HD

    def q_map(k, m, sidx_ref):
        return (sidx_ref[m], 0, k)

    def skv_map(k, m, sidx_ref):
        return (sidx_ref[m], 0, 0, k)

    def pkv_map(k, m, sidx_ref):
        return (0, 0, 0, k)

    out_shape = (
        jax.ShapeDtypeStruct((suffix_count, seq, qwidth), jnp.bfloat16),
        jax.ShapeDtypeStruct((suffix_count, 2, seq, kv_width), jnp.bfloat16),
        jax.ShapeDtypeStruct((1, 2, prefix_rows, kv_width), jnp.float32),
    )
    in_specs = [
        pl.BlockSpec(memory_space=pltpu.SMEM),
        pl.BlockSpec(memory_space=pltpu.SMEM),
        pl.BlockSpec((1, seq, qb), q_map),
        pl.BlockSpec((1, seq, qb), q_map),
        pl.BlockSpec((1, 2, seq, HD), skv_map),
        pl.BlockSpec((1, 2, prefix_rows, HD), pkv_map),
    ]
    operands = [length, coef, queries, out_grad, suffix_kv, prefix_one]
    aliases = {}
    if chain is not None:
        in_specs += [pl.BlockSpec(memory_space=pl.ANY)] * 2
        operands += list(chain)
        aliases = {7: 0, 8: 1}
    kernel = functools.partial(slot_kernel, group=group, seq=seq, prefix_rows=prefix_rows,
                               chained=chain is not None)
    grid_spec = pltpu.PrefetchScalarGridSpec(
        num_scalar_prefetch=1,
        grid=(kv_local, 2),
        in_specs=in_specs,
        out_specs=[
            pl.BlockSpec((1, seq, qb), q_map),
            pl.BlockSpec((1, 2, seq, HD), skv_map),
            pl.BlockSpec((1, 2, prefix_rows, HD), pkv_map),
        ],
    )
    steps = 2 * kv_local
    cost = pl.CostEstimate(
        flops=steps * 2_200_000_000,
        transcendentals=steps * group * seq * (prefix_rows + seq),
        bytes_accessed=steps * (4 * seq * qb + 4 * seq * HD + 6 * prefix_rows * HD) * 2,
    )
    return pl.pallas_call(
        kernel,
        grid_spec=grid_spec,
        out_shape=out_shape,
        input_output_aliases=aliases,
        cost_estimate=cost,
        compiler_params=pltpu.CompilerParams(dimension_semantics=("arbitrary", "arbitrary")),
    )(sidx, *operands)


def attend_all(slots, goals, lengths, coef, queries, out_grad, suffix_kv, prefix_all):
    suffix_count, seq, qwidth = queries.shape
    kv_width = suffix_kv.shape[-1]
    kv_local = kv_width // HD
    group = qwidth // kv_width
    goal_count, _, prefix_rows, _ = prefix_all.shape
    pair_count = goals.shape[0]
    qb = group * HD

    def q_map(p, k, m, slots_ref, goal_ref, len_ref):
        return (slots_ref[2 * p + m], 0, k)

    def skv_map(p, k, m, slots_ref, goal_ref, len_ref):
        return (slots_ref[2 * p + m], 0, 0, k)

    def pkv_map(p, k, m, slots_ref, goal_ref, len_ref):
        return (goal_ref[p], 0, 0, k)

    kernel = functools.partial(attend_kernel, group=group, seq=seq, prefix_rows=prefix_rows)
    out_shape = (
        jax.ShapeDtypeStruct((suffix_count, seq, qwidth), jnp.bfloat16),
        jax.ShapeDtypeStruct((suffix_count, 2, seq, kv_width), jnp.bfloat16),
        jax.ShapeDtypeStruct((goal_count, 2, prefix_rows, kv_width), jnp.float32),
    )
    in_specs = [
        pl.BlockSpec(memory_space=pltpu.SMEM),
        pl.BlockSpec((1, seq, qb), q_map),
        pl.BlockSpec((1, seq, qb), q_map),
        pl.BlockSpec((1, 2, seq, HD), skv_map),
        pl.BlockSpec((1, 2, prefix_rows, HD), pkv_map),
    ]
    operands = [coef, queries, out_grad, suffix_kv, prefix_all]
    aliases = {}
    if pair_count < goal_count:
        in_specs.append(pl.BlockSpec(memory_space=pl.ANY))
        operands.append(jnp.zeros(out_shape[2].shape, jnp.float32))
        aliases = {3 + len(operands) - 1: 2}

        def kernel_with_zero(*refs):
            return kernel(*refs[:8], *refs[9:])
        body = kernel_with_zero
    else:
        body = kernel
    grid_spec = pltpu.PrefetchScalarGridSpec(
        num_scalar_prefetch=3,
        grid=(pair_count, kv_local, 2),
        in_specs=in_specs,
        out_specs=[
            pl.BlockSpec((1, seq, qb), q_map),
            pl.BlockSpec((1, 2, seq, HD), skv_map),
            pl.BlockSpec((1, 2, prefix_rows, HD), pkv_map),
        ],
    )
    return pl.pallas_call(
        body,
        grid_spec=grid_spec,
        out_shape=out_shape,
        input_output_aliases=aliases,
        compiler_params=pltpu.CompilerParams(
            dimension_semantics=("arbitrary", "arbitrary", "arbitrary")),
    )(slots, goals, lengths, *operands)


def shards(queries, suffix_kv, out_grad, prefix_kv, logratio, pair_slots, pair_goal, prefix_len):
    suffix_count = queries.shape[0]
    chosen = pair_slots[:, 0]
    rejected = pair_slots[:, 1]
    positions = jnp.arange(suffix_count)
    pick_chosen = chosen[:, None] == positions[None, :]
    pick_rejected = rejected[:, None] == positions[None, :]
    ratio_chosen = jnp.sum(jnp.where(pick_chosen, logratio[None, :], 0.0), 1)
    ratio_rejected = jnp.sum(jnp.where(pick_rejected, logratio[None, :], 0.0), 1)
    weight = dpo_beta * jax.nn.sigmoid(-dpo_beta * (ratio_chosen - ratio_rejected))
    coefficient = jnp.sum(
        jnp.where(pick_rejected, weight[:, None], 0.0)
        - jnp.where(pick_chosen, weight[:, None], 0.0),
        0,
    )
    dp_size = lax.axis_size("dp")
    pair_count = pair_slots.shape[0]
    if dp_size == 4 and pair_count == dp_size:
        return pipelined(queries, suffix_kv, out_grad, prefix_kv, coefficient,
                         pair_slots, pair_goal, prefix_len)
    slots = pair_slots.reshape(-1).astype(jnp.int32)
    goals = pair_goal[:, 0].astype(jnp.int32)
    prefix_all = lax.all_gather(prefix_kv, "dp", axis=0, tiled=True)
    grad_q, grad_kv, partial = attend_all(
        slots, goals, prefix_len.astype(jnp.int32), coefficient,
        queries, out_grad, suffix_kv, prefix_all)
    prefix_grad = lax.psum_scatter(partial, "dp", scatter_dimension=0, tiled=True)
    return grad_q, grad_kv, prefix_grad.astype(jnp.bfloat16)


def pipelined(queries, suffix_kv, out_grad, prefix_kv, coefficient, pair_slots, pair_goal, prefix_len):
    me = lax.axis_index("dp")
    partner = [(i, i ^ 1) for i in range(4)]
    across = [(i, i ^ 2) for i in range(4)]
    pre_partner = lax.ppermute(prefix_kv, "dp", partner)
    pre_across = lax.ppermute(prefix_kv, "dp", across)
    pre_relay = lax.ppermute(pre_across, "dp", partner)
    pair_ids = jnp.arange(pair_slots.shape[0], dtype=jnp.int32)
    goals = pair_goal[:, 0].astype(jnp.int32)

    def slot_args(goal):
        pair = jnp.sum(jnp.where(goals == goal, pair_ids, 0))
        sidx = lax.dynamic_index_in_dim(pair_slots, pair, 0, keepdims=False).astype(jnp.int32)
        length = lax.dynamic_slice_in_dim(prefix_len, goal, 1).astype(jnp.int32)
        return sidx, length, coefficient[sidx]

    chain = None
    partials = []
    for goal, prefix_one in ((me, prefix_kv), (me ^ 2, pre_across), (me ^ 3, pre_relay),
                             (me ^ 1, pre_partner)):
        sidx, length, coef = slot_args(goal)
        grad_q, grad_kv, partial = attend_slot(sidx, length, coef, queries, out_grad, suffix_kv,
                                               prefix_one, chain)
        chain = (grad_q, grad_kv)
        partials.append(partial)
    own, cross, relay, near = partials
    forward = (cross + lax.ppermute(relay, "dp", partner)).astype(jnp.bfloat16)
    total = own + lax.ppermute(near, "dp", partner) + lax.ppermute(forward, "dp", across).astype(jnp.float32)
    return chain[0], chain[1], total.astype(jnp.bfloat16)


def solution(mesh):
    return jax.shard_map(
        shards,
        mesh=mesh,
        in_specs=(
            P(("groups", "dp"), None, "tensor"),
            P(("groups", "dp"), None, None, "tensor"),
            P(("groups", "dp"), None, "tensor"),
            P(("groups", "dp"), None, None, "tensor"),
            P(("groups", "dp")),
            P(("groups", "dp"), None),
            P(("groups", "dp"), None),
            P("groups"),
        ),
        out_specs=(
            P(("groups", "dp"), None, "tensor"),
            P(("groups", "dp"), None, None, "tensor"),
            P(("groups", "dp"), None, None, "tensor"),
        ),
        check_vma=False,
    )
```

```python
import functools

import jax
import jax.numpy as jnp
from jax import lax
from jax.experimental import pallas as pl
from jax.experimental.pallas import tpu as pltpu
from jax.sharding import PartitionSpec as P

HD = 128

dpo_beta = 0.5


def mask_bias(length, *, group, seq, prefix_rows):
    shape = (group * seq, prefix_rows + seq)
    key_index = lax.broadcasted_iota(jnp.int32, shape, 1)
    tok_index = lax.broadcasted_iota(jnp.int32, shape, 0) % seq
    in_prefix = key_index < prefix_rows
    allowed = (in_prefix & (key_index < length)) | (
        jnp.logical_not(in_prefix) & (key_index - prefix_rows <= tok_index))
    return jnp.where(allowed, 0.0, -1e30).astype(jnp.float32)


def attend_math(q_blk, og_blk, keys_pre, values_pre, keys_own, values_own, length, coef,
                *, group, seq, prefix_rows, bias=None):
    scale = HD ** (-0.5)
    cot_blk = (coef * og_blk.astype(jnp.float32)).astype(jnp.bfloat16)
    q_rows = jnp.concatenate([q_blk[:, g * HD:(g + 1) * HD] for g in range(group)], 0)
    c_rows = jnp.concatenate([cot_blk[:, g * HD:(g + 1) * HD] for g in range(group)], 0)
    keys = jnp.concatenate([keys_pre, keys_own], 0)
    values = jnp.concatenate([values_pre, values_own], 0)

    nt = (((1,), (1,)), ((), ()))
    tn = (((0,), (0,)), ((), ()))
    scores = lax.dot_general(q_rows, keys, nt, preferred_element_type=jnp.float32) * scale
    if bias is None:
        bias = mask_bias(length, group=group, seq=seq, prefix_rows=prefix_rows)
    scores = scores + bias
    row_max = jnp.max(scores, -1, keepdims=True)
    raised = jnp.exp(scores - row_max)
    prob = raised * (1.0 / jnp.sum(raised, -1, keepdims=True))
    prob_low = prob.astype(jnp.bfloat16)
    output = jnp.dot(prob_low, values, preferred_element_type=jnp.float32)
    row_dot = jnp.sum(c_rows.astype(jnp.float32) * output, -1, keepdims=True)
    grad_prob = lax.dot_general(c_rows, values, nt, preferred_element_type=jnp.float32)
    grad_score = (prob * (grad_prob - row_dot)).astype(jnp.bfloat16)
    grad_q = (scale * jnp.dot(grad_score, keys, preferred_element_type=jnp.float32)).astype(jnp.bfloat16)
    grad_k = scale * lax.dot_general(grad_score, q_rows, tn, preferred_element_type=jnp.float32)
    grad_v = lax.dot_general(prob_low, c_rows, tn, preferred_element_type=jnp.float32)
    return grad_q, grad_k, grad_v


def store_grads(grad_q, grad_k, grad_v, member, dq_ref, dkv_ref, dpre_ref, *, group, seq, prefix_rows):
    for g in range(group):
        dq_ref[0, :, g * HD:(g + 1) * HD] = grad_q[g * seq:(g + 1) * seq]
    dkv_ref[0, 0] = grad_k[prefix_rows:].astype(jnp.bfloat16)
    dkv_ref[0, 1] = grad_v[prefix_rows:].astype(jnp.bfloat16)

    @pl.when(member == 0)
    def _():
        dpre_ref[0, 0] = grad_k[:prefix_rows]
        dpre_ref[0, 1] = grad_v[:prefix_rows]

    @pl.when(member != 0)
    def _():
        dpre_ref[0, 0] += grad_k[:prefix_rows]
        dpre_ref[0, 1] += grad_v[:prefix_rows]


def attend_kernel(slots_ref, goal_ref, len_ref, coef_ref,
                  q_ref, og_ref, skv_ref, pkv_ref,
                  dq_ref, dkv_ref, dpre_ref, *, group, seq, prefix_rows):
    p = pl.program_id(0)
    member = pl.program_id(2)
    s = slots_ref[2 * p + member]
    length = len_ref[goal_ref[p]]
    dims = dict(group=group, seq=seq, prefix_rows=prefix_rows)
    grads = attend_math(q_ref[0], og_ref[0], pkv_ref[0, 0], pkv_ref[0, 1], skv_ref[0, 0], skv_ref[0, 1],
                        length, coef_ref[s], **dims)
    store_grads(*grads, member, dq_ref, dkv_ref, dpre_ref, **dims)


def pair_of(goal, goal_ref, pair_count):
    pair = 0
    for p in range(pair_count):
        pair = jnp.where(goal_ref[p] == goal, p, pair)
    return pair


def slot_kernel(me_ref, goal_ref, slots_ref, len_ref, lr_ref, q_ref, og_ref, skv_ref, pkv_ref, *rest,
                group, seq, prefix_rows, flip, pair_count, chained):
    if chained:
        rest = rest[2:]
    dq_ref, dkv_ref, dpre_ref, bias_ref = rest
    k = pl.program_id(0)
    member = pl.program_id(1)
    goal = me_ref[0] ^ flip
    pair = pair_of(goal, goal_ref, pair_count)
    length = len_ref[goal]
    dims = dict(group=group, seq=seq, prefix_rows=prefix_rows)

    @pl.when((k == 0) & (member == 0))
    def _():
        bias_ref[...] = mask_bias(length, **dims)

    gap = lr_ref[slots_ref[2 * pair]] - lr_ref[slots_ref[2 * pair + 1]]
    x = jnp.full((1, 128), -dpo_beta * gap, jnp.float32)
    weight = dpo_beta * (1.0 / (1.0 + jnp.exp(-x)))
    coef = jnp.where(member == 0, -weight, weight)[:, :1]
    grads = attend_math(q_ref[0], og_ref[0], pkv_ref[0, 0], pkv_ref[0, 1], skv_ref[0, 0], skv_ref[0, 1],
                        length, coef, bias=bias_ref[...], **dims)
    store_grads(*grads, member, dq_ref, dkv_ref, dpre_ref, **dims)


def attend_slot(flip, me, goals, slots, lengths, logratio, queries, out_grad, suffix_kv, prefix_one, chain):
    suffix_count, seq, qwidth = queries.shape
    kv_width = suffix_kv.shape[-1]
    kv_local = kv_width // HD
    group = qwidth // kv_width
    prefix_rows = prefix_one.shape[2]
    pair_count = goals.shape[0]
    qb = group * HD

    def suffix_of(m, me_ref, goal_ref, slots_ref):
        pair = pair_of(me_ref[0] ^ flip, goal_ref, pair_count)
        return slots_ref[2 * pair + m]

    def q_map(k, m, me_ref, goal_ref, slots_ref, len_ref):
        return (suffix_of(m, me_ref, goal_ref, slots_ref), 0, k)

    def skv_map(k, m, me_ref, goal_ref, slots_ref, len_ref):
        return (suffix_of(m, me_ref, goal_ref, slots_ref), 0, 0, k)

    def pkv_map(k, m, me_ref, goal_ref, slots_ref, len_ref):
        return (0, 0, 0, k)

    out_shape = (
        jax.ShapeDtypeStruct((suffix_count, seq, qwidth), jnp.bfloat16),
        jax.ShapeDtypeStruct((suffix_count, 2, seq, kv_width), jnp.bfloat16),
        jax.ShapeDtypeStruct((1, 2, prefix_rows, kv_width), jnp.float32),
    )
    in_specs = [
        pl.BlockSpec(memory_space=pltpu.SMEM),
        pl.BlockSpec((1, seq, qb), q_map),
        pl.BlockSpec((1, seq, qb), q_map),
        pl.BlockSpec((1, 2, seq, HD), skv_map),
        pl.BlockSpec((1, 2, prefix_rows, HD), pkv_map),
    ]
    operands = [logratio, queries, out_grad, suffix_kv, prefix_one]
    aliases = {}
    if chain is not None:
        in_specs += [pl.BlockSpec(memory_space=pl.ANY)] * 2
        operands += list(chain)
        aliases = {9: 0, 10: 1}
    kernel = functools.partial(slot_kernel, group=group, seq=seq, prefix_rows=prefix_rows, flip=flip,
                               pair_count=pair_count, chained=chain is not None)
    grid_spec = pltpu.PrefetchScalarGridSpec(
        num_scalar_prefetch=4,
        grid=(kv_local, 2),
        in_specs=in_specs,
        out_specs=[
            pl.BlockSpec((1, seq, qb), q_map),
            pl.BlockSpec((1, 2, seq, HD), skv_map),
            pl.BlockSpec((1, 2, prefix_rows, HD), pkv_map),
        ],
        scratch_shapes=[pltpu.VMEM((group * seq, prefix_rows + seq), jnp.float32)],
    )
    steps = 2 * kv_local
    cost = pl.CostEstimate(
        flops=steps * 2_200_000_000,
        transcendentals=steps * group * seq * (prefix_rows + seq),
        bytes_accessed=steps * (4 * seq * qb + 4 * seq * HD + 6 * prefix_rows * HD) * 2,
    )
    return pl.pallas_call(
        kernel,
        grid_spec=grid_spec,
        out_shape=out_shape,
        input_output_aliases=aliases,
        cost_estimate=cost,
        compiler_params=pltpu.CompilerParams(dimension_semantics=("arbitrary", "arbitrary")),
    )(me, goals, slots, lengths, *operands)


def attend_all(slots, goals, lengths, coef, queries, out_grad, suffix_kv, prefix_all):
    suffix_count, seq, qwidth = queries.shape
    kv_width = suffix_kv.shape[-1]
    kv_local = kv_width // HD
    group = qwidth // kv_width
    goal_count, _, prefix_rows, _ = prefix_all.shape
    pair_count = goals.shape[0]
    qb = group * HD

    def q_map(p, k, m, slots_ref, goal_ref, len_ref):
        return (slots_ref[2 * p + m], 0, k)

    def skv_map(p, k, m, slots_ref, goal_ref, len_ref):
        return (slots_ref[2 * p + m], 0, 0, k)

    def pkv_map(p, k, m, slots_ref, goal_ref, len_ref):
        return (goal_ref[p], 0, 0, k)

    kernel = functools.partial(attend_kernel, group=group, seq=seq, prefix_rows=prefix_rows)
    out_shape = (
        jax.ShapeDtypeStruct((suffix_count, seq, qwidth), jnp.bfloat16),
        jax.ShapeDtypeStruct((suffix_count, 2, seq, kv_width), jnp.bfloat16),
        jax.ShapeDtypeStruct((goal_count, 2, prefix_rows, kv_width), jnp.float32),
    )
    in_specs = [
        pl.BlockSpec(memory_space=pltpu.SMEM),
        pl.BlockSpec((1, seq, qb), q_map),
        pl.BlockSpec((1, seq, qb), q_map),
        pl.BlockSpec((1, 2, seq, HD), skv_map),
        pl.BlockSpec((1, 2, prefix_rows, HD), pkv_map),
    ]
    operands = [coef, queries, out_grad, suffix_kv, prefix_all]
    aliases = {}
    if pair_count < goal_count:
        in_specs.append(pl.BlockSpec(memory_space=pl.ANY))
        operands.append(jnp.zeros(out_shape[2].shape, jnp.float32))
        aliases = {3 + len(operands) - 1: 2}

        def kernel_with_zero(*refs):
            return kernel(*refs[:8], *refs[9:])
        body = kernel_with_zero
    else:
        body = kernel
    grid_spec = pltpu.PrefetchScalarGridSpec(
        num_scalar_prefetch=3,
        grid=(pair_count, kv_local, 2),
        in_specs=in_specs,
        out_specs=[
            pl.BlockSpec((1, seq, qb), q_map),
            pl.BlockSpec((1, 2, seq, HD), skv_map),
            pl.BlockSpec((1, 2, prefix_rows, HD), pkv_map),
        ],
    )
    return pl.pallas_call(
        body,
        grid_spec=grid_spec,
        out_shape=out_shape,
        input_output_aliases=aliases,
        compiler_params=pltpu.CompilerParams(
            dimension_semantics=("arbitrary", "arbitrary", "arbitrary")),
    )(slots, goals, lengths, *operands)


def shards(queries, suffix_kv, out_grad, prefix_kv, logratio, pair_slots, pair_goal, prefix_len):
    dp_size = lax.axis_size("dp")
    pair_count = pair_slots.shape[0]
    if dp_size == 4 and pair_count == dp_size:
        return pipelined(queries, suffix_kv, out_grad, prefix_kv, logratio,
                         pair_slots, pair_goal, prefix_len)
    suffix_count = queries.shape[0]
    chosen = pair_slots[:, 0]
    rejected = pair_slots[:, 1]
    positions = jnp.arange(suffix_count)
    pick_chosen = chosen[:, None] == positions[None, :]
    pick_rejected = rejected[:, None] == positions[None, :]
    ratio_chosen = jnp.sum(jnp.where(pick_chosen, logratio[None, :], 0.0), 1)
    ratio_rejected = jnp.sum(jnp.where(pick_rejected, logratio[None, :], 0.0), 1)
    weight = dpo_beta * jax.nn.sigmoid(-dpo_beta * (ratio_chosen - ratio_rejected))
    coefficient = jnp.sum(
        jnp.where(pick_rejected, weight[:, None], 0.0)
        - jnp.where(pick_chosen, weight[:, None], 0.0),
        0,
    )
    slots = pair_slots.reshape(-1).astype(jnp.int32)
    goals = pair_goal[:, 0].astype(jnp.int32)
    prefix_all = lax.all_gather(prefix_kv, "dp", axis=0, tiled=True)
    grad_q, grad_kv, partial = attend_all(
        slots, goals, prefix_len.astype(jnp.int32), coefficient,
        queries, out_grad, suffix_kv, prefix_all)
    prefix_grad = lax.psum_scatter(partial, "dp", scatter_dimension=0, tiled=True)
    return grad_q, grad_kv, prefix_grad.astype(jnp.bfloat16)


def pipelined(queries, suffix_kv, out_grad, prefix_kv, logratio, pair_slots, pair_goal, prefix_len):
    partner = [(i, i ^ 1) for i in range(4)]
    across = [(i, i ^ 2) for i in range(4)]
    pre_across = lax.ppermute(prefix_kv, "dp", across)
    pre_partner = lax.ppermute(prefix_kv, "dp", partner)
    pre_relay = lax.ppermute(pre_across, "dp", partner)
    me = lax.axis_index("dp").astype(jnp.int32).reshape(1)
    tables = (me, pair_goal.reshape(-1).astype(jnp.int32), pair_slots.reshape(-1).astype(jnp.int32),
              prefix_len.astype(jnp.int32), logratio)

    def run(flip, prefix_one, chain):
        grad_q, grad_kv, partial = attend_slot(flip, *tables, queries, out_grad, suffix_kv, prefix_one, chain)
        return (grad_q, grad_kv), partial

    chain, own = run(0, prefix_kv, None)
    chain, cross = run(2, pre_across, chain)
    chain, relay = run(3, pre_relay, chain)
    forward = (cross + lax.ppermute(relay, "dp", partner)).astype(jnp.bfloat16)
    forward, pre_partner = lax.optimization_barrier((forward, pre_partner))
    chain, near = run(1, pre_partner, chain)
    total = own + lax.ppermute(near, "dp", partner) + lax.ppermute(forward, "dp", across).astype(jnp.float32)
    return chain[0], chain[1], total.astype(jnp.bfloat16)


def solution(mesh):
    return jax.shard_map(
        shards,
        mesh=mesh,
        in_specs=(
            P(("groups", "dp"), None, "tensor"),
            P(("groups", "dp"), None, None, "tensor"),
            P(("groups", "dp"), None, "tensor"),
            P(("groups", "dp"), None, None, "tensor"),
            P(("groups", "dp")),
            P(("groups", "dp"), None),
            P(("groups", "dp"), None),
            P("groups"),
        ),
        out_specs=(
            P(("groups", "dp"), None, "tensor"),
            P(("groups", "dp"), None, None, "tensor"),
            P(("groups", "dp"), None, None, "tensor"),
        ),
        check_vma=False,
    )
```

```python
import functools

import jax
import jax.numpy as jnp
from jax import lax
from jax.experimental import pallas as pl
from jax.experimental.pallas import tpu as pltpu
from jax.sharding import PartitionSpec as P

HD = 128

dpo_beta = 0.5


def mask_bias(length, *, group, seq, prefix_rows):
    shape = (group * seq, prefix_rows + seq)
    key_index = lax.broadcasted_iota(jnp.int32, shape, 1)
    tok_index = lax.broadcasted_iota(jnp.int32, shape, 0) % seq
    in_prefix = key_index < prefix_rows
    allowed = (in_prefix & (key_index < length)) | (
        jnp.logical_not(in_prefix) & (key_index - prefix_rows <= tok_index))
    return jnp.where(allowed, 0.0, -1e30).astype(jnp.float32)


def attend_math(q_blk, og_blk, keys_pre, values_pre, keys_own, values_own, length, coef,
                *, group, seq, prefix_rows, bias=None):
    scale = HD ** (-0.5)
    cot_blk = (coef * og_blk.astype(jnp.float32)).astype(jnp.bfloat16)
    q_rows = jnp.concatenate([q_blk[:, g * HD:(g + 1) * HD] for g in range(group)], 0)
    c_rows = jnp.concatenate([cot_blk[:, g * HD:(g + 1) * HD] for g in range(group)], 0)
    keys = jnp.concatenate([keys_pre, keys_own], 0)
    values = jnp.concatenate([values_pre, values_own], 0)

    nt = (((1,), (1,)), ((), ()))
    tn = (((0,), (0,)), ((), ()))
    scores = lax.dot_general(q_rows, keys, nt, preferred_element_type=jnp.float32) * scale
    if bias is None:
        bias = mask_bias(length, group=group, seq=seq, prefix_rows=prefix_rows)
    scores = scores + bias
    row_max = jnp.max(scores, -1, keepdims=True)
    raised = jnp.exp(scores - row_max)
    prob = raised * (1.0 / jnp.sum(raised, -1, keepdims=True))
    prob_low = prob.astype(jnp.bfloat16)
    output = jnp.dot(prob_low, values, preferred_element_type=jnp.float32)
    row_dot = jnp.sum(c_rows.astype(jnp.float32) * output, -1, keepdims=True)
    grad_prob = lax.dot_general(c_rows, values, nt, preferred_element_type=jnp.float32)
    grad_score = (prob * (grad_prob - row_dot)).astype(jnp.bfloat16)
    grad_q = (scale * jnp.dot(grad_score, keys, preferred_element_type=jnp.float32)).astype(jnp.bfloat16)
    grad_k = scale * lax.dot_general(grad_score, q_rows, tn, preferred_element_type=jnp.float32)
    grad_v = lax.dot_general(prob_low, c_rows, tn, preferred_element_type=jnp.float32)
    return grad_q, grad_k, grad_v


def store_grads(grad_q, grad_k, grad_v, member, dq_ref, dkv_ref, dpre_ref, *, group, seq, prefix_rows):
    for g in range(group):
        dq_ref[0, :, g * HD:(g + 1) * HD] = grad_q[g * seq:(g + 1) * seq]
    dkv_ref[0, 0] = grad_k[prefix_rows:].astype(jnp.bfloat16)
    dkv_ref[0, 1] = grad_v[prefix_rows:].astype(jnp.bfloat16)

    @pl.when(member == 0)
    def _():
        dpre_ref[0, 0] = grad_k[:prefix_rows]
        dpre_ref[0, 1] = grad_v[:prefix_rows]

    @pl.when(member != 0)
    def _():
        dpre_ref[0, 0] += grad_k[:prefix_rows]
        dpre_ref[0, 1] += grad_v[:prefix_rows]


def attend_kernel(slots_ref, goal_ref, len_ref, coef_ref,
                  q_ref, og_ref, skv_ref, pkv_ref,
                  dq_ref, dkv_ref, dpre_ref, *, group, seq, prefix_rows):
    p = pl.program_id(0)
    member = pl.program_id(2)
    s = slots_ref[2 * p + member]
    length = len_ref[goal_ref[p]]
    dims = dict(group=group, seq=seq, prefix_rows=prefix_rows)
    grads = attend_math(q_ref[0], og_ref[0], pkv_ref[0, 0], pkv_ref[0, 1], skv_ref[0, 0], skv_ref[0, 1],
                        length, coef_ref[s], **dims)
    store_grads(*grads, member, dq_ref, dkv_ref, dpre_ref, **dims)


def pair_of(goal, goal_ref, pair_count):
    pair = 0
    for p in range(pair_count):
        pair = jnp.where(goal_ref[p] == goal, p, pair)
    return pair


def slot_kernel(me_ref, goal_ref, slots_ref, len_ref, lr_ref, q_ref, og_ref, skv_ref, pkv_ref, *rest,
                group, seq, prefix_rows, flip, pair_count, chained):
    if chained:
        rest = rest[2:]
    dq_ref, dkv_ref, dpre_ref, bias_ref = rest
    k = pl.program_id(0)
    member = pl.program_id(1)
    goal = me_ref[0] ^ flip
    pair = pair_of(goal, goal_ref, pair_count)
    length = len_ref[goal]
    dims = dict(group=group, seq=seq, prefix_rows=prefix_rows)

    @pl.when((k == 0) & (member == 0))
    def _():
        bias_ref[...] = mask_bias(length, **dims)

    gap = lr_ref[slots_ref[2 * pair]] - lr_ref[slots_ref[2 * pair + 1]]
    x = jnp.full((1, 128), -dpo_beta * gap, jnp.float32)
    weight = dpo_beta * (1.0 / (1.0 + jnp.exp(-x)))
    coef = jnp.where(member == 0, -weight, weight)[:, :1]
    grads = attend_math(q_ref[0], og_ref[0], pkv_ref[0, 0], pkv_ref[0, 1], skv_ref[0, 0], skv_ref[0, 1],
                        length, coef, bias=bias_ref[...], **dims)
    store_grads(*grads, member, dq_ref, dkv_ref, dpre_ref, **dims)


def attend_slot(flip, me, goals, slots, lengths, logratio, queries, out_grad, suffix_kv, prefix_one, chain):
    suffix_count, seq, qwidth = queries.shape
    kv_width = suffix_kv.shape[-1]
    kv_local = kv_width // HD
    group = qwidth // kv_width
    prefix_rows = prefix_one.shape[2]
    pair_count = goals.shape[0]
    qb = group * HD

    def suffix_of(m, me_ref, goal_ref, slots_ref):
        pair = pair_of(me_ref[0] ^ flip, goal_ref, pair_count)
        return slots_ref[2 * pair + m]

    def q_map(k, m, me_ref, goal_ref, slots_ref, len_ref):
        return (suffix_of(m, me_ref, goal_ref, slots_ref), 0, k)

    def skv_map(k, m, me_ref, goal_ref, slots_ref, len_ref):
        return (suffix_of(m, me_ref, goal_ref, slots_ref), 0, 0, k)

    def pkv_map(k, m, me_ref, goal_ref, slots_ref, len_ref):
        return (0, 0, 0, k)

    out_shape = (
        jax.ShapeDtypeStruct((suffix_count, seq, qwidth), jnp.bfloat16),
        jax.ShapeDtypeStruct((suffix_count, 2, seq, kv_width), jnp.bfloat16),
        jax.ShapeDtypeStruct((1, 2, prefix_rows, kv_width), jnp.float32),
    )
    in_specs = [
        pl.BlockSpec(memory_space=pltpu.SMEM),
        pl.BlockSpec((1, seq, qb), q_map),
        pl.BlockSpec((1, seq, qb), q_map),
        pl.BlockSpec((1, 2, seq, HD), skv_map),
        pl.BlockSpec((1, 2, prefix_rows, HD), pkv_map),
    ]
    operands = [logratio, queries, out_grad, suffix_kv, prefix_one]
    aliases = {}
    if chain is not None:
        in_specs += [pl.BlockSpec(memory_space=pl.ANY)] * 2
        operands += list(chain)
        aliases = {9: 0, 10: 1}
    kernel = functools.partial(slot_kernel, group=group, seq=seq, prefix_rows=prefix_rows, flip=flip,
                               pair_count=pair_count, chained=chain is not None)
    grid_spec = pltpu.PrefetchScalarGridSpec(
        num_scalar_prefetch=4,
        grid=(kv_local, 2),
        in_specs=in_specs,
        out_specs=[
            pl.BlockSpec((1, seq, qb), q_map),
            pl.BlockSpec((1, 2, seq, HD), skv_map),
            pl.BlockSpec((1, 2, prefix_rows, HD), pkv_map),
        ],
        scratch_shapes=[pltpu.VMEM((group * seq, prefix_rows + seq), jnp.float32)],
    )
    steps = 2 * kv_local
    cost = pl.CostEstimate(
        flops=steps * 2_200_000_000,
        transcendentals=steps * group * seq * (prefix_rows + seq),
        bytes_accessed=steps * (4 * seq * qb + 4 * seq * HD + 6 * prefix_rows * HD) * 2,
    )
    return pl.pallas_call(
        kernel,
        grid_spec=grid_spec,
        out_shape=out_shape,
        input_output_aliases=aliases,
        cost_estimate=cost,
        compiler_params=pltpu.CompilerParams(dimension_semantics=("arbitrary", "arbitrary")),
    )(me, goals, slots, lengths, *operands)


def attend_all(slots, goals, lengths, coef, queries, out_grad, suffix_kv, prefix_all):
    suffix_count, seq, qwidth = queries.shape
    kv_width = suffix_kv.shape[-1]
    kv_local = kv_width // HD
    group = qwidth // kv_width
    goal_count, _, prefix_rows, _ = prefix_all.shape
    pair_count = goals.shape[0]
    qb = group * HD

    def q_map(p, k, m, slots_ref, goal_ref, len_ref):
        return (slots_ref[2 * p + m], 0, k)

    def skv_map(p, k, m, slots_ref, goal_ref, len_ref):
        return (slots_ref[2 * p + m], 0, 0, k)

    def pkv_map(p, k, m, slots_ref, goal_ref, len_ref):
        return (goal_ref[p], 0, 0, k)

    kernel = functools.partial(attend_kernel, group=group, seq=seq, prefix_rows=prefix_rows)
    out_shape = (
        jax.ShapeDtypeStruct((suffix_count, seq, qwidth), jnp.bfloat16),
        jax.ShapeDtypeStruct((suffix_count, 2, seq, kv_width), jnp.bfloat16),
        jax.ShapeDtypeStruct((goal_count, 2, prefix_rows, kv_width), jnp.float32),
    )
    in_specs = [
        pl.BlockSpec(memory_space=pltpu.SMEM),
        pl.BlockSpec((1, seq, qb), q_map),
        pl.BlockSpec((1, seq, qb), q_map),
        pl.BlockSpec((1, 2, seq, HD), skv_map),
        pl.BlockSpec((1, 2, prefix_rows, HD), pkv_map),
    ]
    operands = [coef, queries, out_grad, suffix_kv, prefix_all]
    aliases = {}
    if pair_count < goal_count:
        in_specs.append(pl.BlockSpec(memory_space=pl.ANY))
        operands.append(jnp.zeros(out_shape[2].shape, jnp.float32))
        aliases = {3 + len(operands) - 1: 2}

        def kernel_with_zero(*refs):
            return kernel(*refs[:8], *refs[9:])
        body = kernel_with_zero
    else:
        body = kernel
    grid_spec = pltpu.PrefetchScalarGridSpec(
        num_scalar_prefetch=3,
        grid=(pair_count, kv_local, 2),
        in_specs=in_specs,
        out_specs=[
            pl.BlockSpec((1, seq, qb), q_map),
            pl.BlockSpec((1, 2, seq, HD), skv_map),
            pl.BlockSpec((1, 2, prefix_rows, HD), pkv_map),
        ],
    )
    return pl.pallas_call(
        body,
        grid_spec=grid_spec,
        out_shape=out_shape,
        input_output_aliases=aliases,
        compiler_params=pltpu.CompilerParams(
            dimension_semantics=("arbitrary", "arbitrary", "arbitrary")),
    )(slots, goals, lengths, *operands)


def shards(queries, suffix_kv, out_grad, prefix_kv, logratio, pair_slots, pair_goal, prefix_len):
    dp_size = lax.axis_size("dp")
    pair_count = pair_slots.shape[0]
    if dp_size == 4 and pair_count == dp_size:
        return pipelined(queries, suffix_kv, out_grad, prefix_kv, logratio,
                         pair_slots, pair_goal, prefix_len)
    suffix_count = queries.shape[0]
    chosen = pair_slots[:, 0]
    rejected = pair_slots[:, 1]
    positions = jnp.arange(suffix_count)
    pick_chosen = chosen[:, None] == positions[None, :]
    pick_rejected = rejected[:, None] == positions[None, :]
    ratio_chosen = jnp.sum(jnp.where(pick_chosen, logratio[None, :], 0.0), 1)
    ratio_rejected = jnp.sum(jnp.where(pick_rejected, logratio[None, :], 0.0), 1)
    weight = dpo_beta * jax.nn.sigmoid(-dpo_beta * (ratio_chosen - ratio_rejected))
    coefficient = jnp.sum(
        jnp.where(pick_rejected, weight[:, None], 0.0)
        - jnp.where(pick_chosen, weight[:, None], 0.0),
        0,
    )
    slots = pair_slots.reshape(-1).astype(jnp.int32)
    goals = pair_goal[:, 0].astype(jnp.int32)
    prefix_all = lax.all_gather(prefix_kv, "dp", axis=0, tiled=True)
    grad_q, grad_kv, partial = attend_all(
        slots, goals, prefix_len.astype(jnp.int32), coefficient,
        queries, out_grad, suffix_kv, prefix_all)
    prefix_grad = lax.psum_scatter(partial, "dp", scatter_dimension=0, tiled=True)
    return grad_q, grad_kv, prefix_grad.astype(jnp.bfloat16)


def pipelined(queries, suffix_kv, out_grad, prefix_kv, logratio, pair_slots, pair_goal, prefix_len):
    partner = [(i, i ^ 1) for i in range(4)]
    across = [(i, i ^ 2) for i in range(4)]
    pre_across = lax.ppermute(prefix_kv, "dp", across)
    pre_partner = lax.ppermute(prefix_kv, "dp", partner)
    me = lax.axis_index("dp").astype(jnp.int32).reshape(1)
    tables = (me, pair_goal.reshape(-1).astype(jnp.int32), pair_slots.reshape(-1).astype(jnp.int32),
              prefix_len.astype(jnp.int32), logratio)

    def run(flip, prefix_one, chain):
        grad_q, grad_kv, partial = attend_slot(flip, *tables, queries, out_grad, suffix_kv, prefix_one, chain)
        return (grad_q, grad_kv), partial

    chain, near = run(1, pre_partner, None)
    pre_across, near = lax.optimization_barrier((pre_across, near))
    pre_relay = lax.ppermute(pre_across, "dp", partner)
    near_sent = lax.ppermute(near, "dp", partner)
    chain, cross = run(2, pre_across, chain)
    chain, relay = run(3, pre_relay, chain)
    forward = (cross + lax.ppermute(relay, "dp", partner)).astype(jnp.bfloat16)
    forward, own_prefix = lax.optimization_barrier((forward, prefix_kv))
    chain, own = run(0, own_prefix, chain)
    total = own + near_sent + lax.ppermute(forward, "dp", across).astype(jnp.float32)
    return chain[0], chain[1], total.astype(jnp.bfloat16)


def solution(mesh):
    return jax.shard_map(
        shards,
        mesh=mesh,
        in_specs=(
            P(("groups", "dp"), None, "tensor"),
            P(("groups", "dp"), None, None, "tensor"),
            P(("groups", "dp"), None, "tensor"),
            P(("groups", "dp"), None, None, "tensor"),
            P(("groups", "dp")),
            P(("groups", "dp"), None),
            P(("groups", "dp"), None),
            P("groups"),
        ),
        out_specs=(
            P(("groups", "dp"), None, "tensor"),
            P(("groups", "dp"), None, None, "tensor"),
            P(("groups", "dp"), None, None, "tensor"),
        ),
        check_vma=False,
    )
```

```python
import functools

import jax
import jax.numpy as jnp
from jax import lax
from jax.experimental import pallas as pl
from jax.experimental.pallas import tpu as pltpu
from jax.sharding import PartitionSpec as P

HD = 128

dpo_beta = 0.5


def mask_bias(length, *, group, seq, prefix_rows):
    shape = (group * seq, seq + prefix_rows)
    key_index = lax.broadcasted_iota(jnp.int32, shape, 1)
    tok_index = lax.broadcasted_iota(jnp.int32, shape, 0) % seq
    in_suffix = key_index < seq
    allowed = (in_suffix & (key_index <= tok_index)) | (
        jnp.logical_not(in_suffix) & (key_index - seq < length))
    return jnp.where(allowed, 0.0, -1e30).astype(jnp.float32)


def attend_math(q_blk, og_blk, keys_pre, values_pre, keys_own, values_own, bias, coef, *, group, seq):
    scale = HD ** (-0.5)
    cot_blk = (coef * og_blk.astype(jnp.float32)).astype(jnp.bfloat16)
    q_rows = jnp.concatenate([q_blk[:, g * HD:(g + 1) * HD] for g in range(group)], 0)
    c_rows = jnp.concatenate([cot_blk[:, g * HD:(g + 1) * HD] for g in range(group)], 0)
    keys = jnp.concatenate([keys_own, keys_pre], 0)
    values = jnp.concatenate([values_own, values_pre], 0)

    nt = (((1,), (1,)), ((), ()))
    tn = (((0,), (0,)), ((), ()))
    scores = lax.dot_general(q_rows, keys, nt, preferred_element_type=jnp.float32) * scale
    scores = scores + bias
    row_max = jnp.max(scores, -1, keepdims=True)
    raised = jnp.exp(scores - row_max)
    prob = raised * (1.0 / jnp.sum(raised, -1, keepdims=True))
    prob_low = prob.astype(jnp.bfloat16)
    output = jnp.dot(prob_low, values, preferred_element_type=jnp.float32)
    row_dot = jnp.sum(c_rows.astype(jnp.float32) * output, -1, keepdims=True)
    grad_prob = lax.dot_general(c_rows, values, nt, preferred_element_type=jnp.float32)
    grad_score = (prob * (grad_prob - row_dot)).astype(jnp.bfloat16)
    grad_q = (scale * jnp.dot(grad_score, keys, preferred_element_type=jnp.float32)).astype(jnp.bfloat16)
    grad_k = scale * lax.dot_general(grad_score, q_rows, tn, preferred_element_type=jnp.float32)
    grad_v = lax.dot_general(prob_low, c_rows, tn, preferred_element_type=jnp.float32)
    return grad_q, grad_k, grad_v


def store_grads(grad_q, grad_k, grad_v, member, dq_ref, dkv_ref, dpre_ref, *, group, seq, prefix_rows):
    active = grad_k.shape[0] - seq
    for g in range(group):
        dq_ref[0, :, g * HD:(g + 1) * HD] = grad_q[g * seq:(g + 1) * seq]
    dkv_ref[0, 0] = grad_k[:seq].astype(jnp.bfloat16)
    dkv_ref[0, 1] = grad_v[:seq].astype(jnp.bfloat16)

    @pl.when(member == 0)
    def _():
        dpre_ref[0, 0, :active] = grad_k[seq:]
        dpre_ref[0, 1, :active] = grad_v[seq:]
        if active < prefix_rows:
            zeros = jnp.zeros((prefix_rows - active, HD), jnp.float32)
            dpre_ref[0, 0, active:] = zeros
            dpre_ref[0, 1, active:] = zeros

    @pl.when(member != 0)
    def _():
        dpre_ref[0, 0, :active] += grad_k[seq:]
        dpre_ref[0, 1, :active] += grad_v[seq:]


def attend_kernel(slots_ref, goal_ref, len_ref, coef_ref,
                  q_ref, og_ref, skv_ref, pkv_ref,
                  dq_ref, dkv_ref, dpre_ref, *, group, seq, prefix_rows):
    p = pl.program_id(0)
    member = pl.program_id(2)
    s = slots_ref[2 * p + member]
    length = len_ref[goal_ref[p]]
    bias = mask_bias(length, group=group, seq=seq, prefix_rows=prefix_rows)
    grads = attend_math(q_ref[0], og_ref[0], pkv_ref[0, 0], pkv_ref[0, 1], skv_ref[0, 0], skv_ref[0, 1],
                        bias, coef_ref[s], group=group, seq=seq)
    store_grads(*grads, member, dq_ref, dkv_ref, dpre_ref, group=group, seq=seq, prefix_rows=prefix_rows)


def pair_of(goal, goal_ref, pair_count):
    pair = 0
    for p in range(pair_count):
        pair = jnp.where(goal_ref[p] == goal, p, pair)
    return pair


def slot_kernel(me_ref, goal_ref, slots_ref, len_ref, lr_ref, q_ref, og_ref, skv_ref, pkv_ref, *rest,
                group, seq, prefix_rows, flip, pair_count, chained):
    if chained:
        rest = rest[2:]
    dq_ref, dkv_ref, dpre_ref, bias_ref = rest
    k = pl.program_id(0)
    member = pl.program_id(1)
    goal = me_ref[0] ^ flip
    pair = pair_of(goal, goal_ref, pair_count)
    length = len_ref[goal]
    dims = dict(group=group, seq=seq, prefix_rows=prefix_rows)

    @pl.when((k == 0) & (member == 0))
    def _():
        bias_ref[...] = mask_bias(length, **dims)

    gap = lr_ref[slots_ref[2 * pair]] - lr_ref[slots_ref[2 * pair + 1]]
    x = jnp.full((1, 128), -dpo_beta * gap, jnp.float32)
    weight = dpo_beta * (1.0 / (1.0 + jnp.exp(-x)))
    coef = jnp.where(member == 0, -weight, weight)[:, :1]
    blocks = (seq + length + 127) // 128
    for used in range(1, (seq + prefix_rows + 127) // 128 + 1):
        @pl.when(blocks == used)
        def _():
            width = min(used * 128, seq + prefix_rows)
            active = width - seq
            grads = attend_math(q_ref[0], og_ref[0], pkv_ref[0, 0, :active], pkv_ref[0, 1, :active],
                                skv_ref[0, 0], skv_ref[0, 1], bias_ref[:, :width], coef,
                                group=group, seq=seq)
            store_grads(*grads, member, dq_ref, dkv_ref, dpre_ref, **dims)


def attend_slot(flip, me, goals, slots, lengths, logratio, queries, out_grad, suffix_kv, prefix_one, chain):
    suffix_count, seq, qwidth = queries.shape
    kv_width = suffix_kv.shape[-1]
    kv_local = kv_width // HD
    group = qwidth // kv_width
    prefix_rows = prefix_one.shape[2]
    pair_count = goals.shape[0]
    qb = group * HD

    def suffix_of(m, me_ref, goal_ref, slots_ref):
        pair = pair_of(me_ref[0] ^ flip, goal_ref, pair_count)
        return slots_ref[2 * pair + m]

    def q_map(k, m, me_ref, goal_ref, slots_ref, len_ref):
        return (suffix_of(m, me_ref, goal_ref, slots_ref), 0, k)

    def skv_map(k, m, me_ref, goal_ref, slots_ref, len_ref):
        return (suffix_of(m, me_ref, goal_ref, slots_ref), 0, 0, k)

    def pkv_map(k, m, me_ref, goal_ref, slots_ref, len_ref):
        return (0, 0, 0, k)

    out_shape = (
        jax.ShapeDtypeStruct((suffix_count, seq, qwidth), jnp.bfloat16),
        jax.ShapeDtypeStruct((suffix_count, 2, seq, kv_width), jnp.bfloat16),
        jax.ShapeDtypeStruct((1, 2, prefix_rows, kv_width), jnp.float32),
    )
    in_specs = [
        pl.BlockSpec(memory_space=pltpu.SMEM),
        pl.BlockSpec((1, seq, qb), q_map),
        pl.BlockSpec((1, seq, qb), q_map),
        pl.BlockSpec((1, 2, seq, HD), skv_map),
        pl.BlockSpec((1, 2, prefix_rows, HD), pkv_map),
    ]
    operands = [logratio, queries, out_grad, suffix_kv, prefix_one]
    aliases = {}
    if chain is not None:
        in_specs += [pl.BlockSpec(memory_space=pl.ANY)] * 2
        operands += list(chain)
        aliases = {9: 0, 10: 1}
    kernel = functools.partial(slot_kernel, group=group, seq=seq, prefix_rows=prefix_rows, flip=flip,
                               pair_count=pair_count, chained=chain is not None)
    grid_spec = pltpu.PrefetchScalarGridSpec(
        num_scalar_prefetch=4,
        grid=(kv_local, 2),
        in_specs=in_specs,
        out_specs=[
            pl.BlockSpec((1, seq, qb), q_map),
            pl.BlockSpec((1, 2, seq, HD), skv_map),
            pl.BlockSpec((1, 2, prefix_rows, HD), pkv_map),
        ],
        scratch_shapes=[pltpu.VMEM((group * seq, prefix_rows + seq), jnp.float32)],
    )
    steps = 2 * kv_local
    cost = pl.CostEstimate(
        flops=steps * 2_200_000_000,
        transcendentals=steps * group * seq * (prefix_rows + seq),
        bytes_accessed=steps * (4 * seq * qb + 4 * seq * HD + 6 * prefix_rows * HD) * 2,
    )
    return pl.pallas_call(
        kernel,
        grid_spec=grid_spec,
        out_shape=out_shape,
        input_output_aliases=aliases,
        cost_estimate=cost,
        compiler_params=pltpu.CompilerParams(dimension_semantics=("arbitrary", "arbitrary")),
    )(me, goals, slots, lengths, *operands)


def attend_all(slots, goals, lengths, coef, queries, out_grad, suffix_kv, prefix_all):
    suffix_count, seq, qwidth = queries.shape
    kv_width = suffix_kv.shape[-1]
    kv_local = kv_width // HD
    group = qwidth // kv_width
    goal_count, _, prefix_rows, _ = prefix_all.shape
    pair_count = goals.shape[0]
    qb = group * HD

    def q_map(p, k, m, slots_ref, goal_ref, len_ref):
        return (slots_ref[2 * p + m], 0, k)

    def skv_map(p, k, m, slots_ref, goal_ref, len_ref):
        return (slots_ref[2 * p + m], 0, 0, k)

    def pkv_map(p, k, m, slots_ref, goal_ref, len_ref):
        return (goal_ref[p], 0, 0, k)

    kernel = functools.partial(attend_kernel, group=group, seq=seq, prefix_rows=prefix_rows)
    out_shape = (
        jax.ShapeDtypeStruct((suffix_count, seq, qwidth), jnp.bfloat16),
        jax.ShapeDtypeStruct((suffix_count, 2, seq, kv_width), jnp.bfloat16),
        jax.ShapeDtypeStruct((goal_count, 2, prefix_rows, kv_width), jnp.float32),
    )
    in_specs = [
        pl.BlockSpec(memory_space=pltpu.SMEM),
        pl.BlockSpec((1, seq, qb), q_map),
        pl.BlockSpec((1, seq, qb), q_map),
        pl.BlockSpec((1, 2, seq, HD), skv_map),
        pl.BlockSpec((1, 2, prefix_rows, HD), pkv_map),
    ]
    operands = [coef, queries, out_grad, suffix_kv, prefix_all]
    aliases = {}
    if pair_count < goal_count:
        in_specs.append(pl.BlockSpec(memory_space=pl.ANY))
        operands.append(jnp.zeros(out_shape[2].shape, jnp.float32))
        aliases = {3 + len(operands) - 1: 2}

        def kernel_with_zero(*refs):
            return kernel(*refs[:8], *refs[9:])
        body = kernel_with_zero
    else:
        body = kernel
    grid_spec = pltpu.PrefetchScalarGridSpec(
        num_scalar_prefetch=3,
        grid=(pair_count, kv_local, 2),
        in_specs=in_specs,
        out_specs=[
            pl.BlockSpec((1, seq, qb), q_map),
            pl.BlockSpec((1, 2, seq, HD), skv_map),
            pl.BlockSpec((1, 2, prefix_rows, HD), pkv_map),
        ],
    )
    return pl.pallas_call(
        body,
        grid_spec=grid_spec,
        out_shape=out_shape,
        input_output_aliases=aliases,
        compiler_params=pltpu.CompilerParams(
            dimension_semantics=("arbitrary", "arbitrary", "arbitrary")),
    )(slots, goals, lengths, *operands)


def shards(queries, suffix_kv, out_grad, prefix_kv, logratio, pair_slots, pair_goal, prefix_len):
    dp_size = lax.axis_size("dp")
    pair_count = pair_slots.shape[0]
    if dp_size == 4 and pair_count == dp_size:
        return pipelined(queries, suffix_kv, out_grad, prefix_kv, logratio,
                         pair_slots, pair_goal, prefix_len)
    suffix_count = queries.shape[0]
    chosen = pair_slots[:, 0]
    rejected = pair_slots[:, 1]
    positions = jnp.arange(suffix_count)
    pick_chosen = chosen[:, None] == positions[None, :]
    pick_rejected = rejected[:, None] == positions[None, :]
    ratio_chosen = jnp.sum(jnp.where(pick_chosen, logratio[None, :], 0.0), 1)
    ratio_rejected = jnp.sum(jnp.where(pick_rejected, logratio[None, :], 0.0), 1)
    weight = dpo_beta * jax.nn.sigmoid(-dpo_beta * (ratio_chosen - ratio_rejected))
    coefficient = jnp.sum(
        jnp.where(pick_rejected, weight[:, None], 0.0)
        - jnp.where(pick_chosen, weight[:, None], 0.0),
        0,
    )
    slots = pair_slots.reshape(-1).astype(jnp.int32)
    goals = pair_goal[:, 0].astype(jnp.int32)
    prefix_all = lax.all_gather(prefix_kv, "dp", axis=0, tiled=True)
    grad_q, grad_kv, partial = attend_all(
        slots, goals, prefix_len.astype(jnp.int32), coefficient,
        queries, out_grad, suffix_kv, prefix_all)
    prefix_grad = lax.psum_scatter(partial, "dp", scatter_dimension=0, tiled=True)
    return grad_q, grad_kv, prefix_grad.astype(jnp.bfloat16)


def pipelined(queries, suffix_kv, out_grad, prefix_kv, logratio, pair_slots, pair_goal, prefix_len):
    partner = [(i, i ^ 1) for i in range(4)]
    across = [(i, i ^ 2) for i in range(4)]
    pre_across = lax.ppermute(prefix_kv, "dp", across)
    pre_partner = lax.ppermute(prefix_kv, "dp", partner)
    me = lax.axis_index("dp").astype(jnp.int32).reshape(1)
    tables = (me, pair_goal.reshape(-1).astype(jnp.int32), pair_slots.reshape(-1).astype(jnp.int32),
              prefix_len.astype(jnp.int32), logratio)

    def run(flip, prefix_one, chain):
        grad_q, grad_kv, partial = attend_slot(flip, *tables, queries, out_grad, suffix_kv, prefix_one, chain)
        return (grad_q, grad_kv), partial

    chain, near = run(1, pre_partner, None)
    pre_across, near = lax.optimization_barrier((pre_across, near))
    pre_relay = lax.ppermute(pre_across, "dp", partner)
    near_sent = lax.ppermute(near, "dp", partner)
    chain, cross = run(2, pre_across, chain)
    chain, relay = run(3, pre_relay, chain)
    forward = (cross + lax.ppermute(relay, "dp", partner)).astype(jnp.bfloat16)
    forward, own_prefix = lax.optimization_barrier((forward, prefix_kv))
    chain, own = run(0, own_prefix, chain)
    total = own + near_sent + lax.ppermute(forward, "dp", across).astype(jnp.float32)
    return chain[0], chain[1], total.astype(jnp.bfloat16)


def solution(mesh):
    return jax.shard_map(
        shards,
        mesh=mesh,
        in_specs=(
            P(("groups", "dp"), None, "tensor"),
            P(("groups", "dp"), None, None, "tensor"),
            P(("groups", "dp"), None, "tensor"),
            P(("groups", "dp"), None, None, "tensor"),
            P(("groups", "dp")),
            P(("groups", "dp"), None),
            P(("groups", "dp"), None),
            P("groups"),
        ),
        out_specs=(
            P(("groups", "dp"), None, "tensor"),
            P(("groups", "dp"), None, None, "tensor"),
            P(("groups", "dp"), None, None, "tensor"),
        ),
        check_vma=False,
    )
```

```python
import functools

import jax
import jax.numpy as jnp
from jax import lax
from jax.experimental import pallas as pl
from jax.experimental.pallas import tpu as pltpu
from jax.sharding import PartitionSpec as P

HD = 128

dpo_beta = 0.5


def mask_bias(length, *, group, seq, prefix_rows):
    shape = (seq + prefix_rows, group * seq)
    key_index = lax.broadcasted_iota(jnp.int32, shape, 0)
    tok_index = lax.broadcasted_iota(jnp.int32, shape, 1) % seq
    in_suffix = key_index < seq
    allowed = (in_suffix & (key_index <= tok_index)) | (
        jnp.logical_not(in_suffix) & (key_index - seq < length))
    return jnp.where(allowed, 0.0, -1e30).astype(jnp.float32)


def attend_math(q_blk, og_blk, keys_pre, values_pre, keys_own, values_own, bias, coef, *, group, seq):
    scale = HD ** (-0.5)
    cot_blk = (coef * og_blk.astype(jnp.float32)).astype(jnp.bfloat16)
    q_rows = jnp.concatenate([q_blk[:, g * HD:(g + 1) * HD] for g in range(group)], 0)
    c_rows = jnp.concatenate([cot_blk[:, g * HD:(g + 1) * HD] for g in range(group)], 0)
    keys = jnp.concatenate([keys_own, keys_pre], 0)
    values = jnp.concatenate([values_own, values_pre], 0)

    nt = (((1,), (1,)), ((), ()))
    scores_t = lax.dot_general(keys, q_rows, nt, preferred_element_type=jnp.float32) * scale
    scores_t = scores_t + bias
    col_max = jnp.max(scores_t, 0, keepdims=True)
    raised = jnp.exp(scores_t - col_max)
    prob_t = raised * (1.0 / jnp.sum(raised, 0, keepdims=True))
    prob_low_t = prob_t.astype(jnp.bfloat16)
    output_t = jnp.dot(values.T, prob_low_t, preferred_element_type=jnp.float32)
    row_dot = jnp.sum(c_rows.T.astype(jnp.float32) * output_t, 0, keepdims=True)
    grad_prob_t = lax.dot_general(values, c_rows, nt, preferred_element_type=jnp.float32)
    grad_score_t = (prob_t * (grad_prob_t - row_dot)).astype(jnp.bfloat16)
    grad_q_t = jnp.dot(keys.T, grad_score_t, preferred_element_type=jnp.float32)
    grad_q = (scale * grad_q_t.T).astype(jnp.bfloat16)
    grad_k = scale * jnp.dot(grad_score_t, q_rows, preferred_element_type=jnp.float32)
    grad_v = jnp.dot(prob_low_t, c_rows, preferred_element_type=jnp.float32)
    return grad_q, grad_k, grad_v


def store_grads(grad_q, grad_k, grad_v, member, dq_ref, dkv_ref, dpre_ref, *, group, seq, prefix_rows):
    active = grad_k.shape[0] - seq
    for g in range(group):
        dq_ref[0, :, g * HD:(g + 1) * HD] = grad_q[g * seq:(g + 1) * seq]
    dkv_ref[0, 0] = grad_k[:seq].astype(jnp.bfloat16)
    dkv_ref[0, 1] = grad_v[:seq].astype(jnp.bfloat16)

    @pl.when(member == 0)
    def _():
        dpre_ref[0, 0, :active] = grad_k[seq:]
        dpre_ref[0, 1, :active] = grad_v[seq:]
        if active < prefix_rows:
            zeros = jnp.zeros((prefix_rows - active, HD), jnp.float32)
            dpre_ref[0, 0, active:] = zeros
            dpre_ref[0, 1, active:] = zeros

    @pl.when(member != 0)
    def _():
        dpre_ref[0, 0, :active] += grad_k[seq:]
        dpre_ref[0, 1, :active] += grad_v[seq:]


def attend_kernel(slots_ref, goal_ref, len_ref, coef_ref,
                  q_ref, og_ref, skv_ref, pkv_ref,
                  dq_ref, dkv_ref, dpre_ref, *, group, seq, prefix_rows):
    p = pl.program_id(0)
    member = pl.program_id(2)
    s = slots_ref[2 * p + member]
    length = len_ref[goal_ref[p]]
    bias = mask_bias(length, group=group, seq=seq, prefix_rows=prefix_rows)
    grads = attend_math(q_ref[0], og_ref[0], pkv_ref[0, 0], pkv_ref[0, 1], skv_ref[0, 0], skv_ref[0, 1],
                        bias, coef_ref[s], group=group, seq=seq)
    store_grads(*grads, member, dq_ref, dkv_ref, dpre_ref, group=group, seq=seq, prefix_rows=prefix_rows)


def pair_of(goal, goal_ref, pair_count):
    pair = 0
    for p in range(pair_count):
        pair = jnp.where(goal_ref[p] == goal, p, pair)
    return pair


def slot_kernel(me_ref, goal_ref, slots_ref, len_ref, lr_ref, q_ref, og_ref, skv_ref, pkv_ref, *rest,
                group, seq, prefix_rows, flip, pair_count, chained):
    if chained:
        rest = rest[2:]
    dq_ref, dkv_ref, dpre_ref, bias_ref = rest
    k = pl.program_id(0)
    member = pl.program_id(1)
    goal = me_ref[0] ^ flip
    pair = pair_of(goal, goal_ref, pair_count)
    length = len_ref[goal]
    dims = dict(group=group, seq=seq, prefix_rows=prefix_rows)

    @pl.when((k == 0) & (member == 0))
    def _():
        bias_ref[...] = mask_bias(length, **dims)

    gap = lr_ref[slots_ref[2 * pair]] - lr_ref[slots_ref[2 * pair + 1]]
    x = jnp.full((1, 128), -dpo_beta * gap, jnp.float32)
    weight = dpo_beta * (1.0 / (1.0 + jnp.exp(-x)))
    coef = jnp.where(member == 0, -weight, weight)[:, :1]
    blocks = (seq + length + 127) // 128
    for used in range(1, (seq + prefix_rows + 127) // 128 + 1):
        @pl.when(blocks == used)
        def _():
            width = min(used * 128, seq + prefix_rows)
            active = width - seq
            grads = attend_math(q_ref[0], og_ref[0], pkv_ref[0, 0, :active], pkv_ref[0, 1, :active],
                                skv_ref[0, 0], skv_ref[0, 1], bias_ref[:width], coef,
                                group=group, seq=seq)
            store_grads(*grads, member, dq_ref, dkv_ref, dpre_ref, **dims)


def attend_slot(flip, me, goals, slots, lengths, logratio, queries, out_grad, suffix_kv, prefix_one, chain):
    suffix_count, seq, qwidth = queries.shape
    kv_width = suffix_kv.shape[-1]
    kv_local = kv_width // HD
    group = qwidth // kv_width
    prefix_rows = prefix_one.shape[2]
    pair_count = goals.shape[0]
    qb = group * HD

    def suffix_of(m, me_ref, goal_ref, slots_ref):
        pair = pair_of(me_ref[0] ^ flip, goal_ref, pair_count)
        return slots_ref[2 * pair + m]

    def q_map(k, m, me_ref, goal_ref, slots_ref, len_ref):
        return (suffix_of(m, me_ref, goal_ref, slots_ref), 0, k)

    def skv_map(k, m, me_ref, goal_ref, slots_ref, len_ref):
        return (suffix_of(m, me_ref, goal_ref, slots_ref), 0, 0, k)

    def pkv_map(k, m, me_ref, goal_ref, slots_ref, len_ref):
        return (0, 0, 0, k)

    out_shape = (
        jax.ShapeDtypeStruct((suffix_count, seq, qwidth), jnp.bfloat16),
        jax.ShapeDtypeStruct((suffix_count, 2, seq, kv_width), jnp.bfloat16),
        jax.ShapeDtypeStruct((1, 2, prefix_rows, kv_width), jnp.float32),
    )
    in_specs = [
        pl.BlockSpec(memory_space=pltpu.SMEM),
        pl.BlockSpec((1, seq, qb), q_map),
        pl.BlockSpec((1, seq, qb), q_map),
        pl.BlockSpec((1, 2, seq, HD), skv_map),
        pl.BlockSpec((1, 2, prefix_rows, HD), pkv_map),
    ]
    operands = [logratio, queries, out_grad, suffix_kv, prefix_one]
    aliases = {}
    if chain is not None:
        in_specs += [pl.BlockSpec(memory_space=pl.ANY)] * 2
        operands += list(chain)
        aliases = {9: 0, 10: 1}
    kernel = functools.partial(slot_kernel, group=group, seq=seq, prefix_rows=prefix_rows, flip=flip,
                               pair_count=pair_count, chained=chain is not None)
    grid_spec = pltpu.PrefetchScalarGridSpec(
        num_scalar_prefetch=4,
        grid=(kv_local, 2),
        in_specs=in_specs,
        out_specs=[
            pl.BlockSpec((1, seq, qb), q_map),
            pl.BlockSpec((1, 2, seq, HD), skv_map),
            pl.BlockSpec((1, 2, prefix_rows, HD), pkv_map),
        ],
        scratch_shapes=[pltpu.VMEM((prefix_rows + seq, group * seq), jnp.float32)],
    )
    steps = 2 * kv_local
    cost = pl.CostEstimate(
        flops=steps * 2_200_000_000,
        transcendentals=steps * group * seq * (prefix_rows + seq),
        bytes_accessed=steps * (4 * seq * qb + 4 * seq * HD + 6 * prefix_rows * HD) * 2,
    )
    return pl.pallas_call(
        kernel,
        grid_spec=grid_spec,
        out_shape=out_shape,
        input_output_aliases=aliases,
        cost_estimate=cost,
        compiler_params=pltpu.CompilerParams(dimension_semantics=("arbitrary", "arbitrary")),
    )(me, goals, slots, lengths, *operands)


def attend_all(slots, goals, lengths, coef, queries, out_grad, suffix_kv, prefix_all):
    suffix_count, seq, qwidth = queries.shape
    kv_width = suffix_kv.shape[-1]
    kv_local = kv_width // HD
    group = qwidth // kv_width
    goal_count, _, prefix_rows, _ = prefix_all.shape
    pair_count = goals.shape[0]
    qb = group * HD

    def q_map(p, k, m, slots_ref, goal_ref, len_ref):
        return (slots_ref[2 * p + m], 0, k)

    def skv_map(p, k, m, slots_ref, goal_ref, len_ref):
        return (slots_ref[2 * p + m], 0, 0, k)

    def pkv_map(p, k, m, slots_ref, goal_ref, len_ref):
        return (goal_ref[p], 0, 0, k)

    kernel = functools.partial(attend_kernel, group=group, seq=seq, prefix_rows=prefix_rows)
    out_shape = (
        jax.ShapeDtypeStruct((suffix_count, seq, qwidth), jnp.bfloat16),
        jax.ShapeDtypeStruct((suffix_count, 2, seq, kv_width), jnp.bfloat16),
        jax.ShapeDtypeStruct((goal_count, 2, prefix_rows, kv_width), jnp.float32),
    )
    in_specs = [
        pl.BlockSpec(memory_space=pltpu.SMEM),
        pl.BlockSpec((1, seq, qb), q_map),
        pl.BlockSpec((1, seq, qb), q_map),
        pl.BlockSpec((1, 2, seq, HD), skv_map),
        pl.BlockSpec((1, 2, prefix_rows, HD), pkv_map),
    ]
    operands = [coef, queries, out_grad, suffix_kv, prefix_all]
    aliases = {}
    if pair_count < goal_count:
        in_specs.append(pl.BlockSpec(memory_space=pl.ANY))
        operands.append(jnp.zeros(out_shape[2].shape, jnp.float32))
        aliases = {3 + len(operands) - 1: 2}

        def kernel_with_zero(*refs):
            return kernel(*refs[:8], *refs[9:])
        body = kernel_with_zero
    else:
        body = kernel
    grid_spec = pltpu.PrefetchScalarGridSpec(
        num_scalar_prefetch=3,
        grid=(pair_count, kv_local, 2),
        in_specs=in_specs,
        out_specs=[
            pl.BlockSpec((1, seq, qb), q_map),
            pl.BlockSpec((1, 2, seq, HD), skv_map),
            pl.BlockSpec((1, 2, prefix_rows, HD), pkv_map),
        ],
    )
    return pl.pallas_call(
        body,
        grid_spec=grid_spec,
        out_shape=out_shape,
        input_output_aliases=aliases,
        compiler_params=pltpu.CompilerParams(
            dimension_semantics=("arbitrary", "arbitrary", "arbitrary")),
    )(slots, goals, lengths, *operands)


def shards(queries, suffix_kv, out_grad, prefix_kv, logratio, pair_slots, pair_goal, prefix_len):
    dp_size = lax.axis_size("dp")
    pair_count = pair_slots.shape[0]
    if dp_size == 4 and pair_count == dp_size:
        return pipelined(queries, suffix_kv, out_grad, prefix_kv, logratio,
                         pair_slots, pair_goal, prefix_len)
    suffix_count = queries.shape[0]
    chosen = pair_slots[:, 0]
    rejected = pair_slots[:, 1]
    positions = jnp.arange(suffix_count)
    pick_chosen = chosen[:, None] == positions[None, :]
    pick_rejected = rejected[:, None] == positions[None, :]
    ratio_chosen = jnp.sum(jnp.where(pick_chosen, logratio[None, :], 0.0), 1)
    ratio_rejected = jnp.sum(jnp.where(pick_rejected, logratio[None, :], 0.0), 1)
    weight = dpo_beta * jax.nn.sigmoid(-dpo_beta * (ratio_chosen - ratio_rejected))
    coefficient = jnp.sum(
        jnp.where(pick_rejected, weight[:, None], 0.0)
        - jnp.where(pick_chosen, weight[:, None], 0.0),
        0,
    )
    slots = pair_slots.reshape(-1).astype(jnp.int32)
    goals = pair_goal[:, 0].astype(jnp.int32)
    prefix_all = lax.all_gather(prefix_kv, "dp", axis=0, tiled=True)
    grad_q, grad_kv, partial = attend_all(
        slots, goals, prefix_len.astype(jnp.int32), coefficient,
        queries, out_grad, suffix_kv, prefix_all)
    prefix_grad = lax.psum_scatter(partial, "dp", scatter_dimension=0, tiled=True)
    return grad_q, grad_kv, prefix_grad.astype(jnp.bfloat16)


def pipelined(queries, suffix_kv, out_grad, prefix_kv, logratio, pair_slots, pair_goal, prefix_len):
    partner = [(i, i ^ 1) for i in range(4)]
    across = [(i, i ^ 2) for i in range(4)]
    pre_across = lax.ppermute(prefix_kv, "dp", across)
    pre_partner = lax.ppermute(prefix_kv, "dp", partner)
    me = lax.axis_index("dp").astype(jnp.int32).reshape(1)
    tables = (me, pair_goal.reshape(-1).astype(jnp.int32), pair_slots.reshape(-1).astype(jnp.int32),
              prefix_len.astype(jnp.int32), logratio)

    def run(flip, prefix_one, chain):
        grad_q, grad_kv, partial = attend_slot(flip, *tables, queries, out_grad, suffix_kv, prefix_one, chain)
        return (grad_q, grad_kv), partial

    chain, near = run(1, pre_partner, None)
    pre_across, near = lax.optimization_barrier((pre_across, near))
    pre_relay = lax.ppermute(pre_across, "dp", partner)
    near_sent = lax.ppermute(near, "dp", partner)
    chain, cross = run(2, pre_across, chain)
    chain, relay = run(3, pre_relay, chain)
    forward = (cross + lax.ppermute(relay, "dp", partner)).astype(jnp.bfloat16)
    forward, own_prefix = lax.optimization_barrier((forward, prefix_kv))
    chain, own = run(0, own_prefix, chain)
    total = own + near_sent + lax.ppermute(forward, "dp", across).astype(jnp.float32)
    return chain[0], chain[1], total.astype(jnp.bfloat16)


def solution(mesh):
    return jax.shard_map(
        shards,
        mesh=mesh,
        in_specs=(
            P(("groups", "dp"), None, "tensor"),
            P(("groups", "dp"), None, None, "tensor"),
            P(("groups", "dp"), None, "tensor"),
            P(("groups", "dp"), None, None, "tensor"),
            P(("groups", "dp")),
            P(("groups", "dp"), None),
            P(("groups", "dp"), None),
            P("groups"),
        ),
        out_specs=(
            P(("groups", "dp"), None, "tensor"),
            P(("groups", "dp"), None, None, "tensor"),
            P(("groups", "dp"), None, None, "tensor"),
        ),
        check_vma=False,
    )
```

```python
import functools

import jax
import jax.numpy as jnp
from jax import lax
from jax.experimental import pallas as pl
from jax.experimental.pallas import tpu as pltpu
from jax.sharding import PartitionSpec as P

HD = 128

dpo_beta = 0.5


def mask_bias(length, *, group, seq, prefix_rows):
    shape = (seq + prefix_rows, group * seq)
    key_index = lax.broadcasted_iota(jnp.int32, shape, 0)
    tok_index = lax.broadcasted_iota(jnp.int32, shape, 1) % seq
    in_suffix = key_index < seq
    allowed = (in_suffix & (key_index <= tok_index)) | (
        jnp.logical_not(in_suffix) & (key_index - seq < length))
    return jnp.where(allowed, 0.0, -1e30).astype(jnp.float32)


def attend_math(q_blk, og_blk, keys_pre, values_pre, keys_own, values_own, bias, coef, *, group, seq):
    scale = HD ** (-0.5)
    cot_blk = (coef * og_blk.astype(jnp.float32)).astype(jnp.bfloat16)
    q_rows = jnp.concatenate([q_blk[:, g * HD:(g + 1) * HD] for g in range(group)], 0)
    c_rows = jnp.concatenate([cot_blk[:, g * HD:(g + 1) * HD] for g in range(group)], 0)
    keys = jnp.concatenate([keys_own, keys_pre], 0)
    values = jnp.concatenate([values_own, values_pre], 0)

    nt = (((1,), (1,)), ((), ()))
    scores_t = lax.dot_general(keys, q_rows, nt, preferred_element_type=jnp.float32) * scale
    scores_t = scores_t + bias
    col_max = jnp.max(scores_t, 0, keepdims=True)
    raised = jnp.exp(scores_t - col_max)
    prob_t = raised * (1.0 / jnp.sum(raised, 0, keepdims=True))
    prob_low_t = prob_t.astype(jnp.bfloat16)
    output_t = jnp.dot(values.T, prob_low_t, preferred_element_type=jnp.float32)
    row_dot = jnp.sum(c_rows.T.astype(jnp.float32) * output_t, 0, keepdims=True)
    grad_prob_t = lax.dot_general(values, c_rows, nt, preferred_element_type=jnp.float32)
    grad_score_t = (prob_t * (grad_prob_t - row_dot)).astype(jnp.bfloat16)
    grad_q_t = jnp.dot(keys.T, grad_score_t, preferred_element_type=jnp.float32)
    grad_q = (scale * grad_q_t.T).astype(jnp.bfloat16)
    grad_k = scale * jnp.dot(grad_score_t, q_rows, preferred_element_type=jnp.float32)
    grad_v = jnp.dot(prob_low_t, c_rows, preferred_element_type=jnp.float32)
    return grad_q, grad_k, grad_v


def store_grads(grad_q, grad_k, grad_v, member, dq_ref, dkv_ref, dpre_ref, *, group, seq, prefix_rows):
    active = grad_k.shape[0] - seq
    for g in range(group):
        dq_ref[0, :, g * HD:(g + 1) * HD] = grad_q[g * seq:(g + 1) * seq]
    dkv_ref[0, 0] = grad_k[:seq].astype(jnp.bfloat16)
    dkv_ref[0, 1] = grad_v[:seq].astype(jnp.bfloat16)

    @pl.when(member == 0)
    def _():
        dpre_ref[0, 0, :active] = grad_k[seq:]
        dpre_ref[0, 1, :active] = grad_v[seq:]
        if active < prefix_rows:
            zeros = jnp.zeros((prefix_rows - active, HD), jnp.float32)
            dpre_ref[0, 0, active:] = zeros
            dpre_ref[0, 1, active:] = zeros

    @pl.when(member != 0)
    def _():
        dpre_ref[0, 0, :active] += grad_k[seq:]
        dpre_ref[0, 1, :active] += grad_v[seq:]


def attend_kernel(slots_ref, goal_ref, len_ref, coef_ref,
                  q_ref, og_ref, skv_ref, pkv_ref,
                  dq_ref, dkv_ref, dpre_ref, *, group, seq, prefix_rows):
    p = pl.program_id(0)
    member = pl.program_id(2)
    s = slots_ref[2 * p + member]
    length = len_ref[goal_ref[p]]
    bias = mask_bias(length, group=group, seq=seq, prefix_rows=prefix_rows)
    grads = attend_math(q_ref[0], og_ref[0], pkv_ref[0, 0], pkv_ref[0, 1], skv_ref[0, 0], skv_ref[0, 1],
                        bias, coef_ref[s], group=group, seq=seq)
    store_grads(*grads, member, dq_ref, dkv_ref, dpre_ref, group=group, seq=seq, prefix_rows=prefix_rows)


def pair_of(goal, goal_ref, pair_count):
    pair = 0
    for p in range(pair_count):
        pair = jnp.where(goal_ref[p, 0] == goal, p, pair)
    return pair


def slot_kernel(me_ref, goal_ref, slots_ref, len_ref, lr_ref, q_ref, og_ref, skv_ref, pkv_ref, *rest,
                group, seq, prefix_rows, flip, pair_count, chained, seeded, low):
    if chained:
        rest = rest[2:]
    seed_ref = None
    if seeded:
        seed_ref, rest = rest[0], rest[1:]
    dq_ref, dkv_ref, dpre_ref, bias_ref = rest[:4]
    acc_ref = rest[4] if low else dpre_ref
    k = pl.program_id(0)
    member = pl.program_id(1)
    goal = me_ref[0] ^ flip
    pair = pair_of(goal, goal_ref, pair_count)
    length = len_ref[goal]
    dims = dict(group=group, seq=seq, prefix_rows=prefix_rows)

    @pl.when((k == 0) & (member == 0))
    def _():
        bias_ref[...] = mask_bias(length, **dims)

    gap = lr_ref[slots_ref[pair, 0]] - lr_ref[slots_ref[pair, 1]]
    x = jnp.full((1, 128), -dpo_beta * gap, jnp.float32)
    weight = dpo_beta * (1.0 / (1.0 + jnp.exp(-x)))
    coef = jnp.where(member == 0, -weight, weight)[:, :1]
    blocks = (seq + length + 127) // 128
    for used in range(1, (seq + prefix_rows + 127) // 128 + 1):
        @pl.when(blocks == used)
        def _():
            width = min(used * 128, seq + prefix_rows)
            grads = attend_math(q_ref[0], og_ref[0], pkv_ref[0, 0, :width - seq], pkv_ref[0, 1, :width - seq],
                                skv_ref[0, 0], skv_ref[0, 1], bias_ref[:width], coef,
                                group=group, seq=seq)
            store_grads(*grads, member, dq_ref, dkv_ref, acc_ref, **dims)

    if seeded:
        @pl.when(member == 1)
        def _():
            dpre_ref[...] += seed_ref[...]
    if low:
        @pl.when(member == 1)
        def _():
            dpre_ref[...] = acc_ref[...].astype(dpre_ref.dtype)


def attend_slot(flip, me, goals, slots, lengths, logratio, queries, out_grad, suffix_kv, prefix_one, chain,
                seed=None, low=False):
    suffix_count, seq, qwidth = queries.shape
    kv_width = suffix_kv.shape[-1]
    kv_local = kv_width // HD
    group = qwidth // kv_width
    prefix_rows = prefix_one.shape[2]
    pair_count = goals.shape[0]
    qb = group * HD

    def suffix_of(m, me_ref, goal_ref, slots_ref):
        pair = pair_of(me_ref[0] ^ flip, goal_ref, pair_count)
        return slots_ref[pair, m]

    def q_map(k, m, me_ref, goal_ref, slots_ref, len_ref):
        return (suffix_of(m, me_ref, goal_ref, slots_ref), 0, k)

    def skv_map(k, m, me_ref, goal_ref, slots_ref, len_ref):
        return (suffix_of(m, me_ref, goal_ref, slots_ref), 0, 0, k)

    def pkv_map(k, m, me_ref, goal_ref, slots_ref, len_ref):
        return (0, 0, 0, k)

    out_shape = (
        jax.ShapeDtypeStruct((suffix_count, seq, qwidth), jnp.bfloat16),
        jax.ShapeDtypeStruct((suffix_count, 2, seq, kv_width), jnp.bfloat16),
        jax.ShapeDtypeStruct((1, 2, prefix_rows, kv_width), jnp.bfloat16 if low else jnp.float32),
    )
    in_specs = [
        pl.BlockSpec(memory_space=pltpu.SMEM),
        pl.BlockSpec((1, seq, qb), q_map),
        pl.BlockSpec((1, seq, qb), q_map),
        pl.BlockSpec((1, 2, seq, HD), skv_map),
        pl.BlockSpec((1, 2, prefix_rows, HD), pkv_map),
    ]
    operands = [logratio, queries, out_grad, suffix_kv, prefix_one]
    aliases = {}
    if chain is not None:
        in_specs += [pl.BlockSpec(memory_space=pl.ANY)] * 2
        operands += list(chain)
        aliases = {9: 0, 10: 1}
    if seed is not None:
        in_specs.append(pl.BlockSpec((1, 2, prefix_rows, HD), pkv_map))
        operands.append(seed)
    scratch = [pltpu.VMEM((prefix_rows + seq, group * seq), jnp.float32)]
    if low:
        scratch.append(pltpu.VMEM((1, 2, prefix_rows, HD), jnp.float32))
    kernel = functools.partial(slot_kernel, group=group, seq=seq, prefix_rows=prefix_rows, flip=flip,
                               pair_count=pair_count, chained=chain is not None, seeded=seed is not None,
                               low=low)
    grid_spec = pltpu.PrefetchScalarGridSpec(
        num_scalar_prefetch=4,
        grid=(kv_local, 2),
        in_specs=in_specs,
        out_specs=[
            pl.BlockSpec((1, seq, qb), q_map),
            pl.BlockSpec((1, 2, seq, HD), skv_map),
            pl.BlockSpec((1, 2, prefix_rows, HD), pkv_map),
        ],
        scratch_shapes=scratch,
    )
    steps = 2 * kv_local
    cost = pl.CostEstimate(
        flops=steps * 2_200_000_000,
        transcendentals=steps * group * seq * (prefix_rows + seq),
        bytes_accessed=steps * (4 * seq * qb + 4 * seq * HD + 6 * prefix_rows * HD) * 2,
    )
    return pl.pallas_call(
        kernel,
        grid_spec=grid_spec,
        out_shape=out_shape,
        input_output_aliases=aliases,
        cost_estimate=cost,
        compiler_params=pltpu.CompilerParams(dimension_semantics=("arbitrary", "arbitrary")),
    )(me, goals, slots, lengths, *operands)


def attend_all(slots, goals, lengths, coef, queries, out_grad, suffix_kv, prefix_all):
    suffix_count, seq, qwidth = queries.shape
    kv_width = suffix_kv.shape[-1]
    kv_local = kv_width // HD
    group = qwidth // kv_width
    goal_count, _, prefix_rows, _ = prefix_all.shape
    pair_count = goals.shape[0]
    qb = group * HD

    def q_map(p, k, m, slots_ref, goal_ref, len_ref):
        return (slots_ref[2 * p + m], 0, k)

    def skv_map(p, k, m, slots_ref, goal_ref, len_ref):
        return (slots_ref[2 * p + m], 0, 0, k)

    def pkv_map(p, k, m, slots_ref, goal_ref, len_ref):
        return (goal_ref[p], 0, 0, k)

    kernel = functools.partial(attend_kernel, group=group, seq=seq, prefix_rows=prefix_rows)
    out_shape = (
        jax.ShapeDtypeStruct((suffix_count, seq, qwidth), jnp.bfloat16),
        jax.ShapeDtypeStruct((suffix_count, 2, seq, kv_width), jnp.bfloat16),
        jax.ShapeDtypeStruct((goal_count, 2, prefix_rows, kv_width), jnp.float32),
    )
    in_specs = [
        pl.BlockSpec(memory_space=pltpu.SMEM),
        pl.BlockSpec((1, seq, qb), q_map),
        pl.BlockSpec((1, seq, qb), q_map),
        pl.BlockSpec((1, 2, seq, HD), skv_map),
        pl.BlockSpec((1, 2, prefix_rows, HD), pkv_map),
    ]
    operands = [coef, queries, out_grad, suffix_kv, prefix_all]
    aliases = {}
    if pair_count < goal_count:
        in_specs.append(pl.BlockSpec(memory_space=pl.ANY))
        operands.append(jnp.zeros(out_shape[2].shape, jnp.float32))
        aliases = {3 + len(operands) - 1: 2}

        def kernel_with_zero(*refs):
            return kernel(*refs[:8], *refs[9:])
        body = kernel_with_zero
    else:
        body = kernel
    grid_spec = pltpu.PrefetchScalarGridSpec(
        num_scalar_prefetch=3,
        grid=(pair_count, kv_local, 2),
        in_specs=in_specs,
        out_specs=[
            pl.BlockSpec((1, seq, qb), q_map),
            pl.BlockSpec((1, 2, seq, HD), skv_map),
            pl.BlockSpec((1, 2, prefix_rows, HD), pkv_map),
        ],
    )
    return pl.pallas_call(
        body,
        grid_spec=grid_spec,
        out_shape=out_shape,
        input_output_aliases=aliases,
        compiler_params=pltpu.CompilerParams(
            dimension_semantics=("arbitrary", "arbitrary", "arbitrary")),
    )(slots, goals, lengths, *operands)


def shards(queries, suffix_kv, out_grad, prefix_kv, logratio, pair_slots, pair_goal, prefix_len):
    dp_size = lax.axis_size("dp")
    pair_count = pair_slots.shape[0]
    if dp_size == 4 and pair_count == dp_size:
        return pipelined(queries, suffix_kv, out_grad, prefix_kv, logratio,
                         pair_slots, pair_goal, prefix_len)
    suffix_count = queries.shape[0]
    chosen = pair_slots[:, 0]
    rejected = pair_slots[:, 1]
    positions = jnp.arange(suffix_count)
    pick_chosen = chosen[:, None] == positions[None, :]
    pick_rejected = rejected[:, None] == positions[None, :]
    ratio_chosen = jnp.sum(jnp.where(pick_chosen, logratio[None, :], 0.0), 1)
    ratio_rejected = jnp.sum(jnp.where(pick_rejected, logratio[None, :], 0.0), 1)
    weight = dpo_beta * jax.nn.sigmoid(-dpo_beta * (ratio_chosen - ratio_rejected))
    coefficient = jnp.sum(
        jnp.where(pick_rejected, weight[:, None], 0.0)
        - jnp.where(pick_chosen, weight[:, None], 0.0),
        0,
    )
    slots = pair_slots.reshape(-1).astype(jnp.int32)
    goals = pair_goal[:, 0].astype(jnp.int32)
    prefix_all = lax.all_gather(prefix_kv, "dp", axis=0, tiled=True)
    grad_q, grad_kv, partial = attend_all(
        slots, goals, prefix_len.astype(jnp.int32), coefficient,
        queries, out_grad, suffix_kv, prefix_all)
    prefix_grad = lax.psum_scatter(partial, "dp", scatter_dimension=0, tiled=True)
    return grad_q, grad_kv, prefix_grad.astype(jnp.bfloat16)


def pipelined(queries, suffix_kv, out_grad, prefix_kv, logratio, pair_slots, pair_goal, prefix_len):
    partner = [(i, i ^ 1) for i in range(4)]
    across = [(i, i ^ 2) for i in range(4)]
    pre_across = lax.ppermute(prefix_kv, "dp", across)
    pre_partner = lax.ppermute(prefix_kv, "dp", partner)
    me = lax.axis_index("dp").astype(jnp.int32).reshape(1)
    tables = (me, pair_goal.astype(jnp.int32), pair_slots.astype(jnp.int32),
              prefix_len.astype(jnp.int32), logratio)

    def run(flip, prefix_one, chain, **extra):
        grad_q, grad_kv, partial = attend_slot(flip, *tables, queries, out_grad, suffix_kv, prefix_one, chain,
                                               **extra)
        return (grad_q, grad_kv), partial

    chain, near = run(1, pre_partner, None)
    pre_across, near = lax.optimization_barrier((pre_across, near))
    pre_relay = lax.ppermute(pre_across, "dp", partner)
    near_sent = lax.ppermute(near, "dp", partner)
    chain, cross = run(2, pre_across, chain)
    chain, relay = run(3, pre_relay, chain, low=True)
    forward = (cross + lax.ppermute(relay, "dp", partner).astype(jnp.float32)).astype(jnp.bfloat16)
    forward, own_prefix = lax.optimization_barrier((forward, prefix_kv))
    chain, own = run(0, own_prefix, chain, seed=near_sent)
    total = own + lax.ppermute(forward, "dp", across).astype(jnp.float32)
    return chain[0], chain[1], total.astype(jnp.bfloat16)


def solution(mesh):
    return jax.shard_map(
        shards,
        mesh=mesh,
        in_specs=(
            P(("groups", "dp"), None, "tensor"),
            P(("groups", "dp"), None, None, "tensor"),
            P(("groups", "dp"), None, "tensor"),
            P(("groups", "dp"), None, None, "tensor"),
            P(("groups", "dp")),
            P(("groups", "dp"), None),
            P(("groups", "dp"), None),
            P("groups"),
        ),
        out_specs=(
            P(("groups", "dp"), None, "tensor"),
            P(("groups", "dp"), None, None, "tensor"),
            P(("groups", "dp"), None, None, "tensor"),
        ),
        check_vma=False,
    )
```

```python
import functools

import jax
import jax.numpy as jnp
from jax import lax
from jax.experimental import pallas as pl
from jax.experimental.pallas import tpu as pltpu
from jax.sharding import PartitionSpec as P

HD = 128

dpo_beta = 0.5


def mask_bias(length, *, group, seq, prefix_rows):
    shape = (seq + prefix_rows, group * seq)
    key_index = lax.broadcasted_iota(jnp.int32, shape, 0)
    tok_index = lax.broadcasted_iota(jnp.int32, shape, 1) % seq
    in_suffix = key_index < seq
    allowed = (in_suffix & (key_index <= tok_index)) | (
        jnp.logical_not(in_suffix) & (key_index - seq < length))
    return jnp.where(allowed, 0.0, -1e30).astype(jnp.float32)


def attend_math(q_blk, og_blk, keys_pre, values_pre, keys_own, values_own, bias, coef, *, group, seq):
    scale = HD ** (-0.5)
    cot_blk = (coef * og_blk.astype(jnp.float32)).astype(jnp.bfloat16)
    q_rows = jnp.concatenate([q_blk[:, g * HD:(g + 1) * HD] for g in range(group)], 0)
    c_rows = jnp.concatenate([cot_blk[:, g * HD:(g + 1) * HD] for g in range(group)], 0)
    keys = jnp.concatenate([keys_own, keys_pre], 0)
    values = jnp.concatenate([values_own, values_pre], 0)

    nt = (((1,), (1,)), ((), ()))
    scores_t = lax.dot_general(keys, q_rows, nt, preferred_element_type=jnp.float32) * scale
    scores_t = scores_t + bias
    col_max = jnp.max(scores_t, 0, keepdims=True)
    raised = jnp.exp(scores_t - col_max)
    prob_t = raised * (1.0 / jnp.sum(raised, 0, keepdims=True))
    prob_low_t = prob_t.astype(jnp.bfloat16)
    output_t = jnp.dot(values.T, prob_low_t, preferred_element_type=jnp.float32)
    row_dot = jnp.sum(c_rows.T.astype(jnp.float32) * output_t, 0, keepdims=True)
    grad_prob_t = lax.dot_general(values, c_rows, nt, preferred_element_type=jnp.float32)
    grad_score_t = (prob_t * (grad_prob_t - row_dot)).astype(jnp.bfloat16)
    grad_q_t = jnp.dot(keys.T, grad_score_t, preferred_element_type=jnp.float32)
    grad_q = (scale * grad_q_t.T).astype(jnp.bfloat16)
    grad_k = scale * jnp.dot(grad_score_t, q_rows, preferred_element_type=jnp.float32)
    grad_v = jnp.dot(prob_low_t, c_rows, preferred_element_type=jnp.float32)
    return grad_q, grad_k, grad_v


def store_grads(grad_q, grad_k, grad_v, member, dq_ref, dkv_ref, dpre_ref, *, group, seq, prefix_rows):
    active = grad_k.shape[0] - seq
    for g in range(group):
        dq_ref[0, :, g * HD:(g + 1) * HD] = grad_q[g * seq:(g + 1) * seq]
    dkv_ref[0, 0] = grad_k[:seq].astype(jnp.bfloat16)
    dkv_ref[0, 1] = grad_v[:seq].astype(jnp.bfloat16)

    @pl.when(member == 0)
    def _():
        dpre_ref[0, 0, :active] = grad_k[seq:]
        dpre_ref[0, 1, :active] = grad_v[seq:]
        if active < prefix_rows:
            zeros = jnp.zeros((prefix_rows - active, HD), jnp.float32)
            dpre_ref[0, 0, active:] = zeros
            dpre_ref[0, 1, active:] = zeros

    @pl.when(member != 0)
    def _():
        dpre_ref[0, 0, :active] += grad_k[seq:]
        dpre_ref[0, 1, :active] += grad_v[seq:]


def attend_kernel(slots_ref, goal_ref, len_ref, coef_ref,
                  q_ref, og_ref, skv_ref, pkv_ref,
                  dq_ref, dkv_ref, dpre_ref, *, group, seq, prefix_rows):
    p = pl.program_id(0)
    member = pl.program_id(2)
    s = slots_ref[2 * p + member]
    length = len_ref[goal_ref[p]]
    bias = mask_bias(length, group=group, seq=seq, prefix_rows=prefix_rows)
    grads = attend_math(q_ref[0], og_ref[0], pkv_ref[0, 0], pkv_ref[0, 1], skv_ref[0, 0], skv_ref[0, 1],
                        bias, coef_ref[s], group=group, seq=seq)
    store_grads(*grads, member, dq_ref, dkv_ref, dpre_ref, group=group, seq=seq, prefix_rows=prefix_rows)


def pair_of(goal, goal_ref, pair_count):
    pair = 0
    for p in range(pair_count):
        pair = jnp.where(goal_ref[p] == goal, p, pair)
    return pair


def slot_kernel(me_ref, goal_ref, slots_ref, len_ref, lr_ref, q_ref, og_ref, skv_ref, pkv_ref, *rest,
                group, seq, prefix_rows, flip, pair_count, chained, seeded, low):
    if chained:
        rest = rest[2:]
    seed_ref = None
    if seeded:
        seed_ref, rest = rest[0], rest[1:]
    dq_ref, dkv_ref, dpre_ref, bias_ref = rest[:4]
    acc_ref = rest[4] if low else dpre_ref
    k = pl.program_id(0)
    member = pl.program_id(1)
    goal = me_ref[0] ^ flip
    pair = pair_of(goal, goal_ref, pair_count)
    length = len_ref[goal]
    dims = dict(group=group, seq=seq, prefix_rows=prefix_rows)

    @pl.when((k == 0) & (member == 0))
    def _():
        bias_ref[...] = mask_bias(length, **dims)

    gap = lr_ref[slots_ref[pair, 0]] - lr_ref[slots_ref[pair, 1]]
    x = jnp.full((1, 128), -dpo_beta * gap, jnp.float32)
    weight = dpo_beta * (1.0 / (1.0 + jnp.exp(-x)))
    coef = jnp.where(member == 0, -weight, weight)[:, :1]
    blocks = (seq + length + 127) // 128
    for used in range(1, (seq + prefix_rows + 127) // 128 + 1):
        @pl.when(blocks == used)
        def _():
            width = min(used * 128, seq + prefix_rows)
            grads = attend_math(q_ref[0], og_ref[0], pkv_ref[0, 0, :width - seq], pkv_ref[0, 1, :width - seq],
                                skv_ref[0, 0], skv_ref[0, 1], bias_ref[:width], coef,
                                group=group, seq=seq)
            store_grads(*grads, member, dq_ref, dkv_ref, acc_ref, **dims)

    if seeded:
        @pl.when(member == 1)
        def _():
            dpre_ref[...] += seed_ref[...]
    if low:
        @pl.when(member == 1)
        def _():
            dpre_ref[...] = acc_ref[...].astype(dpre_ref.dtype)


def attend_slot(flip, me, goals, slots, lengths, logratio, queries, out_grad, suffix_kv, prefix_one, chain,
                seed=None, low=False):
    suffix_count, seq, qwidth = queries.shape
    kv_width = suffix_kv.shape[-1]
    kv_local = kv_width // HD
    group = qwidth // kv_width
    prefix_rows = prefix_one.shape[2]
    pair_count = goals.shape[0]
    qb = group * HD

    def suffix_of(m, me_ref, goal_ref, slots_ref):
        pair = pair_of(me_ref[0] ^ flip, goal_ref, pair_count)
        return slots_ref[pair, m]

    def q_map(k, m, me_ref, goal_ref, slots_ref, len_ref):
        return (suffix_of(m, me_ref, goal_ref, slots_ref), 0, k)

    def skv_map(k, m, me_ref, goal_ref, slots_ref, len_ref):
        return (suffix_of(m, me_ref, goal_ref, slots_ref), 0, 0, k)

    def pkv_map(k, m, me_ref, goal_ref, slots_ref, len_ref):
        return (0, 0, 0, k)

    out_shape = (
        jax.ShapeDtypeStruct((suffix_count, seq, qwidth), jnp.bfloat16),
        jax.ShapeDtypeStruct((suffix_count, 2, seq, kv_width), jnp.bfloat16),
        jax.ShapeDtypeStruct((1, 2, prefix_rows, kv_width), jnp.bfloat16 if low else jnp.float32),
    )
    in_specs = [
        pl.BlockSpec(memory_space=pltpu.SMEM),
        pl.BlockSpec((1, seq, qb), q_map),
        pl.BlockSpec((1, seq, qb), q_map),
        pl.BlockSpec((1, 2, seq, HD), skv_map),
        pl.BlockSpec((1, 2, prefix_rows, HD), pkv_map),
    ]
    operands = [logratio, queries, out_grad, suffix_kv, prefix_one]
    aliases = {}
    if chain is not None:
        in_specs += [pl.BlockSpec(memory_space=pl.ANY)] * 2
        operands += list(chain)
        aliases = {9: 0, 10: 1}
    if seed is not None:
        in_specs.append(pl.BlockSpec((1, 2, prefix_rows, HD), pkv_map))
        operands.append(seed)
    scratch = [pltpu.VMEM((prefix_rows + seq, group * seq), jnp.float32)]
    if low:
        scratch.append(pltpu.VMEM((1, 2, prefix_rows, HD), jnp.float32))
    kernel = functools.partial(slot_kernel, group=group, seq=seq, prefix_rows=prefix_rows, flip=flip,
                               pair_count=pair_count, chained=chain is not None, seeded=seed is not None,
                               low=low)
    grid_spec = pltpu.PrefetchScalarGridSpec(
        num_scalar_prefetch=4,
        grid=(kv_local, 2),
        in_specs=in_specs,
        out_specs=[
            pl.BlockSpec((1, seq, qb), q_map),
            pl.BlockSpec((1, 2, seq, HD), skv_map),
            pl.BlockSpec((1, 2, prefix_rows, HD), pkv_map),
        ],
        scratch_shapes=scratch,
    )
    steps = 2 * kv_local
    cost = pl.CostEstimate(
        flops=steps * 2_200_000_000,
        transcendentals=steps * group * seq * (prefix_rows + seq),
        bytes_accessed=steps * (4 * seq * qb + 4 * seq * HD + 6 * prefix_rows * HD) * 2,
    )
    return pl.pallas_call(
        kernel,
        grid_spec=grid_spec,
        out_shape=out_shape,
        input_output_aliases=aliases,
        cost_estimate=cost,
        compiler_params=pltpu.CompilerParams(dimension_semantics=("arbitrary", "arbitrary")),
    )(me, goals, slots, lengths, *operands)


def attend_all(slots, goals, lengths, coef, queries, out_grad, suffix_kv, prefix_all):
    suffix_count, seq, qwidth = queries.shape
    kv_width = suffix_kv.shape[-1]
    kv_local = kv_width // HD
    group = qwidth // kv_width
    goal_count, _, prefix_rows, _ = prefix_all.shape
    pair_count = goals.shape[0]
    qb = group * HD

    def q_map(p, k, m, slots_ref, goal_ref, len_ref):
        return (slots_ref[2 * p + m], 0, k)

    def skv_map(p, k, m, slots_ref, goal_ref, len_ref):
        return (slots_ref[2 * p + m], 0, 0, k)

    def pkv_map(p, k, m, slots_ref, goal_ref, len_ref):
        return (goal_ref[p], 0, 0, k)

    kernel = functools.partial(attend_kernel, group=group, seq=seq, prefix_rows=prefix_rows)
    out_shape = (
        jax.ShapeDtypeStruct((suffix_count, seq, qwidth), jnp.bfloat16),
        jax.ShapeDtypeStruct((suffix_count, 2, seq, kv_width), jnp.bfloat16),
        jax.ShapeDtypeStruct((goal_count, 2, prefix_rows, kv_width), jnp.float32),
    )
    in_specs = [
        pl.BlockSpec(memory_space=pltpu.SMEM),
        pl.BlockSpec((1, seq, qb), q_map),
        pl.BlockSpec((1, seq, qb), q_map),
        pl.BlockSpec((1, 2, seq, HD), skv_map),
        pl.BlockSpec((1, 2, prefix_rows, HD), pkv_map),
    ]
    operands = [coef, queries, out_grad, suffix_kv, prefix_all]
    aliases = {}
    if pair_count < goal_count:
        in_specs.append(pl.BlockSpec(memory_space=pl.ANY))
        operands.append(jnp.zeros(out_shape[2].shape, jnp.float32))
        aliases = {3 + len(operands) - 1: 2}

        def kernel_with_zero(*refs):
            return kernel(*refs[:8], *refs[9:])
        body = kernel_with_zero
    else:
        body = kernel
    grid_spec = pltpu.PrefetchScalarGridSpec(
        num_scalar_prefetch=3,
        grid=(pair_count, kv_local, 2),
        in_specs=in_specs,
        out_specs=[
            pl.BlockSpec((1, seq, qb), q_map),
            pl.BlockSpec((1, 2, seq, HD), skv_map),
            pl.BlockSpec((1, 2, prefix_rows, HD), pkv_map),
        ],
    )
    return pl.pallas_call(
        body,
        grid_spec=grid_spec,
        out_shape=out_shape,
        input_output_aliases=aliases,
        compiler_params=pltpu.CompilerParams(
            dimension_semantics=("arbitrary", "arbitrary", "arbitrary")),
    )(slots, goals, lengths, *operands)


def shards(queries, suffix_kv, out_grad, prefix_kv, logratio, pair_slots, pair_goal, prefix_len):
    dp_size = lax.axis_size("dp")
    pair_count = pair_slots.shape[0]
    if dp_size == 4 and pair_count == dp_size:
        return pipelined(queries, suffix_kv, out_grad, prefix_kv, logratio,
                         pair_slots, pair_goal, prefix_len)
    suffix_count = queries.shape[0]
    chosen = pair_slots[:, 0]
    rejected = pair_slots[:, 1]
    positions = jnp.arange(suffix_count)
    pick_chosen = chosen[:, None] == positions[None, :]
    pick_rejected = rejected[:, None] == positions[None, :]
    ratio_chosen = jnp.sum(jnp.where(pick_chosen, logratio[None, :], 0.0), 1)
    ratio_rejected = jnp.sum(jnp.where(pick_rejected, logratio[None, :], 0.0), 1)
    weight = dpo_beta * jax.nn.sigmoid(-dpo_beta * (ratio_chosen - ratio_rejected))
    coefficient = jnp.sum(
        jnp.where(pick_rejected, weight[:, None], 0.0)
        - jnp.where(pick_chosen, weight[:, None], 0.0),
        0,
    )
    slots = pair_slots.reshape(-1).astype(jnp.int32)
    goals = pair_goal[:, 0].astype(jnp.int32)
    prefix_all = lax.all_gather(prefix_kv, "dp", axis=0, tiled=True)
    grad_q, grad_kv, partial = attend_all(
        slots, goals, prefix_len.astype(jnp.int32), coefficient,
        queries, out_grad, suffix_kv, prefix_all)
    prefix_grad = lax.psum_scatter(partial, "dp", scatter_dimension=0, tiled=True)
    return grad_q, grad_kv, prefix_grad.astype(jnp.bfloat16)


def add_round_kernel(a_ref, b_ref, o_ref):
    o_ref[...] = (a_ref[...] + b_ref[...].astype(jnp.float32)).astype(o_ref.dtype)


def add_round(a, b):
    return pl.pallas_call(
        add_round_kernel,
        out_shape=jax.ShapeDtypeStruct(a.shape, jnp.bfloat16),
        in_specs=[pl.BlockSpec(memory_space=pltpu.VMEM)] * 2,
        out_specs=pl.BlockSpec(memory_space=pltpu.VMEM),
    )(a, b)


def pipelined(queries, suffix_kv, out_grad, prefix_kv, logratio, pair_slots, pair_goal, prefix_len):
    partner = [(i, i ^ 1) for i in range(4)]
    across = [(i, i ^ 2) for i in range(4)]
    pre_across = lax.ppermute(prefix_kv, "dp", across)
    pre_partner = lax.ppermute(prefix_kv, "dp", partner)
    me = lax.axis_index("dp").astype(jnp.int32).reshape(1)
    tables = (me, pair_goal.reshape(-1).astype(jnp.int32), pair_slots.astype(jnp.int32),
              prefix_len.astype(jnp.int32), logratio)

    def run(flip, prefix_one, chain, **extra):
        grad_q, grad_kv, partial = attend_slot(flip, *tables, queries, out_grad, suffix_kv, prefix_one, chain,
                                               **extra)
        return (grad_q, grad_kv), partial

    chain, near = run(1, pre_partner, None)
    pre_across, near = lax.optimization_barrier((pre_across, near))
    pre_relay = lax.ppermute(pre_across, "dp", partner)
    near_sent = lax.ppermute(near, "dp", partner)
    chain, cross = run(2, pre_across, chain)
    chain, relay = run(3, pre_relay, chain, low=True)
    forward = (cross + lax.ppermute(relay, "dp", partner).astype(jnp.float32)).astype(jnp.bfloat16)
    forward, own_prefix = lax.optimization_barrier((forward, prefix_kv))
    chain, own = run(0, own_prefix, chain, seed=near_sent)
    return chain[0], chain[1], add_round(own, lax.ppermute(forward, "dp", across))


def solution(mesh):
    return jax.shard_map(
        shards,
        mesh=mesh,
        in_specs=(
            P(("groups", "dp"), None, "tensor"),
            P(("groups", "dp"), None, None, "tensor"),
            P(("groups", "dp"), None, "tensor"),
            P(("groups", "dp"), None, None, "tensor"),
            P(("groups", "dp")),
            P(("groups", "dp"), None),
            P(("groups", "dp"), None),
            P("groups"),
        ),
        out_specs=(
            P(("groups", "dp"), None, "tensor"),
            P(("groups", "dp"), None, None, "tensor"),
            P(("groups", "dp"), None, None, "tensor"),
        ),
        check_vma=False,
    )
```

```python
import functools

import jax
import jax.numpy as jnp
from jax import lax
from jax.experimental import pallas as pl
from jax.experimental.pallas import tpu as pltpu
from jax.sharding import PartitionSpec as P

HD = 128

dpo_beta = 0.5


def mask_bias(length, *, group, seq, prefix_rows):
    shape = (seq + prefix_rows, group * seq)
    key_index = lax.broadcasted_iota(jnp.int32, shape, 0)
    tok_index = lax.broadcasted_iota(jnp.int32, shape, 1) % seq
    in_suffix = key_index < seq
    allowed = (in_suffix & (key_index <= tok_index)) | (
        jnp.logical_not(in_suffix) & (key_index - seq < length))
    return jnp.where(allowed, 0.0, -1e30).astype(jnp.float32)


def attend_math(q_blk, og_blk, keys_pre, values_pre, keys_own, values_own, bias, coef, *, group, seq):
    scale = HD ** (-0.5)
    cot_blk = (coef * og_blk.astype(jnp.float32)).astype(jnp.bfloat16)
    q_rows = jnp.concatenate([q_blk[:, g * HD:(g + 1) * HD] for g in range(group)], 0)
    c_rows = jnp.concatenate([cot_blk[:, g * HD:(g + 1) * HD] for g in range(group)], 0)
    keys = jnp.concatenate([keys_own, keys_pre], 0)
    values = jnp.concatenate([values_own, values_pre], 0)

    nt = (((1,), (1,)), ((), ()))
    scores_t = lax.dot_general(keys, q_rows, nt, preferred_element_type=jnp.float32) * scale
    scores_t = scores_t + bias
    col_max = jnp.max(scores_t, 0, keepdims=True)
    raised = jnp.exp(scores_t - col_max)
    prob_t = raised * (1.0 / jnp.sum(raised, 0, keepdims=True))
    prob_low_t = prob_t.astype(jnp.bfloat16)
    output_t = jnp.dot(values.T, prob_low_t, preferred_element_type=jnp.float32)
    row_dot = jnp.sum(c_rows.T.astype(jnp.float32) * output_t, 0, keepdims=True)
    grad_prob_t = lax.dot_general(values, c_rows, nt, preferred_element_type=jnp.float32)
    grad_score_t = (prob_t * (grad_prob_t - row_dot)).astype(jnp.bfloat16)
    grad_q_t = jnp.dot(keys.T, grad_score_t, preferred_element_type=jnp.float32)
    grad_q = (scale * grad_q_t.T).astype(jnp.bfloat16)
    grad_k = scale * jnp.dot(grad_score_t, q_rows, preferred_element_type=jnp.float32)
    grad_v = jnp.dot(prob_low_t, c_rows, preferred_element_type=jnp.float32)
    return grad_q, grad_k, grad_v


def store_grads(grad_q, grad_k, grad_v, member, dq_ref, dkv_ref, dpre_ref, *, group, seq, prefix_rows):
    active = grad_k.shape[0] - seq
    for g in range(group):
        dq_ref[0, :, g * HD:(g + 1) * HD] = grad_q[g * seq:(g + 1) * seq]
    dkv_ref[0, 0] = grad_k[:seq].astype(jnp.bfloat16)
    dkv_ref[0, 1] = grad_v[:seq].astype(jnp.bfloat16)

    @pl.when(member == 0)
    def _():
        dpre_ref[0, 0, :active] = grad_k[seq:]
        dpre_ref[0, 1, :active] = grad_v[seq:]
        if active < prefix_rows:
            zeros = jnp.zeros((prefix_rows - active, HD), jnp.float32)
            dpre_ref[0, 0, active:] = zeros
            dpre_ref[0, 1, active:] = zeros

    @pl.when(member != 0)
    def _():
        dpre_ref[0, 0, :active] += grad_k[seq:]
        dpre_ref[0, 1, :active] += grad_v[seq:]


def attend_kernel(slots_ref, goal_ref, len_ref, coef_ref,
                  q_ref, og_ref, skv_ref, pkv_ref,
                  dq_ref, dkv_ref, dpre_ref, *, group, seq, prefix_rows):
    p = pl.program_id(0)
    member = pl.program_id(2)
    s = slots_ref[2 * p + member]
    length = len_ref[goal_ref[p]]
    bias = mask_bias(length, group=group, seq=seq, prefix_rows=prefix_rows)
    grads = attend_math(q_ref[0], og_ref[0], pkv_ref[0, 0], pkv_ref[0, 1], skv_ref[0, 0], skv_ref[0, 1],
                        bias, coef_ref[s], group=group, seq=seq)
    store_grads(*grads, member, dq_ref, dkv_ref, dpre_ref, group=group, seq=seq, prefix_rows=prefix_rows)


def pair_of(goal, goal_ref, pair_count):
    pair = 0
    for p in range(pair_count):
        pair = jnp.where(goal_ref[p] == goal, p, pair)
    return pair


def slot_kernel(me_ref, goal_ref, slots_ref, len_ref, lr_ref, q_ref, og_ref, skv_ref, pkv_ref, *rest,
                group, seq, prefix_rows, flip, pair_count, chained, seeded, low):
    if chained:
        rest = rest[2:]
    seed_ref = None
    if seeded:
        seed_ref, rest = rest[0], rest[1:]
    dq_ref, dkv_ref, dpre_ref, bias_ref = rest[:4]
    acc_ref = rest[4] if low else dpre_ref
    k = pl.program_id(0)
    member = pl.program_id(1)
    goal = me_ref[0] ^ flip
    pair = pair_of(goal, goal_ref, pair_count)
    length = len_ref[goal]
    dims = dict(group=group, seq=seq, prefix_rows=prefix_rows)

    @pl.when((k == 0) & (member == 0))
    def _():
        bias_ref[...] = mask_bias(length, **dims)

    gap = lr_ref[slots_ref[0, pair]] - lr_ref[slots_ref[1, pair]]
    x = jnp.full((1, 128), -dpo_beta * gap, jnp.float32)
    weight = dpo_beta * (1.0 / (1.0 + jnp.exp(-x)))
    coef = jnp.where(member == 0, -weight, weight)[:, :1]
    blocks = (seq + length + 127) // 128
    for used in range(1, (seq + prefix_rows + 127) // 128 + 1):
        @pl.when(blocks == used)
        def _():
            width = min(used * 128, seq + prefix_rows)
            grads = attend_math(q_ref[0], og_ref[0], pkv_ref[0, 0, :width - seq], pkv_ref[0, 1, :width - seq],
                                skv_ref[0, 0], skv_ref[0, 1], bias_ref[:width], coef,
                                group=group, seq=seq)
            store_grads(*grads, member, dq_ref, dkv_ref, acc_ref, **dims)

    if seeded:
        @pl.when(member == 1)
        def _():
            dpre_ref[...] += seed_ref[...]
    if low:
        @pl.when(member == 1)
        def _():
            dpre_ref[...] = acc_ref[...].astype(dpre_ref.dtype)


def attend_slot(flip, me, goals, slots, lengths, logratio, queries, out_grad, suffix_kv, prefix_one, chain,
                seed=None, low=False):
    suffix_count, seq, qwidth = queries.shape
    kv_width = suffix_kv.shape[-1]
    kv_local = kv_width // HD
    group = qwidth // kv_width
    prefix_rows = prefix_one.shape[2]
    pair_count = goals.shape[0]
    qb = group * HD

    def suffix_of(m, me_ref, goal_ref, slots_ref):
        pair = pair_of(me_ref[0] ^ flip, goal_ref, pair_count)
        return slots_ref[m, pair]

    def q_map(k, m, me_ref, goal_ref, slots_ref, len_ref):
        return (suffix_of(m, me_ref, goal_ref, slots_ref), 0, k)

    def skv_map(k, m, me_ref, goal_ref, slots_ref, len_ref):
        return (suffix_of(m, me_ref, goal_ref, slots_ref), 0, 0, k)

    def pkv_map(k, m, me_ref, goal_ref, slots_ref, len_ref):
        return (0, 0, 0, k)

    out_shape = (
        jax.ShapeDtypeStruct((suffix_count, seq, qwidth), jnp.bfloat16),
        jax.ShapeDtypeStruct((suffix_count, 2, seq, kv_width), jnp.bfloat16),
        jax.ShapeDtypeStruct((1, 2, prefix_rows, kv_width), jnp.bfloat16 if low else jnp.float32),
    )
    in_specs = [
        pl.BlockSpec(memory_space=pltpu.SMEM),
        pl.BlockSpec((1, seq, qb), q_map),
        pl.BlockSpec((1, seq, qb), q_map),
        pl.BlockSpec((1, 2, seq, HD), skv_map),
        pl.BlockSpec((1, 2, prefix_rows, HD), pkv_map),
    ]
    operands = [logratio, queries, out_grad, suffix_kv, prefix_one]
    aliases = {}
    if chain is not None:
        in_specs += [pl.BlockSpec(memory_space=pl.ANY)] * 2
        operands += list(chain)
        aliases = {9: 0, 10: 1}
    if seed is not None:
        in_specs.append(pl.BlockSpec((1, 2, prefix_rows, HD), pkv_map))
        operands.append(seed)
    scratch = [pltpu.VMEM((prefix_rows + seq, group * seq), jnp.float32)]
    if low:
        scratch.append(pltpu.VMEM((1, 2, prefix_rows, HD), jnp.float32))
    kernel = functools.partial(slot_kernel, group=group, seq=seq, prefix_rows=prefix_rows, flip=flip,
                               pair_count=pair_count, chained=chain is not None, seeded=seed is not None,
                               low=low)
    grid_spec = pltpu.PrefetchScalarGridSpec(
        num_scalar_prefetch=4,
        grid=(kv_local, 2),
        in_specs=in_specs,
        out_specs=[
            pl.BlockSpec((1, seq, qb), q_map),
            pl.BlockSpec((1, 2, seq, HD), skv_map),
            pl.BlockSpec((1, 2, prefix_rows, HD), pkv_map),
        ],
        scratch_shapes=scratch,
    )
    steps = 2 * kv_local
    cost = pl.CostEstimate(
        flops=steps * 2_200_000_000,
        transcendentals=steps * group * seq * (prefix_rows + seq),
        bytes_accessed=steps * (4 * seq * qb + 4 * seq * HD + 6 * prefix_rows * HD) * 2,
    )
    return pl.pallas_call(
        kernel,
        grid_spec=grid_spec,
        out_shape=out_shape,
        input_output_aliases=aliases,
        cost_estimate=cost,
        compiler_params=pltpu.CompilerParams(dimension_semantics=("arbitrary", "arbitrary")),
    )(me, goals, slots, lengths, *operands)


def attend_all(slots, goals, lengths, coef, queries, out_grad, suffix_kv, prefix_all):
    suffix_count, seq, qwidth = queries.shape
    kv_width = suffix_kv.shape[-1]
    kv_local = kv_width // HD
    group = qwidth // kv_width
    goal_count, _, prefix_rows, _ = prefix_all.shape
    pair_count = goals.shape[0]
    qb = group * HD

    def q_map(p, k, m, slots_ref, goal_ref, len_ref):
        return (slots_ref[2 * p + m], 0, k)

    def skv_map(p, k, m, slots_ref, goal_ref, len_ref):
        return (slots_ref[2 * p + m], 0, 0, k)

    def pkv_map(p, k, m, slots_ref, goal_ref, len_ref):
        return (goal_ref[p], 0, 0, k)

    kernel = functools.partial(attend_kernel, group=group, seq=seq, prefix_rows=prefix_rows)
    out_shape = (
        jax.ShapeDtypeStruct((suffix_count, seq, qwidth), jnp.bfloat16),
        jax.ShapeDtypeStruct((suffix_count, 2, seq, kv_width), jnp.bfloat16),
        jax.ShapeDtypeStruct((goal_count, 2, prefix_rows, kv_width), jnp.float32),
    )
    in_specs = [
        pl.BlockSpec(memory_space=pltpu.SMEM),
        pl.BlockSpec((1, seq, qb), q_map),
        pl.BlockSpec((1, seq, qb), q_map),
        pl.BlockSpec((1, 2, seq, HD), skv_map),
        pl.BlockSpec((1, 2, prefix_rows, HD), pkv_map),
    ]
    operands = [coef, queries, out_grad, suffix_kv, prefix_all]
    aliases = {}
    if pair_count < goal_count:
        in_specs.append(pl.BlockSpec(memory_space=pl.ANY))
        operands.append(jnp.zeros(out_shape[2].shape, jnp.float32))
        aliases = {3 + len(operands) - 1: 2}

        def kernel_with_zero(*refs):
            return kernel(*refs[:8], *refs[9:])
        body = kernel_with_zero
    else:
        body = kernel
    grid_spec = pltpu.PrefetchScalarGridSpec(
        num_scalar_prefetch=3,
        grid=(pair_count, kv_local, 2),
        in_specs=in_specs,
        out_specs=[
            pl.BlockSpec((1, seq, qb), q_map),
            pl.BlockSpec((1, 2, seq, HD), skv_map),
            pl.BlockSpec((1, 2, prefix_rows, HD), pkv_map),
        ],
    )
    return pl.pallas_call(
        body,
        grid_spec=grid_spec,
        out_shape=out_shape,
        input_output_aliases=aliases,
        compiler_params=pltpu.CompilerParams(
            dimension_semantics=("arbitrary", "arbitrary", "arbitrary")),
    )(slots, goals, lengths, *operands)


def shards(queries, suffix_kv, out_grad, prefix_kv, logratio, pair_slots, pair_goal, prefix_len):
    dp_size = lax.axis_size("dp")
    pair_count = pair_slots.shape[0]
    if dp_size == 4 and pair_count == dp_size:
        return pipelined(queries, suffix_kv, out_grad, prefix_kv, logratio,
                         pair_slots, pair_goal, prefix_len)
    suffix_count = queries.shape[0]
    chosen = pair_slots[:, 0]
    rejected = pair_slots[:, 1]
    positions = jnp.arange(suffix_count)
    pick_chosen = chosen[:, None] == positions[None, :]
    pick_rejected = rejected[:, None] == positions[None, :]
    ratio_chosen = jnp.sum(jnp.where(pick_chosen, logratio[None, :], 0.0), 1)
    ratio_rejected = jnp.sum(jnp.where(pick_rejected, logratio[None, :], 0.0), 1)
    weight = dpo_beta * jax.nn.sigmoid(-dpo_beta * (ratio_chosen - ratio_rejected))
    coefficient = jnp.sum(
        jnp.where(pick_rejected, weight[:, None], 0.0)
        - jnp.where(pick_chosen, weight[:, None], 0.0),
        0,
    )
    slots = pair_slots.reshape(-1).astype(jnp.int32)
    goals = pair_goal[:, 0].astype(jnp.int32)
    prefix_all = lax.all_gather(prefix_kv, "dp", axis=0, tiled=True)
    grad_q, grad_kv, partial = attend_all(
        slots, goals, prefix_len.astype(jnp.int32), coefficient,
        queries, out_grad, suffix_kv, prefix_all)
    prefix_grad = lax.psum_scatter(partial, "dp", scatter_dimension=0, tiled=True)
    return grad_q, grad_kv, prefix_grad.astype(jnp.bfloat16)


def pipelined(queries, suffix_kv, out_grad, prefix_kv, logratio, pair_slots, pair_goal, prefix_len):
    partner = [(i, i ^ 1) for i in range(4)]
    across = [(i, i ^ 2) for i in range(4)]
    pre_across = lax.ppermute(prefix_kv, "dp", across)
    pre_partner = lax.ppermute(prefix_kv, "dp", partner)
    me = lax.axis_index("dp").astype(jnp.int32).reshape(1)
    tables = (me, pair_goal.reshape(-1).astype(jnp.int32), pair_slots.T.astype(jnp.int32),
              prefix_len.astype(jnp.int32), logratio)

    def run(flip, prefix_one, chain, **extra):
        grad_q, grad_kv, partial = attend_slot(flip, *tables, queries, out_grad, suffix_kv, prefix_one, chain,
                                               **extra)
        return (grad_q, grad_kv), partial

    chain, near = run(1, pre_partner, None)
    pre_across, near = lax.optimization_barrier((pre_across, near))
    pre_relay = lax.ppermute(pre_across, "dp", partner)
    near_sent = lax.ppermute(near, "dp", partner)
    chain, cross = run(2, pre_across, chain)
    chain, relay = run(3, pre_relay, chain, low=True)
    forward = (cross + lax.ppermute(relay, "dp", partner).astype(jnp.float32)).astype(jnp.bfloat16)
    forward, own_prefix = lax.optimization_barrier((forward, prefix_kv))
    chain, own = run(0, own_prefix, chain, seed=near_sent)
    total = own + lax.ppermute(forward, "dp", across).astype(jnp.float32)
    return chain[0], chain[1], total.astype(jnp.bfloat16)


def solution(mesh):
    return jax.shard_map(
        shards,
        mesh=mesh,
        in_specs=(
            P(("groups", "dp"), None, "tensor"),
            P(("groups", "dp"), None, None, "tensor"),
            P(("groups", "dp"), None, "tensor"),
            P(("groups", "dp"), None, None, "tensor"),
            P(("groups", "dp")),
            P(("groups", "dp"), None),
            P(("groups", "dp"), None),
            P("groups"),
        ),
        out_specs=(
            P(("groups", "dp"), None, "tensor"),
            P(("groups", "dp"), None, None, "tensor"),
            P(("groups", "dp"), None, None, "tensor"),
        ),
        check_vma=False,
    )
```

```python
import functools

import jax
import jax.numpy as jnp
from jax import lax
from jax.experimental import pallas as pl
from jax.experimental.pallas import tpu as pltpu
from jax.sharding import PartitionSpec as P

HD = 128
LOG2E = 1.4426950408889634

dpo_beta = 0.5


def mask_bias(length, *, group, seq, prefix_rows):
    shape = (seq + prefix_rows, group * seq)
    key_index = lax.broadcasted_iota(jnp.int32, shape, 0)
    tok_index = lax.broadcasted_iota(jnp.int32, shape, 1) % seq
    in_suffix = key_index < seq
    allowed = (in_suffix & (key_index <= tok_index)) | (
        jnp.logical_not(in_suffix) & (key_index - seq < length))
    return jnp.where(allowed, 0.0, -1e30).astype(jnp.float32)


def attend_math(q_blk, og_blk, keys_pre, values_pre, keys_own, values_own, bias, coef, *, group, seq):
    scale = HD ** (-0.5)
    cot_blk = (coef * og_blk.astype(jnp.float32)).astype(jnp.bfloat16)
    q_rows = jnp.concatenate([q_blk[:, g * HD:(g + 1) * HD] for g in range(group)], 0)
    c_rows = jnp.concatenate([cot_blk[:, g * HD:(g + 1) * HD] for g in range(group)], 0)
    keys = jnp.concatenate([keys_own, keys_pre], 0)
    values = jnp.concatenate([values_own, values_pre], 0)

    nt = (((1,), (1,)), ((), ()))
    scores_t = lax.dot_general(keys, q_rows, nt, preferred_element_type=jnp.float32) * (scale * LOG2E)
    scores_t = scores_t + bias
    col_max = jnp.max(scores_t, 0, keepdims=True)
    raised = jnp.exp2(scores_t - col_max)
    inv_sum = 1.0 / jnp.sum(raised, 0, keepdims=True)
    prob_low_t = (raised * inv_sum).astype(jnp.bfloat16)
    output_t = jnp.dot(values.T, prob_low_t, preferred_element_type=jnp.float32)
    row_dot = jnp.sum(c_rows.T.astype(jnp.float32) * output_t, 0, keepdims=True)
    grad_prob_t = lax.dot_general(values, c_rows, nt, preferred_element_type=jnp.float32)
    grad_score_t = (raised * ((grad_prob_t - row_dot) * inv_sum)).astype(jnp.bfloat16)
    grad_q_t = jnp.dot(keys.T, grad_score_t, preferred_element_type=jnp.float32)
    grad_q = (scale * grad_q_t.T).astype(jnp.bfloat16)
    grad_k = scale * jnp.dot(grad_score_t, q_rows, preferred_element_type=jnp.float32)
    grad_v = jnp.dot(prob_low_t, c_rows, preferred_element_type=jnp.float32)
    return grad_q, grad_k, grad_v


def store_grads(grad_q, grad_k, grad_v, member, dq_ref, dkv_ref, dpre_ref, *, group, seq, prefix_rows):
    active = grad_k.shape[0] - seq
    for g in range(group):
        dq_ref[0, :, g * HD:(g + 1) * HD] = grad_q[g * seq:(g + 1) * seq]
    dkv_ref[0, 0] = grad_k[:seq].astype(jnp.bfloat16)
    dkv_ref[0, 1] = grad_v[:seq].astype(jnp.bfloat16)

    @pl.when(member == 0)
    def _():
        dpre_ref[0, 0, :active] = grad_k[seq:]
        dpre_ref[0, 1, :active] = grad_v[seq:]
        if active < prefix_rows:
            zeros = jnp.zeros((prefix_rows - active, HD), jnp.float32)
            dpre_ref[0, 0, active:] = zeros
            dpre_ref[0, 1, active:] = zeros

    @pl.when(member != 0)
    def _():
        dpre_ref[0, 0, :active] += grad_k[seq:]
        dpre_ref[0, 1, :active] += grad_v[seq:]


def attend_kernel(slots_ref, goal_ref, len_ref, coef_ref,
                  q_ref, og_ref, skv_ref, pkv_ref,
                  dq_ref, dkv_ref, dpre_ref, *, group, seq, prefix_rows):
    p = pl.program_id(0)
    member = pl.program_id(2)
    s = slots_ref[2 * p + member]
    length = len_ref[goal_ref[p]]
    bias = mask_bias(length, group=group, seq=seq, prefix_rows=prefix_rows)
    grads = attend_math(q_ref[0], og_ref[0], pkv_ref[0, 0], pkv_ref[0, 1], skv_ref[0, 0], skv_ref[0, 1],
                        bias, coef_ref[s], group=group, seq=seq)
    store_grads(*grads, member, dq_ref, dkv_ref, dpre_ref, group=group, seq=seq, prefix_rows=prefix_rows)


def pair_of(goal, goal_ref, pair_count):
    pair = 0
    for p in range(pair_count):
        pair = jnp.where(goal_ref[p] == goal, p, pair)
    return pair


def slot_kernel(me_ref, goal_ref, slots_ref, len_ref, lr_ref, q_ref, og_ref, skv_ref, pkv_ref, *rest,
                group, seq, prefix_rows, flip, pair_count, chained, seeded, low):
    if chained:
        rest = rest[2:]
    seed_ref = None
    if seeded:
        seed_ref, rest = rest[0], rest[1:]
    dq_ref, dkv_ref, dpre_ref, bias_ref = rest[:4]
    acc_ref = rest[4] if low else dpre_ref
    k = pl.program_id(0)
    member = pl.program_id(1)
    goal = me_ref[0] ^ flip
    pair = pair_of(goal, goal_ref, pair_count)
    length = len_ref[goal]
    dims = dict(group=group, seq=seq, prefix_rows=prefix_rows)

    @pl.when((k == 0) & (member == 0))
    def _():
        bias_ref[...] = mask_bias(length, **dims)

    gap = lr_ref[slots_ref[0, pair]] - lr_ref[slots_ref[1, pair]]
    x = jnp.full((1, 128), -dpo_beta * gap, jnp.float32)
    weight = dpo_beta * (1.0 / (1.0 + jnp.exp(-x)))
    coef = jnp.where(member == 0, -weight, weight)[:, :1]
    blocks = (seq + length + 127) // 128
    for used in range(1, (seq + prefix_rows + 127) // 128 + 1):
        @pl.when(blocks == used)
        def _():
            width = min(used * 128, seq + prefix_rows)
            grads = attend_math(q_ref[0], og_ref[0], pkv_ref[0, 0, :width - seq], pkv_ref[0, 1, :width - seq],
                                skv_ref[0, 0], skv_ref[0, 1], bias_ref[:width], coef,
                                group=group, seq=seq)
            store_grads(*grads, member, dq_ref, dkv_ref, acc_ref, **dims)

    if seeded:
        @pl.when(member == 1)
        def _():
            dpre_ref[...] += seed_ref[...]
    if low:
        @pl.when(member == 1)
        def _():
            dpre_ref[...] = acc_ref[...].astype(dpre_ref.dtype)


def attend_slot(flip, me, goals, slots, lengths, logratio, queries, out_grad, suffix_kv, prefix_one, chain,
                seed=None, low=False):
    suffix_count, seq, qwidth = queries.shape
    kv_width = suffix_kv.shape[-1]
    kv_local = kv_width // HD
    group = qwidth // kv_width
    prefix_rows = prefix_one.shape[2]
    pair_count = goals.shape[0]
    qb = group * HD

    def suffix_of(m, me_ref, goal_ref, slots_ref):
        pair = pair_of(me_ref[0] ^ flip, goal_ref, pair_count)
        return slots_ref[m, pair]

    def q_map(k, m, me_ref, goal_ref, slots_ref, len_ref):
        return (suffix_of(m, me_ref, goal_ref, slots_ref), 0, k)

    def skv_map(k, m, me_ref, goal_ref, slots_ref, len_ref):
        return (suffix_of(m, me_ref, goal_ref, slots_ref), 0, 0, k)

    def pkv_map(k, m, me_ref, goal_ref, slots_ref, len_ref):
        return (0, 0, 0, k)

    out_shape = (
        jax.ShapeDtypeStruct((suffix_count, seq, qwidth), jnp.bfloat16),
        jax.ShapeDtypeStruct((suffix_count, 2, seq, kv_width), jnp.bfloat16),
        jax.ShapeDtypeStruct((1, 2, prefix_rows, kv_width), jnp.bfloat16 if low else jnp.float32),
    )
    in_specs = [
        pl.BlockSpec(memory_space=pltpu.SMEM),
        pl.BlockSpec((1, seq, qb), q_map),
        pl.BlockSpec((1, seq, qb), q_map),
        pl.BlockSpec((1, 2, seq, HD), skv_map),
        pl.BlockSpec((1, 2, prefix_rows, HD), pkv_map),
    ]
    operands = [logratio, queries, out_grad, suffix_kv, prefix_one]
    aliases = {}
    if chain is not None:
        in_specs += [pl.BlockSpec(memory_space=pl.ANY)] * 2
        operands += list(chain)
        aliases = {9: 0, 10: 1}
    if seed is not None:
        in_specs.append(pl.BlockSpec((1, 2, prefix_rows, HD), pkv_map))
        operands.append(seed)
    scratch = [pltpu.VMEM((prefix_rows + seq, group * seq), jnp.float32)]
    if low:
        scratch.append(pltpu.VMEM((1, 2, prefix_rows, HD), jnp.float32))
    kernel = functools.partial(slot_kernel, group=group, seq=seq, prefix_rows=prefix_rows, flip=flip,
                               pair_count=pair_count, chained=chain is not None, seeded=seed is not None,
                               low=low)
    grid_spec = pltpu.PrefetchScalarGridSpec(
        num_scalar_prefetch=4,
        grid=(kv_local, 2),
        in_specs=in_specs,
        out_specs=[
            pl.BlockSpec((1, seq, qb), q_map),
            pl.BlockSpec((1, 2, seq, HD), skv_map),
            pl.BlockSpec((1, 2, prefix_rows, HD), pkv_map),
        ],
        scratch_shapes=scratch,
    )
    steps = 2 * kv_local
    cost = pl.CostEstimate(
        flops=steps * 2_200_000_000,
        transcendentals=steps * group * seq * (prefix_rows + seq),
        bytes_accessed=steps * (4 * seq * qb + 4 * seq * HD + 6 * prefix_rows * HD) * 2,
    )
    return pl.pallas_call(
        kernel,
        grid_spec=grid_spec,
        out_shape=out_shape,
        input_output_aliases=aliases,
        cost_estimate=cost,
        compiler_params=pltpu.CompilerParams(dimension_semantics=("arbitrary", "arbitrary")),
    )(me, goals, slots, lengths, *operands)


def attend_all(slots, goals, lengths, coef, queries, out_grad, suffix_kv, prefix_all):
    suffix_count, seq, qwidth = queries.shape
    kv_width = suffix_kv.shape[-1]
    kv_local = kv_width // HD
    group = qwidth // kv_width
    goal_count, _, prefix_rows, _ = prefix_all.shape
    pair_count = goals.shape[0]
    qb = group * HD

    def q_map(p, k, m, slots_ref, goal_ref, len_ref):
        return (slots_ref[2 * p + m], 0, k)

    def skv_map(p, k, m, slots_ref, goal_ref, len_ref):
        return (slots_ref[2 * p + m], 0, 0, k)

    def pkv_map(p, k, m, slots_ref, goal_ref, len_ref):
        return (goal_ref[p], 0, 0, k)

    kernel = functools.partial(attend_kernel, group=group, seq=seq, prefix_rows=prefix_rows)
    out_shape = (
        jax.ShapeDtypeStruct((suffix_count, seq, qwidth), jnp.bfloat16),
        jax.ShapeDtypeStruct((suffix_count, 2, seq, kv_width), jnp.bfloat16),
        jax.ShapeDtypeStruct((goal_count, 2, prefix_rows, kv_width), jnp.float32),
    )
    in_specs = [
        pl.BlockSpec(memory_space=pltpu.SMEM),
        pl.BlockSpec((1, seq, qb), q_map),
        pl.BlockSpec((1, seq, qb), q_map),
        pl.BlockSpec((1, 2, seq, HD), skv_map),
        pl.BlockSpec((1, 2, prefix_rows, HD), pkv_map),
    ]
    operands = [coef, queries, out_grad, suffix_kv, prefix_all]
    aliases = {}
    if pair_count < goal_count:
        in_specs.append(pl.BlockSpec(memory_space=pl.ANY))
        operands.append(jnp.zeros(out_shape[2].shape, jnp.float32))
        aliases = {3 + len(operands) - 1: 2}

        def kernel_with_zero(*refs):
            return kernel(*refs[:8], *refs[9:])
        body = kernel_with_zero
    else:
        body = kernel
    grid_spec = pltpu.PrefetchScalarGridSpec(
        num_scalar_prefetch=3,
        grid=(pair_count, kv_local, 2),
        in_specs=in_specs,
        out_specs=[
            pl.BlockSpec((1, seq, qb), q_map),
            pl.BlockSpec((1, 2, seq, HD), skv_map),
            pl.BlockSpec((1, 2, prefix_rows, HD), pkv_map),
        ],
    )
    return pl.pallas_call(
        body,
        grid_spec=grid_spec,
        out_shape=out_shape,
        input_output_aliases=aliases,
        compiler_params=pltpu.CompilerParams(
            dimension_semantics=("arbitrary", "arbitrary", "arbitrary")),
    )(slots, goals, lengths, *operands)


def shards(queries, suffix_kv, out_grad, prefix_kv, logratio, pair_slots, pair_goal, prefix_len):
    dp_size = lax.axis_size("dp")
    pair_count = pair_slots.shape[0]
    if dp_size == 4 and pair_count == dp_size:
        return pipelined(queries, suffix_kv, out_grad, prefix_kv, logratio,
                         pair_slots, pair_goal, prefix_len)
    suffix_count = queries.shape[0]
    chosen = pair_slots[:, 0]
    rejected = pair_slots[:, 1]
    positions = jnp.arange(suffix_count)
    pick_chosen = chosen[:, None] == positions[None, :]
    pick_rejected = rejected[:, None] == positions[None, :]
    ratio_chosen = jnp.sum(jnp.where(pick_chosen, logratio[None, :], 0.0), 1)
    ratio_rejected = jnp.sum(jnp.where(pick_rejected, logratio[None, :], 0.0), 1)
    weight = dpo_beta * jax.nn.sigmoid(-dpo_beta * (ratio_chosen - ratio_rejected))
    coefficient = jnp.sum(
        jnp.where(pick_rejected, weight[:, None], 0.0)
        - jnp.where(pick_chosen, weight[:, None], 0.0),
        0,
    )
    slots = pair_slots.reshape(-1).astype(jnp.int32)
    goals = pair_goal[:, 0].astype(jnp.int32)
    prefix_all = lax.all_gather(prefix_kv, "dp", axis=0, tiled=True)
    grad_q, grad_kv, partial = attend_all(
        slots, goals, prefix_len.astype(jnp.int32), coefficient,
        queries, out_grad, suffix_kv, prefix_all)
    prefix_grad = lax.psum_scatter(partial, "dp", scatter_dimension=0, tiled=True)
    return grad_q, grad_kv, prefix_grad.astype(jnp.bfloat16)


def pipelined(queries, suffix_kv, out_grad, prefix_kv, logratio, pair_slots, pair_goal, prefix_len):
    partner = [(i, i ^ 1) for i in range(4)]
    across = [(i, i ^ 2) for i in range(4)]
    pre_across = lax.ppermute(prefix_kv, "dp", across)
    pre_partner = lax.ppermute(prefix_kv, "dp", partner)
    me = lax.axis_index("dp").astype(jnp.int32).reshape(1)
    tables = (me, pair_goal.reshape(-1).astype(jnp.int32), pair_slots.T.astype(jnp.int32),
              prefix_len.astype(jnp.int32), logratio)

    def run(flip, prefix_one, chain, **extra):
        grad_q, grad_kv, partial = attend_slot(flip, *tables, queries, out_grad, suffix_kv, prefix_one, chain,
                                               **extra)
        return (grad_q, grad_kv), partial

    chain, near = run(1, pre_partner, None)
    pre_across, near = lax.optimization_barrier((pre_across, near))
    pre_relay = lax.ppermute(pre_across, "dp", partner)
    near_sent = lax.ppermute(near, "dp", partner)
    chain, cross = run(2, pre_across, chain)
    chain, relay = run(3, pre_relay, chain, low=True)
    forward = (cross + lax.ppermute(relay, "dp", partner).astype(jnp.float32)).astype(jnp.bfloat16)
    forward, own_prefix = lax.optimization_barrier((forward, prefix_kv))
    chain, own = run(0, own_prefix, chain, seed=near_sent)
    total = own + lax.ppermute(forward, "dp", across).astype(jnp.float32)
    return chain[0], chain[1], total.astype(jnp.bfloat16)


def solution(mesh):
    return jax.shard_map(
        shards,
        mesh=mesh,
        in_specs=(
            P(("groups", "dp"), None, "tensor"),
            P(("groups", "dp"), None, None, "tensor"),
            P(("groups", "dp"), None, "tensor"),
            P(("groups", "dp"), None, None, "tensor"),
            P(("groups", "dp")),
            P(("groups", "dp"), None),
            P(("groups", "dp"), None),
            P("groups"),
        ),
        out_specs=(
            P(("groups", "dp"), None, "tensor"),
            P(("groups", "dp"), None, None, "tensor"),
            P(("groups", "dp"), None, None, "tensor"),
        ),
        check_vma=False,
    )
```

```python
import functools

import jax
import jax.numpy as jnp
from jax import lax
from jax.experimental import pallas as pl
from jax.experimental.pallas import tpu as pltpu
from jax.sharding import PartitionSpec as P

HD = 128
LOG2E = 1.4426950408889634

dpo_beta = 0.5


def mask_bias(length, *, group, seq, prefix_rows):
    shape = (seq + prefix_rows, group * seq)
    key_index = lax.broadcasted_iota(jnp.int32, shape, 0)
    tok_index = lax.broadcasted_iota(jnp.int32, shape, 1) % seq
    in_suffix = key_index < seq
    allowed = (in_suffix & (key_index <= tok_index)) | (
        jnp.logical_not(in_suffix) & (key_index - seq < length))
    return jnp.where(allowed, 0.0, -1e30).astype(jnp.float32)


def attend_math(q_blk, og_blk, keys_pre, values_pre, keys_own, values_own, bias, coef, *, group, seq):
    scale = HD ** (-0.5)
    cot_blk = (coef * og_blk.astype(jnp.float32)).astype(jnp.bfloat16)
    q_rows = jnp.concatenate([q_blk[:, g * HD:(g + 1) * HD] for g in range(group)], 0)
    c_rows = jnp.concatenate([cot_blk[:, g * HD:(g + 1) * HD] for g in range(group)], 0)
    keys = jnp.concatenate([keys_own, keys_pre], 0)
    values = jnp.concatenate([values_own, values_pre], 0)

    nt = (((1,), (1,)), ((), ()))
    scores_t = lax.dot_general(keys, q_rows, nt, preferred_element_type=jnp.float32) * (scale * LOG2E)
    scores_t = scores_t + bias
    col_max = jnp.max(scores_t, 0, keepdims=True)
    raised = jnp.exp2(scores_t - col_max)
    inv_sum = 1.0 / jnp.sum(raised, 0, keepdims=True)
    prob_low_t = (raised * inv_sum).astype(jnp.bfloat16)
    output_t = jnp.dot(values.T, prob_low_t, preferred_element_type=jnp.float32)
    row_dot = jnp.sum(c_rows.T.astype(jnp.float32) * output_t, 0, keepdims=True)
    grad_prob_t = lax.dot_general(values, c_rows, nt, preferred_element_type=jnp.float32)
    grad_score_t = (raised * ((grad_prob_t - row_dot) * inv_sum)).astype(jnp.bfloat16)
    grad_q_t = jnp.dot(keys.T, grad_score_t, preferred_element_type=jnp.float32)
    grad_q = (scale * grad_q_t.T).astype(jnp.bfloat16)
    grad_k = scale * jnp.dot(grad_score_t, q_rows, preferred_element_type=jnp.float32)
    grad_v = jnp.dot(prob_low_t, c_rows, preferred_element_type=jnp.float32)
    return grad_q, grad_k, grad_v


def store_grads(grad_q, grad_k, grad_v, member, dq_ref, dkv_ref, dpre_ref, *, group, seq, prefix_rows, head=0):
    active = grad_k.shape[0] - seq
    kv_cols = pl.ds(pl.multiple_of(head * HD, HD), HD)
    for g in range(group):
        q_cols = pl.ds(pl.multiple_of((head * group + g) * HD, HD), HD)
        dq_ref[0, :, q_cols] = grad_q[g * seq:(g + 1) * seq]
    dkv_ref[0, 0, :, kv_cols] = grad_k[:seq].astype(jnp.bfloat16)
    dkv_ref[0, 1, :, kv_cols] = grad_v[:seq].astype(jnp.bfloat16)

    @pl.when(member == 0)
    def _():
        dpre_ref[0, 0, :active, kv_cols] = grad_k[seq:]
        dpre_ref[0, 1, :active, kv_cols] = grad_v[seq:]
        if active < prefix_rows:
            zeros = jnp.zeros((prefix_rows - active, HD), jnp.float32)
            dpre_ref[0, 0, active:, kv_cols] = zeros
            dpre_ref[0, 1, active:, kv_cols] = zeros

    @pl.when(member != 0)
    def _():
        dpre_ref[0, 0, :active, kv_cols] += grad_k[seq:]
        dpre_ref[0, 1, :active, kv_cols] += grad_v[seq:]


def attend_kernel(slots_ref, goal_ref, len_ref, coef_ref,
                  q_ref, og_ref, skv_ref, pkv_ref,
                  dq_ref, dkv_ref, dpre_ref, *, group, seq, prefix_rows):
    p = pl.program_id(0)
    member = pl.program_id(2)
    s = slots_ref[2 * p + member]
    length = len_ref[goal_ref[p]]
    bias = mask_bias(length, group=group, seq=seq, prefix_rows=prefix_rows)
    grads = attend_math(q_ref[0], og_ref[0], pkv_ref[0, 0], pkv_ref[0, 1], skv_ref[0, 0], skv_ref[0, 1],
                        bias, coef_ref[s], group=group, seq=seq)
    store_grads(*grads, member, dq_ref, dkv_ref, dpre_ref, group=group, seq=seq, prefix_rows=prefix_rows)


def pair_of(goal, goal_ref, pair_count):
    pair = 0
    for p in range(pair_count):
        pair = jnp.where(goal_ref[p] == goal, p, pair)
    return pair


def slot_kernel(me_ref, goal_ref, slots_ref, len_ref, lr_ref, q_ref, og_ref, skv_ref, pkv_ref, *rest,
                group, seq, prefix_rows, flip, pair_count, chained, seeded, low):
    if chained:
        rest = rest[2:]
    seed_ref = None
    if seeded:
        seed_ref, rest = rest[0], rest[1:]
    dq_ref, dkv_ref, dpre_ref, bias_ref = rest[:4]
    acc_ref = rest[4] if low else dpre_ref
    member = pl.program_id(0)
    goal = me_ref[0] ^ flip
    pair = pair_of(goal, goal_ref, pair_count)
    length = len_ref[goal]
    dims = dict(group=group, seq=seq, prefix_rows=prefix_rows)
    heads = skv_ref.shape[-1] // HD
    qb = group * HD

    @pl.when(member == 0)
    def _():
        bias_ref[...] = mask_bias(length, **dims)

    gap = lr_ref[slots_ref[0, pair]] - lr_ref[slots_ref[1, pair]]
    x = jnp.full((1, 128), -dpo_beta * gap, jnp.float32)
    weight = dpo_beta * (1.0 / (1.0 + jnp.exp(-x)))
    coef = jnp.where(member == 0, -weight, weight)[:, :1]
    blocks = (seq + length + 127) // 128

    def one_head(h, carry):
        q_cols = pl.ds(pl.multiple_of(h * qb, qb), qb)
        kv_cols = pl.ds(pl.multiple_of(h * HD, HD), HD)
        for used in range(1, (seq + prefix_rows + 127) // 128 + 1):
            @pl.when(blocks == used)
            def _():
                width = min(used * 128, seq + prefix_rows)
                grads = attend_math(q_ref[0, :, q_cols], og_ref[0, :, q_cols],
                                    pkv_ref[0, 0, :width - seq, kv_cols], pkv_ref[0, 1, :width - seq, kv_cols],
                                    skv_ref[0, 0, :, kv_cols], skv_ref[0, 1, :, kv_cols], bias_ref[:width], coef,
                                    group=group, seq=seq)
                store_grads(*grads, member, dq_ref, dkv_ref, acc_ref, head=h, **dims)
        return carry

    lax.fori_loop(0, heads, one_head, 0)

    if seeded:
        @pl.when(member == 1)
        def _():
            dpre_ref[...] += seed_ref[...]
    if low:
        @pl.when(member == 1)
        def _():
            dpre_ref[...] = acc_ref[...].astype(dpre_ref.dtype)


def attend_slot(flip, me, goals, slots, lengths, logratio, queries, out_grad, suffix_kv, prefix_one, chain,
                seed=None, low=False):
    suffix_count, seq, qwidth = queries.shape
    kv_width = suffix_kv.shape[-1]
    kv_local = kv_width // HD
    group = qwidth // kv_width
    prefix_rows = prefix_one.shape[2]
    pair_count = goals.shape[0]
    qb = group * HD

    def suffix_of(m, me_ref, goal_ref, slots_ref):
        pair = pair_of(me_ref[0] ^ flip, goal_ref, pair_count)
        return slots_ref[m, pair]

    def q_map(m, me_ref, goal_ref, slots_ref, len_ref):
        return (suffix_of(m, me_ref, goal_ref, slots_ref), 0, 0)

    def skv_map(m, me_ref, goal_ref, slots_ref, len_ref):
        return (suffix_of(m, me_ref, goal_ref, slots_ref), 0, 0, 0)

    def pkv_map(m, me_ref, goal_ref, slots_ref, len_ref):
        return (0, 0, 0, 0)

    out_shape = (
        jax.ShapeDtypeStruct((suffix_count, seq, qwidth), jnp.bfloat16),
        jax.ShapeDtypeStruct((suffix_count, 2, seq, kv_width), jnp.bfloat16),
        jax.ShapeDtypeStruct((1, 2, prefix_rows, kv_width), jnp.bfloat16 if low else jnp.float32),
    )
    in_specs = [
        pl.BlockSpec(memory_space=pltpu.SMEM),
        pl.BlockSpec((1, seq, qwidth), q_map),
        pl.BlockSpec((1, seq, qwidth), q_map),
        pl.BlockSpec((1, 2, seq, kv_width), skv_map),
        pl.BlockSpec((1, 2, prefix_rows, kv_width), pkv_map),
    ]
    operands = [logratio, queries, out_grad, suffix_kv, prefix_one]
    aliases = {}
    if chain is not None:
        in_specs += [pl.BlockSpec(memory_space=pl.ANY)] * 2
        operands += list(chain)
        aliases = {9: 0, 10: 1}
    if seed is not None:
        in_specs.append(pl.BlockSpec((1, 2, prefix_rows, kv_width), pkv_map))
        operands.append(seed)
    scratch = [pltpu.VMEM((prefix_rows + seq, group * seq), jnp.float32)]
    if low:
        scratch.append(pltpu.VMEM((1, 2, prefix_rows, kv_width), jnp.float32))
    kernel = functools.partial(slot_kernel, group=group, seq=seq, prefix_rows=prefix_rows, flip=flip,
                               pair_count=pair_count, chained=chain is not None, seeded=seed is not None,
                               low=low)
    grid_spec = pltpu.PrefetchScalarGridSpec(
        num_scalar_prefetch=4,
        grid=(2,),
        in_specs=in_specs,
        out_specs=[
            pl.BlockSpec((1, seq, qwidth), q_map),
            pl.BlockSpec((1, 2, seq, kv_width), skv_map),
            pl.BlockSpec((1, 2, prefix_rows, kv_width), pkv_map),
        ],
        scratch_shapes=scratch,
    )
    steps = 2 * kv_local
    cost = pl.CostEstimate(
        flops=steps * 2_200_000_000,
        transcendentals=steps * group * seq * (prefix_rows + seq),
        bytes_accessed=steps * (4 * seq * qb + 4 * seq * HD + 6 * prefix_rows * HD) * 2,
    )
    return pl.pallas_call(
        kernel,
        grid_spec=grid_spec,
        out_shape=out_shape,
        input_output_aliases=aliases,
        cost_estimate=cost,
        compiler_params=pltpu.CompilerParams(dimension_semantics=("arbitrary",)),
    )(me, goals, slots, lengths, *operands)


def attend_all(slots, goals, lengths, coef, queries, out_grad, suffix_kv, prefix_all):
    suffix_count, seq, qwidth = queries.shape
    kv_width = suffix_kv.shape[-1]
    kv_local = kv_width // HD
    group = qwidth // kv_width
    goal_count, _, prefix_rows, _ = prefix_all.shape
    pair_count = goals.shape[0]
    qb = group * HD

    def q_map(p, k, m, slots_ref, goal_ref, len_ref):
        return (slots_ref[2 * p + m], 0, k)

    def skv_map(p, k, m, slots_ref, goal_ref, len_ref):
        return (slots_ref[2 * p + m], 0, 0, k)

    def pkv_map(p, k, m, slots_ref, goal_ref, len_ref):
        return (goal_ref[p], 0, 0, k)

    kernel = functools.partial(attend_kernel, group=group, seq=seq, prefix_rows=prefix_rows)
    out_shape = (
        jax.ShapeDtypeStruct((suffix_count, seq, qwidth), jnp.bfloat16),
        jax.ShapeDtypeStruct((suffix_count, 2, seq, kv_width), jnp.bfloat16),
        jax.ShapeDtypeStruct((goal_count, 2, prefix_rows, kv_width), jnp.float32),
    )
    in_specs = [
        pl.BlockSpec(memory_space=pltpu.SMEM),
        pl.BlockSpec((1, seq, qb), q_map),
        pl.BlockSpec((1, seq, qb), q_map),
        pl.BlockSpec((1, 2, seq, HD), skv_map),
        pl.BlockSpec((1, 2, prefix_rows, HD), pkv_map),
    ]
    operands = [coef, queries, out_grad, suffix_kv, prefix_all]
    aliases = {}
    if pair_count < goal_count:
        in_specs.append(pl.BlockSpec(memory_space=pl.ANY))
        operands.append(jnp.zeros(out_shape[2].shape, jnp.float32))
        aliases = {3 + len(operands) - 1: 2}

        def kernel_with_zero(*refs):
            return kernel(*refs[:8], *refs[9:])
        body = kernel_with_zero
    else:
        body = kernel
    grid_spec = pltpu.PrefetchScalarGridSpec(
        num_scalar_prefetch=3,
        grid=(pair_count, kv_local, 2),
        in_specs=in_specs,
        out_specs=[
            pl.BlockSpec((1, seq, qb), q_map),
            pl.BlockSpec((1, 2, seq, HD), skv_map),
            pl.BlockSpec((1, 2, prefix_rows, HD), pkv_map),
        ],
    )
    return pl.pallas_call(
        body,
        grid_spec=grid_spec,
        out_shape=out_shape,
        input_output_aliases=aliases,
        compiler_params=pltpu.CompilerParams(
            dimension_semantics=("arbitrary", "arbitrary", "arbitrary")),
    )(slots, goals, lengths, *operands)


def shards(queries, suffix_kv, out_grad, prefix_kv, logratio, pair_slots, pair_goal, prefix_len):
    dp_size = lax.axis_size("dp")
    pair_count = pair_slots.shape[0]
    if dp_size == 4 and pair_count == dp_size:
        return pipelined(queries, suffix_kv, out_grad, prefix_kv, logratio,
                         pair_slots, pair_goal, prefix_len)
    suffix_count = queries.shape[0]
    chosen = pair_slots[:, 0]
    rejected = pair_slots[:, 1]
    positions = jnp.arange(suffix_count)
    pick_chosen = chosen[:, None] == positions[None, :]
    pick_rejected = rejected[:, None] == positions[None, :]
    ratio_chosen = jnp.sum(jnp.where(pick_chosen, logratio[None, :], 0.0), 1)
    ratio_rejected = jnp.sum(jnp.where(pick_rejected, logratio[None, :], 0.0), 1)
    weight = dpo_beta * jax.nn.sigmoid(-dpo_beta * (ratio_chosen - ratio_rejected))
    coefficient = jnp.sum(
        jnp.where(pick_rejected, weight[:, None], 0.0)
        - jnp.where(pick_chosen, weight[:, None], 0.0),
        0,
    )
    slots = pair_slots.reshape(-1).astype(jnp.int32)
    goals = pair_goal[:, 0].astype(jnp.int32)
    prefix_all = lax.all_gather(prefix_kv, "dp", axis=0, tiled=True)
    grad_q, grad_kv, partial = attend_all(
        slots, goals, prefix_len.astype(jnp.int32), coefficient,
        queries, out_grad, suffix_kv, prefix_all)
    prefix_grad = lax.psum_scatter(partial, "dp", scatter_dimension=0, tiled=True)
    return grad_q, grad_kv, prefix_grad.astype(jnp.bfloat16)


def pipelined(queries, suffix_kv, out_grad, prefix_kv, logratio, pair_slots, pair_goal, prefix_len):
    partner = [(i, i ^ 1) for i in range(4)]
    across = [(i, i ^ 2) for i in range(4)]
    pre_across = lax.ppermute(prefix_kv, "dp", across)
    pre_partner = lax.ppermute(prefix_kv, "dp", partner)
    me = lax.axis_index("dp").astype(jnp.int32).reshape(1)
    tables = (me, pair_goal.reshape(-1).astype(jnp.int32), pair_slots.T.astype(jnp.int32),
              prefix_len.astype(jnp.int32), logratio)

    def run(flip, prefix_one, chain, **extra):
        grad_q, grad_kv, partial = attend_slot(flip, *tables, queries, out_grad, suffix_kv, prefix_one, chain,
                                               **extra)
        return (grad_q, grad_kv), partial

    chain, near = run(1, pre_partner, None)
    pre_across, near = lax.optimization_barrier((pre_across, near))
    pre_relay = lax.ppermute(pre_across, "dp", partner)
    near_sent = lax.ppermute(near, "dp", partner)
    chain, cross = run(2, pre_across, chain)
    chain, relay = run(3, pre_relay, chain, low=True)
    forward = (cross + lax.ppermute(relay, "dp", partner).astype(jnp.float32)).astype(jnp.bfloat16)
    forward, own_prefix = lax.optimization_barrier((forward, prefix_kv))
    chain, own = run(0, own_prefix, chain, seed=near_sent)
    total = own + lax.ppermute(forward, "dp", across).astype(jnp.float32)
    return chain[0], chain[1], total.astype(jnp.bfloat16)


def solution(mesh):
    return jax.shard_map(
        shards,
        mesh=mesh,
        in_specs=(
            P(("groups", "dp"), None, "tensor"),
            P(("groups", "dp"), None, None, "tensor"),
            P(("groups", "dp"), None, "tensor"),
            P(("groups", "dp"), None, None, "tensor"),
            P(("groups", "dp")),
            P(("groups", "dp"), None),
            P(("groups", "dp"), None),
            P("groups"),
        ),
        out_specs=(
            P(("groups", "dp"), None, "tensor"),
            P(("groups", "dp"), None, None, "tensor"),
            P(("groups", "dp"), None, None, "tensor"),
        ),
        check_vma=False,
    )
```

```python
import functools

import jax
import jax.numpy as jnp
from jax import lax
from jax.experimental import pallas as pl
from jax.experimental.pallas import tpu as pltpu
from jax.sharding import PartitionSpec as P

HD = 128
LOG2E = 1.4426950408889634

dpo_beta = 0.5


def mask_bias(length, *, group, seq, prefix_rows):
    shape = (seq + prefix_rows, group * seq)
    key_index = lax.broadcasted_iota(jnp.int32, shape, 0)
    tok_index = lax.broadcasted_iota(jnp.int32, shape, 1) % seq
    in_suffix = key_index < seq
    allowed = (in_suffix & (key_index <= tok_index)) | (
        jnp.logical_not(in_suffix) & (key_index - seq < length))
    return jnp.where(allowed, 0.0, -1e30).astype(jnp.float32)


def attend_math(q_blk, og_blk, keys_pre, values_pre, keys_own, values_own, bias, coef, *, group, seq):
    scale = HD ** (-0.5)
    cot_blk = (coef * og_blk.astype(jnp.float32)).astype(jnp.bfloat16)
    q_rows = jnp.concatenate([q_blk[:, g * HD:(g + 1) * HD] for g in range(group)], 0)
    c_rows = jnp.concatenate([cot_blk[:, g * HD:(g + 1) * HD] for g in range(group)], 0)
    keys = jnp.concatenate([keys_own, keys_pre], 0)
    values = jnp.concatenate([values_own, values_pre], 0)

    nt = (((1,), (1,)), ((), ()))
    scores_t = lax.dot_general(keys, q_rows, nt, preferred_element_type=jnp.float32) * (scale * LOG2E)
    scores_t = scores_t + bias
    col_max = jnp.max(scores_t, 0, keepdims=True)
    raised = jnp.exp2(scores_t - col_max)
    inv_sum = 1.0 / jnp.sum(raised, 0, keepdims=True)
    prob_low_t = (raised * inv_sum).astype(jnp.bfloat16)
    output_t = jnp.dot(values.T, prob_low_t, preferred_element_type=jnp.float32)
    row_dot = jnp.sum(c_rows.T.astype(jnp.float32) * output_t, 0, keepdims=True)
    grad_prob_t = lax.dot_general(values, c_rows, nt, preferred_element_type=jnp.float32)
    grad_score_t = (raised * ((grad_prob_t - row_dot) * inv_sum)).astype(jnp.bfloat16)
    grad_q_t = jnp.dot(keys.T, grad_score_t, preferred_element_type=jnp.float32)
    grad_q = (scale * grad_q_t.T).astype(jnp.bfloat16)
    grad_k = scale * jnp.dot(grad_score_t, q_rows, preferred_element_type=jnp.float32)
    grad_v = jnp.dot(prob_low_t, c_rows, preferred_element_type=jnp.float32)
    return grad_q, grad_k, grad_v


def store_grads(grad_q, grad_k, grad_v, member, dq_ref, dkv_ref, dpre_ref, *, group, seq, prefix_rows, head=0):
    active = grad_k.shape[0] - seq
    kv_cols = pl.ds(pl.multiple_of(head * HD, HD), HD)
    for g in range(group):
        q_cols = pl.ds(pl.multiple_of((head * group + g) * HD, HD), HD)
        dq_ref[0, :, q_cols] = grad_q[g * seq:(g + 1) * seq]
    dkv_ref[0, 0, :, kv_cols] = grad_k[:seq].astype(jnp.bfloat16)
    dkv_ref[0, 1, :, kv_cols] = grad_v[:seq].astype(jnp.bfloat16)

    @pl.when(member == 0)
    def _():
        dpre_ref[0, 0, :active, kv_cols] = grad_k[seq:]
        dpre_ref[0, 1, :active, kv_cols] = grad_v[seq:]
        if active < prefix_rows:
            zeros = jnp.zeros((prefix_rows - active, HD), jnp.float32)
            dpre_ref[0, 0, active:, kv_cols] = zeros
            dpre_ref[0, 1, active:, kv_cols] = zeros

    @pl.when(member != 0)
    def _():
        dpre_ref[0, 0, :active, kv_cols] += grad_k[seq:]
        dpre_ref[0, 1, :active, kv_cols] += grad_v[seq:]


def attend_kernel(slots_ref, goal_ref, len_ref, coef_ref,
                  q_ref, og_ref, skv_ref, pkv_ref,
                  dq_ref, dkv_ref, dpre_ref, *, group, seq, prefix_rows):
    p = pl.program_id(0)
    member = pl.program_id(2)
    s = slots_ref[2 * p + member]
    length = len_ref[goal_ref[p]]
    bias = mask_bias(length, group=group, seq=seq, prefix_rows=prefix_rows)
    grads = attend_math(q_ref[0], og_ref[0], pkv_ref[0, 0], pkv_ref[0, 1], skv_ref[0, 0], skv_ref[0, 1],
                        bias, coef_ref[s], group=group, seq=seq)
    store_grads(*grads, member, dq_ref, dkv_ref, dpre_ref, group=group, seq=seq, prefix_rows=prefix_rows)


def pair_of(goal, goal_ref, pair_count):
    pair = 0
    for p in range(pair_count):
        pair = jnp.where(goal_ref[p] == goal, p, pair)
    return pair


def slot_kernel(me_ref, goal_ref, slots_ref, len_ref, lr_ref, q_ref, og_ref, skv_ref, pkv_ref, *rest,
                group, seq, prefix_rows, flip, pair_count, chained, seeded, low):
    if chained:
        rest = rest[2:]
    seed_ref = None
    if seeded:
        seed_ref, rest = rest[0], rest[1:]
    dq_ref, dkv_ref, dpre_ref, bias_ref = rest[:4]
    acc_ref = rest[4] if low else dpre_ref
    member = pl.program_id(0)
    goal = me_ref[0] ^ flip
    pair = pair_of(goal, goal_ref, pair_count)
    length = len_ref[goal]
    dims = dict(group=group, seq=seq, prefix_rows=prefix_rows)
    heads = skv_ref.shape[-1] // HD
    qb = group * HD

    @pl.when(member == 0)
    def _():
        bias_ref[...] = mask_bias(length, **dims)

    gap = lr_ref[slots_ref[0, pair]] - lr_ref[slots_ref[1, pair]]
    x = jnp.full((1, 128), -dpo_beta * gap, jnp.float32)
    weight = dpo_beta * (1.0 / (1.0 + jnp.exp(-x)))
    coef = jnp.where(member == 0, -weight, weight)[:, :1]
    blocks = (seq + length + 127) // 128

    def one_head(h, carry):
        q_cols = pl.ds(pl.multiple_of(h * qb, qb), qb)
        kv_cols = pl.ds(pl.multiple_of(h * HD, HD), HD)
        for used in range(1, (seq + prefix_rows + 127) // 128 + 1):
            @pl.when(blocks == used)
            def _():
                width = min(used * 128, seq + prefix_rows)
                grads = attend_math(q_ref[0, :, q_cols], og_ref[0, :, q_cols],
                                    pkv_ref[0, 0, :width - seq, kv_cols], pkv_ref[0, 1, :width - seq, kv_cols],
                                    skv_ref[0, 0, :, kv_cols], skv_ref[0, 1, :, kv_cols], bias_ref[:width], coef,
                                    group=group, seq=seq)
                store_grads(*grads, member, dq_ref, dkv_ref, acc_ref, head=h, **dims)
        return carry

    lax.fori_loop(0, heads, one_head, 0)

    if seeded:
        @pl.when(member == 1)
        def _():
            acc_ref[...] += seed_ref[...]
    if low:
        @pl.when(member == 1)
        def _():
            dpre_ref[...] = acc_ref[...].astype(dpre_ref.dtype)


def attend_slot(flip, me, goals, slots, lengths, logratio, queries, out_grad, suffix_kv, prefix_one, chain,
                seed=None, low=False):
    suffix_count, seq, qwidth = queries.shape
    kv_width = suffix_kv.shape[-1]
    kv_local = kv_width // HD
    group = qwidth // kv_width
    prefix_rows = prefix_one.shape[2]
    pair_count = goals.shape[0]
    qb = group * HD

    def suffix_of(m, me_ref, goal_ref, slots_ref):
        pair = pair_of(me_ref[0] ^ flip, goal_ref, pair_count)
        return slots_ref[m, pair]

    def q_map(m, me_ref, goal_ref, slots_ref, len_ref):
        return (suffix_of(m, me_ref, goal_ref, slots_ref), 0, 0)

    def skv_map(m, me_ref, goal_ref, slots_ref, len_ref):
        return (suffix_of(m, me_ref, goal_ref, slots_ref), 0, 0, 0)

    def pkv_map(m, me_ref, goal_ref, slots_ref, len_ref):
        return (0, 0, 0, 0)

    out_shape = (
        jax.ShapeDtypeStruct((suffix_count, seq, qwidth), jnp.bfloat16),
        jax.ShapeDtypeStruct((suffix_count, 2, seq, kv_width), jnp.bfloat16),
        jax.ShapeDtypeStruct((1, 2, prefix_rows, kv_width), jnp.bfloat16 if low else jnp.float32),
    )
    in_specs = [
        pl.BlockSpec(memory_space=pltpu.SMEM),
        pl.BlockSpec((1, seq, qwidth), q_map),
        pl.BlockSpec((1, seq, qwidth), q_map),
        pl.BlockSpec((1, 2, seq, kv_width), skv_map),
        pl.BlockSpec((1, 2, prefix_rows, kv_width), pkv_map),
    ]
    operands = [logratio, queries, out_grad, suffix_kv, prefix_one]
    aliases = {}
    if chain is not None:
        in_specs += [pl.BlockSpec(memory_space=pl.ANY)] * 2
        operands += list(chain)
        aliases = {9: 0, 10: 1}
    if seed is not None:
        in_specs.append(pl.BlockSpec((1, 2, prefix_rows, kv_width), pkv_map))
        operands.append(seed)
    scratch = [pltpu.VMEM((prefix_rows + seq, group * seq), jnp.float32)]
    if low:
        scratch.append(pltpu.VMEM((1, 2, prefix_rows, kv_width), jnp.float32))
    kernel = functools.partial(slot_kernel, group=group, seq=seq, prefix_rows=prefix_rows, flip=flip,
                               pair_count=pair_count, chained=chain is not None, seeded=seed is not None,
                               low=low)
    grid_spec = pltpu.PrefetchScalarGridSpec(
        num_scalar_prefetch=4,
        grid=(2,),
        in_specs=in_specs,
        out_specs=[
            pl.BlockSpec((1, seq, qwidth), q_map),
            pl.BlockSpec((1, 2, seq, kv_width), skv_map),
            pl.BlockSpec((1, 2, prefix_rows, kv_width), pkv_map),
        ],
        scratch_shapes=scratch,
    )
    steps = 2 * kv_local
    cost = pl.CostEstimate(
        flops=steps * 2_200_000_000,
        transcendentals=steps * group * seq * (prefix_rows + seq),
        bytes_accessed=steps * (4 * seq * qb + 4 * seq * HD + 6 * prefix_rows * HD) * 2,
    )
    return pl.pallas_call(
        kernel,
        grid_spec=grid_spec,
        out_shape=out_shape,
        input_output_aliases=aliases,
        cost_estimate=cost,
        compiler_params=pltpu.CompilerParams(dimension_semantics=("arbitrary",)),
    )(me, goals, slots, lengths, *operands)


def attend_all(slots, goals, lengths, coef, queries, out_grad, suffix_kv, prefix_all):
    suffix_count, seq, qwidth = queries.shape
    kv_width = suffix_kv.shape[-1]
    kv_local = kv_width // HD
    group = qwidth // kv_width
    goal_count, _, prefix_rows, _ = prefix_all.shape
    pair_count = goals.shape[0]
    qb = group * HD

    def q_map(p, k, m, slots_ref, goal_ref, len_ref):
        return (slots_ref[2 * p + m], 0, k)

    def skv_map(p, k, m, slots_ref, goal_ref, len_ref):
        return (slots_ref[2 * p + m], 0, 0, k)

    def pkv_map(p, k, m, slots_ref, goal_ref, len_ref):
        return (goal_ref[p], 0, 0, k)

    kernel = functools.partial(attend_kernel, group=group, seq=seq, prefix_rows=prefix_rows)
    out_shape = (
        jax.ShapeDtypeStruct((suffix_count, seq, qwidth), jnp.bfloat16),
        jax.ShapeDtypeStruct((suffix_count, 2, seq, kv_width), jnp.bfloat16),
        jax.ShapeDtypeStruct((goal_count, 2, prefix_rows, kv_width), jnp.float32),
    )
    in_specs = [
        pl.BlockSpec(memory_space=pltpu.SMEM),
        pl.BlockSpec((1, seq, qb), q_map),
        pl.BlockSpec((1, seq, qb), q_map),
        pl.BlockSpec((1, 2, seq, HD), skv_map),
        pl.BlockSpec((1, 2, prefix_rows, HD), pkv_map),
    ]
    operands = [coef, queries, out_grad, suffix_kv, prefix_all]
    aliases = {}
    if pair_count < goal_count:
        in_specs.append(pl.BlockSpec(memory_space=pl.ANY))
        operands.append(jnp.zeros(out_shape[2].shape, jnp.float32))
        aliases = {3 + len(operands) - 1: 2}

        def kernel_with_zero(*refs):
            return kernel(*refs[:8], *refs[9:])
        body = kernel_with_zero
    else:
        body = kernel
    grid_spec = pltpu.PrefetchScalarGridSpec(
        num_scalar_prefetch=3,
        grid=(pair_count, kv_local, 2),
        in_specs=in_specs,
        out_specs=[
            pl.BlockSpec((1, seq, qb), q_map),
            pl.BlockSpec((1, 2, seq, HD), skv_map),
            pl.BlockSpec((1, 2, prefix_rows, HD), pkv_map),
        ],
    )
    return pl.pallas_call(
        body,
        grid_spec=grid_spec,
        out_shape=out_shape,
        input_output_aliases=aliases,
        compiler_params=pltpu.CompilerParams(
            dimension_semantics=("arbitrary", "arbitrary", "arbitrary")),
    )(slots, goals, lengths, *operands)


def shards(queries, suffix_kv, out_grad, prefix_kv, logratio, pair_slots, pair_goal, prefix_len):
    dp_size = lax.axis_size("dp")
    pair_count = pair_slots.shape[0]
    if dp_size == 4 and pair_count == dp_size:
        return pipelined(queries, suffix_kv, out_grad, prefix_kv, logratio,
                         pair_slots, pair_goal, prefix_len)
    suffix_count = queries.shape[0]
    chosen = pair_slots[:, 0]
    rejected = pair_slots[:, 1]
    positions = jnp.arange(suffix_count)
    pick_chosen = chosen[:, None] == positions[None, :]
    pick_rejected = rejected[:, None] == positions[None, :]
    ratio_chosen = jnp.sum(jnp.where(pick_chosen, logratio[None, :], 0.0), 1)
    ratio_rejected = jnp.sum(jnp.where(pick_rejected, logratio[None, :], 0.0), 1)
    weight = dpo_beta * jax.nn.sigmoid(-dpo_beta * (ratio_chosen - ratio_rejected))
    coefficient = jnp.sum(
        jnp.where(pick_rejected, weight[:, None], 0.0)
        - jnp.where(pick_chosen, weight[:, None], 0.0),
        0,
    )
    slots = pair_slots.reshape(-1).astype(jnp.int32)
    goals = pair_goal[:, 0].astype(jnp.int32)
    prefix_all = lax.all_gather(prefix_kv, "dp", axis=0, tiled=True)
    grad_q, grad_kv, partial = attend_all(
        slots, goals, prefix_len.astype(jnp.int32), coefficient,
        queries, out_grad, suffix_kv, prefix_all)
    prefix_grad = lax.psum_scatter(partial, "dp", scatter_dimension=0, tiled=True)
    return grad_q, grad_kv, prefix_grad.astype(jnp.bfloat16)


def pipelined(queries, suffix_kv, out_grad, prefix_kv, logratio, pair_slots, pair_goal, prefix_len):
    partner = [(i, i ^ 1) for i in range(4)]
    across = [(i, i ^ 2) for i in range(4)]
    pre_across = lax.ppermute(prefix_kv, "dp", across)
    pre_partner = lax.ppermute(prefix_kv, "dp", partner)
    me = lax.axis_index("dp").astype(jnp.int32).reshape(1)
    tables = (me, pair_goal.reshape(-1).astype(jnp.int32), pair_slots.T.astype(jnp.int32),
              prefix_len.astype(jnp.int32), logratio)

    def run(flip, prefix_one, chain, **extra):
        grad_q, grad_kv, partial = attend_slot(flip, *tables, queries, out_grad, suffix_kv, prefix_one, chain,
                                               **extra)
        return (grad_q, grad_kv), partial

    chain, near = run(1, pre_partner, None)
    pre_across, near = lax.optimization_barrier((pre_across, near))
    pre_relay = lax.ppermute(pre_across, "dp", partner)
    near_sent = lax.ppermute(near, "dp", partner)
    chain, cross = run(2, pre_across, chain)
    chain, relay = run(3, pre_relay, chain, low=True)
    forward = (cross + lax.ppermute(relay, "dp", partner).astype(jnp.float32)).astype(jnp.bfloat16)
    forward, own_prefix = lax.optimization_barrier((forward, prefix_kv))
    chain, own = run(0, own_prefix, chain, seed=near_sent, low=True)
    total = own.astype(jnp.float32) + lax.ppermute(forward, "dp", across).astype(jnp.float32)
    return chain[0], chain[1], total.astype(jnp.bfloat16)


def solution(mesh):
    return jax.shard_map(
        shards,
        mesh=mesh,
        in_specs=(
            P(("groups", "dp"), None, "tensor"),
            P(("groups", "dp"), None, None, "tensor"),
            P(("groups", "dp"), None, "tensor"),
            P(("groups", "dp"), None, None, "tensor"),
            P(("groups", "dp")),
            P(("groups", "dp"), None),
            P(("groups", "dp"), None),
            P("groups"),
        ),
        out_specs=(
            P(("groups", "dp"), None, "tensor"),
            P(("groups", "dp"), None, None, "tensor"),
            P(("groups", "dp"), None, None, "tensor"),
        ),
        check_vma=False,
    )
```

```python
import functools

import jax
import jax.numpy as jnp
from jax import lax
from jax.experimental import pallas as pl
from jax.experimental.pallas import tpu as pltpu
from jax.sharding import PartitionSpec as P

HD = 128
LOG2E = 1.4426950408889634

dpo_beta = 0.5


def mask_bias(length, *, group, seq, prefix_rows):
    shape = (seq + prefix_rows, group * seq)
    key_index = lax.broadcasted_iota(jnp.int32, shape, 0)
    tok_index = lax.broadcasted_iota(jnp.int32, shape, 1) % seq
    in_suffix = key_index < seq
    allowed = (in_suffix & (key_index <= tok_index)) | (
        jnp.logical_not(in_suffix) & (key_index - seq < length))
    return jnp.where(allowed, 0.0, -1e30).astype(jnp.float32)


def attend_math(q_blk, og_blk, keys_pre, values_pre, keys_own, values_own, bias, coef, *, group, seq):
    scale = HD ** (-0.5)
    cot_blk = (coef * og_blk.astype(jnp.float32)).astype(jnp.bfloat16)
    q_rows = jnp.concatenate([q_blk[:, g * HD:(g + 1) * HD] for g in range(group)], 0)
    c_rows = jnp.concatenate([cot_blk[:, g * HD:(g + 1) * HD] for g in range(group)], 0)
    keys = jnp.concatenate([keys_own, keys_pre], 0)
    values = jnp.concatenate([values_own, values_pre], 0)

    nt = (((1,), (1,)), ((), ()))
    scores_t = lax.dot_general(keys, q_rows, nt, preferred_element_type=jnp.float32) * (scale * LOG2E)
    scores_t = scores_t + bias
    col_max = jnp.max(scores_t, 0, keepdims=True)
    raised = jnp.exp2(scores_t - col_max)
    inv_sum = 1.0 / jnp.sum(raised, 0, keepdims=True)
    prob_low_t = (raised * inv_sum).astype(jnp.bfloat16)
    output_t = jnp.dot(values.T, prob_low_t, preferred_element_type=jnp.float32)
    row_dot = jnp.sum(c_rows.T.astype(jnp.float32) * output_t, 0, keepdims=True)
    grad_prob_t = lax.dot_general(values, c_rows, nt, preferred_element_type=jnp.float32)
    grad_score_t = (raised * ((grad_prob_t - row_dot) * inv_sum)).astype(jnp.bfloat16)
    grad_q_t = jnp.dot(keys.T, grad_score_t, preferred_element_type=jnp.float32)
    grad_q = (scale * grad_q_t.T).astype(jnp.bfloat16)
    grad_k = scale * jnp.dot(grad_score_t, q_rows, preferred_element_type=jnp.float32)
    grad_v = jnp.dot(prob_low_t, c_rows, preferred_element_type=jnp.float32)
    return grad_q, grad_k, grad_v


def store_grads(grad_q, grad_k, grad_v, member, dq_ref, dkv_ref, dpre_ref, *, group, seq, prefix_rows, head=0):
    active = grad_k.shape[0] - seq
    kv_cols = pl.ds(pl.multiple_of(head * HD, HD), HD)
    for g in range(group):
        q_cols = pl.ds(pl.multiple_of((head * group + g) * HD, HD), HD)
        dq_ref[0, :, q_cols] = grad_q[g * seq:(g + 1) * seq]
    dkv_ref[0, 0, :, kv_cols] = grad_k[:seq].astype(jnp.bfloat16)
    dkv_ref[0, 1, :, kv_cols] = grad_v[:seq].astype(jnp.bfloat16)

    @pl.when(member == 0)
    def _():
        dpre_ref[0, 0, :active, kv_cols] = grad_k[seq:]
        dpre_ref[0, 1, :active, kv_cols] = grad_v[seq:]
        if active < prefix_rows:
            zeros = jnp.zeros((prefix_rows - active, HD), jnp.float32)
            dpre_ref[0, 0, active:, kv_cols] = zeros
            dpre_ref[0, 1, active:, kv_cols] = zeros

    @pl.when(member != 0)
    def _():
        dpre_ref[0, 0, :active, kv_cols] += grad_k[seq:]
        dpre_ref[0, 1, :active, kv_cols] += grad_v[seq:]


def attend_kernel(slots_ref, goal_ref, len_ref, coef_ref,
                  q_ref, og_ref, skv_ref, pkv_ref,
                  dq_ref, dkv_ref, dpre_ref, *, group, seq, prefix_rows):
    p = pl.program_id(0)
    member = pl.program_id(2)
    s = slots_ref[2 * p + member]
    length = len_ref[goal_ref[p]]
    bias = mask_bias(length, group=group, seq=seq, prefix_rows=prefix_rows)
    grads = attend_math(q_ref[0], og_ref[0], pkv_ref[0, 0], pkv_ref[0, 1], skv_ref[0, 0], skv_ref[0, 1],
                        bias, coef_ref[s], group=group, seq=seq)
    store_grads(*grads, member, dq_ref, dkv_ref, dpre_ref, group=group, seq=seq, prefix_rows=prefix_rows)


def pair_of(goal, goal_ref, pair_count):
    pair = 0
    for p in range(pair_count):
        pair = jnp.where(goal_ref[p] == goal, p, pair)
    return pair


def slot_kernel(me_ref, goal_ref, slots_ref, len_ref, lr_ref, q_ref, og_ref, skv_ref, pkv_ref, *rest,
                group, seq, prefix_rows, flip, pair_count, chained, seeded, low):
    if chained:
        rest = rest[2:]
    seed_ref = None
    if seeded:
        seed_ref, rest = rest[0], rest[1:]
    dq_ref, dkv_ref, dpre_ref, bias_ref = rest[:4]
    acc_ref = rest[4] if low else dpre_ref
    member = pl.program_id(0)
    goal = me_ref[0] ^ flip
    pair = pair_of(goal, goal_ref, pair_count)
    length = len_ref[goal]
    dims = dict(group=group, seq=seq, prefix_rows=prefix_rows)
    heads = skv_ref.shape[-1] // HD
    qb = group * HD

    @pl.when(member == 0)
    def _():
        bias_ref[...] = mask_bias(length, **dims)

    gap = lr_ref[slots_ref[0, pair]] - lr_ref[slots_ref[1, pair]]
    x = jnp.full((1, 128), -dpo_beta * gap, jnp.float32)
    weight = dpo_beta * (1.0 / (1.0 + jnp.exp(-x)))
    coef = jnp.where(member == 0, -weight, weight)[:, :1]
    blocks = (length + 63) // 64

    def one_head(h, carry):
        q_cols = pl.ds(pl.multiple_of(h * qb, qb), qb)
        kv_cols = pl.ds(pl.multiple_of(h * HD, HD), HD)
        for used in range(1, (prefix_rows + 63) // 64 + 1):
            @pl.when(blocks == used)
            def _():
                width = min(seq + used * 64, seq + prefix_rows)
                grads = attend_math(q_ref[0, :, q_cols], og_ref[0, :, q_cols],
                                    pkv_ref[0, 0, :width - seq, kv_cols], pkv_ref[0, 1, :width - seq, kv_cols],
                                    skv_ref[0, 0, :, kv_cols], skv_ref[0, 1, :, kv_cols], bias_ref[:width], coef,
                                    group=group, seq=seq)
                store_grads(*grads, member, dq_ref, dkv_ref, acc_ref, head=h, **dims)
        return carry

    lax.fori_loop(0, heads, one_head, 0)

    if seeded:
        @pl.when(member == 1)
        def _():
            dpre_ref[...] += seed_ref[...]
    if low:
        @pl.when(member == 1)
        def _():
            dpre_ref[...] = acc_ref[...].astype(dpre_ref.dtype)


def attend_slot(flip, me, goals, slots, lengths, logratio, queries, out_grad, suffix_kv, prefix_one, chain,
                seed=None, low=False):
    suffix_count, seq, qwidth = queries.shape
    kv_width = suffix_kv.shape[-1]
    kv_local = kv_width // HD
    group = qwidth // kv_width
    prefix_rows = prefix_one.shape[2]
    pair_count = goals.shape[0]
    qb = group * HD

    def suffix_of(m, me_ref, goal_ref, slots_ref):
        pair = pair_of(me_ref[0] ^ flip, goal_ref, pair_count)
        return slots_ref[m, pair]

    def q_map(m, me_ref, goal_ref, slots_ref, len_ref):
        return (suffix_of(m, me_ref, goal_ref, slots_ref), 0, 0)

    def skv_map(m, me_ref, goal_ref, slots_ref, len_ref):
        return (suffix_of(m, me_ref, goal_ref, slots_ref), 0, 0, 0)

    def pkv_map(m, me_ref, goal_ref, slots_ref, len_ref):
        return (0, 0, 0, 0)

    out_shape = (
        jax.ShapeDtypeStruct((suffix_count, seq, qwidth), jnp.bfloat16),
        jax.ShapeDtypeStruct((suffix_count, 2, seq, kv_width), jnp.bfloat16),
        jax.ShapeDtypeStruct((1, 2, prefix_rows, kv_width), jnp.bfloat16 if low else jnp.float32),
    )
    in_specs = [
        pl.BlockSpec(memory_space=pltpu.SMEM),
        pl.BlockSpec((1, seq, qwidth), q_map),
        pl.BlockSpec((1, seq, qwidth), q_map),
        pl.BlockSpec((1, 2, seq, kv_width), skv_map),
        pl.BlockSpec((1, 2, prefix_rows, kv_width), pkv_map),
    ]
    operands = [logratio, queries, out_grad, suffix_kv, prefix_one]
    aliases = {}
    if chain is not None:
        in_specs += [pl.BlockSpec(memory_space=pl.ANY)] * 2
        operands += list(chain)
        aliases = {9: 0, 10: 1}
    if seed is not None:
        in_specs.append(pl.BlockSpec((1, 2, prefix_rows, kv_width), pkv_map))
        operands.append(seed)
    scratch = [pltpu.VMEM((prefix_rows + seq, group * seq), jnp.float32)]
    if low:
        scratch.append(pltpu.VMEM((1, 2, prefix_rows, kv_width), jnp.float32))
    kernel = functools.partial(slot_kernel, group=group, seq=seq, prefix_rows=prefix_rows, flip=flip,
                               pair_count=pair_count, chained=chain is not None, seeded=seed is not None,
                               low=low)
    grid_spec = pltpu.PrefetchScalarGridSpec(
        num_scalar_prefetch=4,
        grid=(2,),
        in_specs=in_specs,
        out_specs=[
            pl.BlockSpec((1, seq, qwidth), q_map),
            pl.BlockSpec((1, 2, seq, kv_width), skv_map),
            pl.BlockSpec((1, 2, prefix_rows, kv_width), pkv_map),
        ],
        scratch_shapes=scratch,
    )
    steps = 2 * kv_local
    cost = pl.CostEstimate(
        flops=steps * 2_200_000_000,
        transcendentals=steps * group * seq * (prefix_rows + seq),
        bytes_accessed=steps * (4 * seq * qb + 4 * seq * HD + 6 * prefix_rows * HD) * 2,
    )
    return pl.pallas_call(
        kernel,
        grid_spec=grid_spec,
        out_shape=out_shape,
        input_output_aliases=aliases,
        cost_estimate=cost,
        compiler_params=pltpu.CompilerParams(dimension_semantics=("arbitrary",)),
    )(me, goals, slots, lengths, *operands)


def attend_all(slots, goals, lengths, coef, queries, out_grad, suffix_kv, prefix_all):
    suffix_count, seq, qwidth = queries.shape
    kv_width = suffix_kv.shape[-1]
    kv_local = kv_width // HD
    group = qwidth // kv_width
    goal_count, _, prefix_rows, _ = prefix_all.shape
    pair_count = goals.shape[0]
    qb = group * HD

    def q_map(p, k, m, slots_ref, goal_ref, len_ref):
        return (slots_ref[2 * p + m], 0, k)

    def skv_map(p, k, m, slots_ref, goal_ref, len_ref):
        return (slots_ref[2 * p + m], 0, 0, k)

    def pkv_map(p, k, m, slots_ref, goal_ref, len_ref):
        return (goal_ref[p], 0, 0, k)

    kernel = functools.partial(attend_kernel, group=group, seq=seq, prefix_rows=prefix_rows)
    out_shape = (
        jax.ShapeDtypeStruct((suffix_count, seq, qwidth), jnp.bfloat16),
        jax.ShapeDtypeStruct((suffix_count, 2, seq, kv_width), jnp.bfloat16),
        jax.ShapeDtypeStruct((goal_count, 2, prefix_rows, kv_width), jnp.float32),
    )
    in_specs = [
        pl.BlockSpec(memory_space=pltpu.SMEM),
        pl.BlockSpec((1, seq, qb), q_map),
        pl.BlockSpec((1, seq, qb), q_map),
        pl.BlockSpec((1, 2, seq, HD), skv_map),
        pl.BlockSpec((1, 2, prefix_rows, HD), pkv_map),
    ]
    operands = [coef, queries, out_grad, suffix_kv, prefix_all]
    aliases = {}
    if pair_count < goal_count:
        in_specs.append(pl.BlockSpec(memory_space=pl.ANY))
        operands.append(jnp.zeros(out_shape[2].shape, jnp.float32))
        aliases = {3 + len(operands) - 1: 2}

        def kernel_with_zero(*refs):
            return kernel(*refs[:8], *refs[9:])
        body = kernel_with_zero
    else:
        body = kernel
    grid_spec = pltpu.PrefetchScalarGridSpec(
        num_scalar_prefetch=3,
        grid=(pair_count, kv_local, 2),
        in_specs=in_specs,
        out_specs=[
            pl.BlockSpec((1, seq, qb), q_map),
            pl.BlockSpec((1, 2, seq, HD), skv_map),
            pl.BlockSpec((1, 2, prefix_rows, HD), pkv_map),
        ],
    )
    return pl.pallas_call(
        body,
        grid_spec=grid_spec,
        out_shape=out_shape,
        input_output_aliases=aliases,
        compiler_params=pltpu.CompilerParams(
            dimension_semantics=("arbitrary", "arbitrary", "arbitrary")),
    )(slots, goals, lengths, *operands)


def shards(queries, suffix_kv, out_grad, prefix_kv, logratio, pair_slots, pair_goal, prefix_len):
    dp_size = lax.axis_size("dp")
    pair_count = pair_slots.shape[0]
    if dp_size == 4 and pair_count == dp_size:
        return pipelined(queries, suffix_kv, out_grad, prefix_kv, logratio,
                         pair_slots, pair_goal, prefix_len)
    suffix_count = queries.shape[0]
    chosen = pair_slots[:, 0]
    rejected = pair_slots[:, 1]
    positions = jnp.arange(suffix_count)
    pick_chosen = chosen[:, None] == positions[None, :]
    pick_rejected = rejected[:, None] == positions[None, :]
    ratio_chosen = jnp.sum(jnp.where(pick_chosen, logratio[None, :], 0.0), 1)
    ratio_rejected = jnp.sum(jnp.where(pick_rejected, logratio[None, :], 0.0), 1)
    weight = dpo_beta * jax.nn.sigmoid(-dpo_beta * (ratio_chosen - ratio_rejected))
    coefficient = jnp.sum(
        jnp.where(pick_rejected, weight[:, None], 0.0)
        - jnp.where(pick_chosen, weight[:, None], 0.0),
        0,
    )
    slots = pair_slots.reshape(-1).astype(jnp.int32)
    goals = pair_goal[:, 0].astype(jnp.int32)
    prefix_all = lax.all_gather(prefix_kv, "dp", axis=0, tiled=True)
    grad_q, grad_kv, partial = attend_all(
        slots, goals, prefix_len.astype(jnp.int32), coefficient,
        queries, out_grad, suffix_kv, prefix_all)
    prefix_grad = lax.psum_scatter(partial, "dp", scatter_dimension=0, tiled=True)
    return grad_q, grad_kv, prefix_grad.astype(jnp.bfloat16)


def pipelined(queries, suffix_kv, out_grad, prefix_kv, logratio, pair_slots, pair_goal, prefix_len):
    partner = [(i, i ^ 1) for i in range(4)]
    across = [(i, i ^ 2) for i in range(4)]
    pre_across = lax.ppermute(prefix_kv, "dp", across)
    pre_partner = lax.ppermute(prefix_kv, "dp", partner)
    me = lax.axis_index("dp").astype(jnp.int32).reshape(1)
    tables = (me, pair_goal.reshape(-1).astype(jnp.int32), pair_slots.T.astype(jnp.int32),
              prefix_len.astype(jnp.int32), logratio)

    def run(flip, prefix_one, chain, **extra):
        grad_q, grad_kv, partial = attend_slot(flip, *tables, queries, out_grad, suffix_kv, prefix_one, chain,
                                               **extra)
        return (grad_q, grad_kv), partial

    chain, near = run(1, pre_partner, None)
    pre_across, near = lax.optimization_barrier((pre_across, near))
    pre_relay = lax.ppermute(pre_across, "dp", partner)
    near_sent = lax.ppermute(near, "dp", partner)
    chain, cross = run(2, pre_across, chain)
    chain, relay = run(3, pre_relay, chain, low=True)
    forward = (cross + lax.ppermute(relay, "dp", partner).astype(jnp.float32)).astype(jnp.bfloat16)
    forward, own_prefix = lax.optimization_barrier((forward, prefix_kv))
    chain, own = run(0, own_prefix, chain, seed=near_sent)
    total = own + lax.ppermute(forward, "dp", across).astype(jnp.float32)
    return chain[0], chain[1], total.astype(jnp.bfloat16)


def solution(mesh):
    return jax.shard_map(
        shards,
        mesh=mesh,
        in_specs=(
            P(("groups", "dp"), None, "tensor"),
            P(("groups", "dp"), None, None, "tensor"),
            P(("groups", "dp"), None, "tensor"),
            P(("groups", "dp"), None, None, "tensor"),
            P(("groups", "dp")),
            P(("groups", "dp"), None),
            P(("groups", "dp"), None),
            P("groups"),
        ),
        out_specs=(
            P(("groups", "dp"), None, "tensor"),
            P(("groups", "dp"), None, None, "tensor"),
            P(("groups", "dp"), None, None, "tensor"),
        ),
        check_vma=False,
    )
```

```python
import functools

import jax
import jax.numpy as jnp
from jax import lax
from jax.experimental import pallas as pl
from jax.experimental.pallas import tpu as pltpu
from jax.sharding import PartitionSpec as P

HD = 128
LOG2E = 1.4426950408889634

dpo_beta = 0.5


def mask_bias(length, *, group, seq, prefix_rows):
    shape = (seq + prefix_rows, group * seq)
    key_index = lax.broadcasted_iota(jnp.int32, shape, 0)
    tok_index = lax.broadcasted_iota(jnp.int32, shape, 1) % seq
    in_suffix = key_index < seq
    allowed = (in_suffix & (key_index <= tok_index)) | (
        jnp.logical_not(in_suffix) & (key_index - seq < length))
    return jnp.where(allowed, 0.0, -1e30).astype(jnp.float32)


def attend_math(q_blk, og_blk, keys_pre, values_pre, keys_own, values_own, bias, coef, *, group, seq):
    scale = HD ** (-0.5)
    cot_blk = (coef * og_blk.astype(jnp.float32)).astype(jnp.bfloat16)
    q_rows = jnp.concatenate([q_blk[:, g * HD:(g + 1) * HD] for g in range(group)], 0)
    c_rows = jnp.concatenate([cot_blk[:, g * HD:(g + 1) * HD] for g in range(group)], 0)
    keys = jnp.concatenate([keys_own, keys_pre], 0)
    values = jnp.concatenate([values_own, values_pre], 0)

    nt = (((1,), (1,)), ((), ()))
    scores_t = lax.dot_general(keys, q_rows, nt, preferred_element_type=jnp.float32) * (scale * LOG2E)
    scores_t = scores_t + bias
    col_max = jnp.max(scores_t, 0, keepdims=True)
    raised = jnp.exp2(scores_t - col_max)
    inv_sum = 1.0 / jnp.sum(raised, 0, keepdims=True)
    prob_low_t = (raised * inv_sum).astype(jnp.bfloat16)
    output_t = jnp.dot(values.T, prob_low_t, preferred_element_type=jnp.float32)
    row_dot = jnp.sum(c_rows.T.astype(jnp.float32) * output_t, 0, keepdims=True)
    grad_prob_t = lax.dot_general(values, c_rows, nt, preferred_element_type=jnp.float32)
    grad_score_t = (raised * ((grad_prob_t - row_dot) * inv_sum)).astype(jnp.bfloat16)
    grad_q_t = jnp.dot(keys.T, grad_score_t, preferred_element_type=jnp.float32)
    grad_q = (scale * grad_q_t.T).astype(jnp.bfloat16)
    grad_k = scale * jnp.dot(grad_score_t, q_rows, preferred_element_type=jnp.float32)
    grad_v = jnp.dot(prob_low_t, c_rows, preferred_element_type=jnp.float32)
    return grad_q, grad_k, grad_v


def store_grads(grad_q, grad_k, grad_v, member, dq_ref, dkv_ref, dpre_ref, *, group, seq, prefix_rows, head=0):
    active = grad_k.shape[0] - seq
    kv_cols = pl.ds(pl.multiple_of(head * HD, HD), HD)
    for g in range(group):
        q_cols = pl.ds(pl.multiple_of((head * group + g) * HD, HD), HD)
        dq_ref[0, :, q_cols] = grad_q[g * seq:(g + 1) * seq]
    dkv_ref[0, 0, :, kv_cols] = grad_k[:seq].astype(jnp.bfloat16)
    dkv_ref[0, 1, :, kv_cols] = grad_v[:seq].astype(jnp.bfloat16)

    @pl.when(member == 0)
    def _():
        dpre_ref[0, 0, :active, kv_cols] = grad_k[seq:]
        dpre_ref[0, 1, :active, kv_cols] = grad_v[seq:]
        if active < prefix_rows:
            zeros = jnp.zeros((prefix_rows - active, HD), jnp.float32)
            dpre_ref[0, 0, active:, kv_cols] = zeros
            dpre_ref[0, 1, active:, kv_cols] = zeros

    @pl.when(member != 0)
    def _():
        dpre_ref[0, 0, :active, kv_cols] += grad_k[seq:]
        dpre_ref[0, 1, :active, kv_cols] += grad_v[seq:]


def attend_kernel(slots_ref, goal_ref, len_ref, coef_ref,
                  q_ref, og_ref, skv_ref, pkv_ref,
                  dq_ref, dkv_ref, dpre_ref, *, group, seq, prefix_rows):
    p = pl.program_id(0)
    member = pl.program_id(2)
    s = slots_ref[2 * p + member]
    length = len_ref[goal_ref[p]]
    bias = mask_bias(length, group=group, seq=seq, prefix_rows=prefix_rows)
    grads = attend_math(q_ref[0], og_ref[0], pkv_ref[0, 0], pkv_ref[0, 1], skv_ref[0, 0], skv_ref[0, 1],
                        bias, coef_ref[s], group=group, seq=seq)
    store_grads(*grads, member, dq_ref, dkv_ref, dpre_ref, group=group, seq=seq, prefix_rows=prefix_rows)


def pair_of(goal, goal_ref, pair_count):
    pair = 0
    for p in range(pair_count):
        pair = jnp.where(goal_ref[p] == goal, p, pair)
    return pair


def flip_of(me, flip):
    if isinstance(flip, tuple):
        return jnp.where(me % 2 == 0, flip[0], flip[1])
    return flip


def slot_kernel(me_ref, goal_ref, slots_ref, len_ref, lr_ref, q_ref, og_ref, skv_ref, pkv_ref, *rest,
                group, seq, prefix_rows, flip, pair_count, chained, seeded, low):
    pkv_other = None
    if isinstance(flip, tuple):
        pkv_other, rest = rest[0], rest[1:]
    if chained:
        rest = rest[2:]
    seed_ref = None
    if seeded:
        seed_ref, rest = rest[0], rest[1:]
    dq_ref, dkv_ref, dpre_ref, bias_ref = rest[:4]
    acc_ref = rest[4] if low else dpre_ref
    member = pl.program_id(0)
    goal = me_ref[0] ^ flip_of(me_ref[0], flip)
    if pkv_other is not None:
        pre_ref = rest[-1]

        @pl.when((member == 0) & (me_ref[0] % 2 == 0))
        def _():
            pre_ref[...] = pkv_ref[...]

        @pl.when((member == 0) & (me_ref[0] % 2 != 0))
        def _():
            pre_ref[...] = pkv_other[...]
        pkv_ref = pre_ref
    pair = pair_of(goal, goal_ref, pair_count)
    length = len_ref[goal]
    dims = dict(group=group, seq=seq, prefix_rows=prefix_rows)
    heads = skv_ref.shape[-1] // HD
    qb = group * HD

    @pl.when(member == 0)
    def _():
        bias_ref[...] = mask_bias(length, **dims)

    gap = lr_ref[slots_ref[0, pair]] - lr_ref[slots_ref[1, pair]]
    x = jnp.full((1, 128), -dpo_beta * gap, jnp.float32)
    weight = dpo_beta * (1.0 / (1.0 + jnp.exp(-x)))
    coef = jnp.where(member == 0, -weight, weight)[:, :1]
    blocks = (seq + length + 127) // 128

    def one_head(h, carry):
        q_cols = pl.ds(pl.multiple_of(h * qb, qb), qb)
        kv_cols = pl.ds(pl.multiple_of(h * HD, HD), HD)
        for used in range(1, (seq + prefix_rows + 127) // 128 + 1):
            @pl.when(blocks == used)
            def _():
                width = min(used * 128, seq + prefix_rows)
                grads = attend_math(q_ref[0, :, q_cols], og_ref[0, :, q_cols],
                                    pkv_ref[0, 0, :width - seq, kv_cols], pkv_ref[0, 1, :width - seq, kv_cols],
                                    skv_ref[0, 0, :, kv_cols], skv_ref[0, 1, :, kv_cols], bias_ref[:width], coef,
                                    group=group, seq=seq)
                store_grads(*grads, member, dq_ref, dkv_ref, acc_ref, head=h, **dims)
        return carry

    lax.fori_loop(0, heads, one_head, 0)

    if seeded:
        @pl.when(member == 1)
        def _():
            dpre_ref[...] += seed_ref[...]
    if low:
        @pl.when(member == 1)
        def _():
            dpre_ref[...] = acc_ref[...].astype(dpre_ref.dtype)


def attend_slot(flip, me, goals, slots, lengths, logratio, queries, out_grad, suffix_kv, prefix_one, chain,
                seed=None, low=False, weight=1.0):
    suffix_count, seq, qwidth = queries.shape
    kv_width = suffix_kv.shape[-1]
    kv_local = kv_width // HD
    group = qwidth // kv_width
    pair_other = None
    if isinstance(prefix_one, tuple):
        prefix_one, pair_other = prefix_one
    prefix_rows = prefix_one.shape[2]
    pair_count = goals.shape[0]
    qb = group * HD

    def suffix_of(m, me_ref, goal_ref, slots_ref):
        pair = pair_of(me_ref[0] ^ flip_of(me_ref[0], flip), goal_ref, pair_count)
        return slots_ref[m, pair]

    def q_map(m, me_ref, goal_ref, slots_ref, len_ref):
        return (suffix_of(m, me_ref, goal_ref, slots_ref), 0, 0)

    def skv_map(m, me_ref, goal_ref, slots_ref, len_ref):
        return (suffix_of(m, me_ref, goal_ref, slots_ref), 0, 0, 0)

    def pkv_map(m, me_ref, goal_ref, slots_ref, len_ref):
        return (0, 0, 0, 0)

    out_shape = (
        jax.ShapeDtypeStruct((suffix_count, seq, qwidth), jnp.bfloat16),
        jax.ShapeDtypeStruct((suffix_count, 2, seq, kv_width), jnp.bfloat16),
        jax.ShapeDtypeStruct((1, 2, prefix_rows, kv_width), jnp.bfloat16 if low else jnp.float32),
    )
    in_specs = [
        pl.BlockSpec(memory_space=pltpu.SMEM),
        pl.BlockSpec((1, seq, qwidth), q_map),
        pl.BlockSpec((1, seq, qwidth), q_map),
        pl.BlockSpec((1, 2, seq, kv_width), skv_map),
        pl.BlockSpec((1, 2, prefix_rows, kv_width), pkv_map),
    ]
    operands = [logratio, queries, out_grad, suffix_kv, prefix_one]
    if pair_other is not None:
        in_specs.append(pl.BlockSpec((1, 2, prefix_rows, kv_width), pkv_map))
        operands.append(pair_other)
    aliases = {}
    if chain is not None:
        in_specs += [pl.BlockSpec(memory_space=pl.ANY)] * 2
        operands += list(chain)
        aliases = {4 + len(operands) - 2: 0, 4 + len(operands) - 1: 1}
    if seed is not None:
        in_specs.append(pl.BlockSpec((1, 2, prefix_rows, kv_width), pkv_map))
        operands.append(seed)
    scratch = [pltpu.VMEM((prefix_rows + seq, group * seq), jnp.float32)]
    if low:
        scratch.append(pltpu.VMEM((1, 2, prefix_rows, kv_width), jnp.float32))
    if pair_other is not None:
        scratch.append(pltpu.VMEM((1, 2, prefix_rows, kv_width), prefix_one.dtype))
    kernel = functools.partial(slot_kernel, group=group, seq=seq, prefix_rows=prefix_rows, flip=flip,
                               pair_count=pair_count, chained=chain is not None, seeded=seed is not None,
                               low=low)
    grid_spec = pltpu.PrefetchScalarGridSpec(
        num_scalar_prefetch=4,
        grid=(2,),
        in_specs=in_specs,
        out_specs=[
            pl.BlockSpec((1, seq, qwidth), q_map),
            pl.BlockSpec((1, 2, seq, kv_width), skv_map),
            pl.BlockSpec((1, 2, prefix_rows, kv_width), pkv_map),
        ],
        scratch_shapes=scratch,
    )
    steps = 2 * kv_local
    cost = pl.CostEstimate(
        flops=int(steps * 2_200_000_000 * weight),
        transcendentals=steps * group * seq * (prefix_rows + seq),
        bytes_accessed=int(weight * steps * (4 * seq * qb + 4 * seq * HD + 6 * prefix_rows * HD) * 2),
    )
    return pl.pallas_call(
        kernel,
        grid_spec=grid_spec,
        out_shape=out_shape,
        input_output_aliases=aliases,
        cost_estimate=cost,
        compiler_params=pltpu.CompilerParams(dimension_semantics=("arbitrary",)),
    )(me, goals, slots, lengths, *operands)


def attend_all(slots, goals, lengths, coef, queries, out_grad, suffix_kv, prefix_all):
    suffix_count, seq, qwidth = queries.shape
    kv_width = suffix_kv.shape[-1]
    kv_local = kv_width // HD
    group = qwidth // kv_width
    goal_count, _, prefix_rows, _ = prefix_all.shape
    pair_count = goals.shape[0]
    qb = group * HD

    def q_map(p, k, m, slots_ref, goal_ref, len_ref):
        return (slots_ref[2 * p + m], 0, k)

    def skv_map(p, k, m, slots_ref, goal_ref, len_ref):
        return (slots_ref[2 * p + m], 0, 0, k)

    def pkv_map(p, k, m, slots_ref, goal_ref, len_ref):
        return (goal_ref[p], 0, 0, k)

    kernel = functools.partial(attend_kernel, group=group, seq=seq, prefix_rows=prefix_rows)
    out_shape = (
        jax.ShapeDtypeStruct((suffix_count, seq, qwidth), jnp.bfloat16),
        jax.ShapeDtypeStruct((suffix_count, 2, seq, kv_width), jnp.bfloat16),
        jax.ShapeDtypeStruct((goal_count, 2, prefix_rows, kv_width), jnp.float32),
    )
    in_specs = [
        pl.BlockSpec(memory_space=pltpu.SMEM),
        pl.BlockSpec((1, seq, qb), q_map),
        pl.BlockSpec((1, seq, qb), q_map),
        pl.BlockSpec((1, 2, seq, HD), skv_map),
        pl.BlockSpec((1, 2, prefix_rows, HD), pkv_map),
    ]
    operands = [coef, queries, out_grad, suffix_kv, prefix_all]
    aliases = {}
    if pair_count < goal_count:
        in_specs.append(pl.BlockSpec(memory_space=pl.ANY))
        operands.append(jnp.zeros(out_shape[2].shape, jnp.float32))
        aliases = {3 + len(operands) - 1: 2}

        def kernel_with_zero(*refs):
            return kernel(*refs[:8], *refs[9:])
        body = kernel_with_zero
    else:
        body = kernel
    grid_spec = pltpu.PrefetchScalarGridSpec(
        num_scalar_prefetch=3,
        grid=(pair_count, kv_local, 2),
        in_specs=in_specs,
        out_specs=[
            pl.BlockSpec((1, seq, qb), q_map),
            pl.BlockSpec((1, 2, seq, HD), skv_map),
            pl.BlockSpec((1, 2, prefix_rows, HD), pkv_map),
        ],
    )
    return pl.pallas_call(
        body,
        grid_spec=grid_spec,
        out_shape=out_shape,
        input_output_aliases=aliases,
        compiler_params=pltpu.CompilerParams(
            dimension_semantics=("arbitrary", "arbitrary", "arbitrary")),
    )(slots, goals, lengths, *operands)


def shards(queries, suffix_kv, out_grad, prefix_kv, logratio, pair_slots, pair_goal, prefix_len):
    dp_size = lax.axis_size("dp")
    pair_count = pair_slots.shape[0]
    if dp_size == 4 and pair_count == dp_size:
        return pipelined(queries, suffix_kv, out_grad, prefix_kv, logratio,
                         pair_slots, pair_goal, prefix_len)
    suffix_count = queries.shape[0]
    chosen = pair_slots[:, 0]
    rejected = pair_slots[:, 1]
    positions = jnp.arange(suffix_count)
    pick_chosen = chosen[:, None] == positions[None, :]
    pick_rejected = rejected[:, None] == positions[None, :]
    ratio_chosen = jnp.sum(jnp.where(pick_chosen, logratio[None, :], 0.0), 1)
    ratio_rejected = jnp.sum(jnp.where(pick_rejected, logratio[None, :], 0.0), 1)
    weight = dpo_beta * jax.nn.sigmoid(-dpo_beta * (ratio_chosen - ratio_rejected))
    coefficient = jnp.sum(
        jnp.where(pick_rejected, weight[:, None], 0.0)
        - jnp.where(pick_chosen, weight[:, None], 0.0),
        0,
    )
    slots = pair_slots.reshape(-1).astype(jnp.int32)
    goals = pair_goal[:, 0].astype(jnp.int32)
    prefix_all = lax.all_gather(prefix_kv, "dp", axis=0, tiled=True)
    grad_q, grad_kv, partial = attend_all(
        slots, goals, prefix_len.astype(jnp.int32), coefficient,
        queries, out_grad, suffix_kv, prefix_all)
    prefix_grad = lax.psum_scatter(partial, "dp", scatter_dimension=0, tiled=True)
    return grad_q, grad_kv, prefix_grad.astype(jnp.bfloat16)


def pipelined(queries, suffix_kv, out_grad, prefix_kv, logratio, pair_slots, pair_goal, prefix_len):
    partner = [(i, i ^ 1) for i in range(4)]
    across = [(i, i ^ 2) for i in range(4)]
    odd_to_even = [(1, 0), (3, 2)]
    even_to_odd = [(0, 1), (2, 3)]
    pre_a = lax.ppermute(prefix_kv, "dp", [(0, 2), (2, 0)])
    pre_partner = lax.ppermute(prefix_kv, "dp", partner)
    me = lax.axis_index("dp").astype(jnp.int32).reshape(1)
    tables = (me, pair_goal.reshape(-1).astype(jnp.int32), pair_slots.T.astype(jnp.int32),
              prefix_len.astype(jnp.int32), logratio)

    def run(flip, prefix_one, chain, **extra):
        grad_q, grad_kv, partial = attend_slot(flip, *tables, queries, out_grad, suffix_kv, prefix_one, chain,
                                               **extra)
        return (grad_q, grad_kv), partial

    chain, near = run(1, pre_partner, None)
    pre_a, near, later = lax.optimization_barrier((pre_a, near, prefix_kv))
    relay_a = lax.ppermute(pre_a, "dp", even_to_odd)
    pre_b = lax.ppermute(later, "dp", [(1, 3), (3, 1)])
    near_sent = lax.ppermute(near, "dp", partner)
    chain, early = run((2, 3), (pre_a, relay_a), chain, low=True)
    relay_b = lax.ppermute(pre_b, "dp", odd_to_even)
    first = (early.astype(jnp.float32)
             + lax.ppermute(early, "dp", odd_to_even).astype(jnp.float32)).astype(jnp.bfloat16)
    first, relay_b = lax.optimization_barrier((first, relay_b))
    first_sent = lax.ppermute(first, "dp", [(0, 2), (2, 0)])
    chain, late = run((3, 2), (relay_b, pre_b), chain, low=True)
    second = (late.astype(jnp.float32)
              + lax.ppermute(late, "dp", even_to_odd).astype(jnp.float32)).astype(jnp.bfloat16)
    second, own_prefix = lax.optimization_barrier((second, prefix_kv))
    second_sent = lax.ppermute(second, "dp", [(1, 3), (3, 1)])
    chain, own = run(0, own_prefix, chain, seed=near_sent)
    even = lax.axis_index("dp") % 2 == 0
    total = own + jnp.where(even, first_sent, second_sent).astype(jnp.float32)
    return chain[0], chain[1], total.astype(jnp.bfloat16)


def solution(mesh):
    return jax.shard_map(
        shards,
        mesh=mesh,
        in_specs=(
            P(("groups", "dp"), None, "tensor"),
            P(("groups", "dp"), None, None, "tensor"),
            P(("groups", "dp"), None, "tensor"),
            P(("groups", "dp"), None, None, "tensor"),
            P(("groups", "dp")),
            P(("groups", "dp"), None),
            P(("groups", "dp"), None),
            P("groups"),
        ),
        out_specs=(
            P(("groups", "dp"), None, "tensor"),
            P(("groups", "dp"), None, None, "tensor"),
            P(("groups", "dp"), None, None, "tensor"),
        ),
        check_vma=False,
    )
```

```python
import functools

import jax
import jax.numpy as jnp
from jax import lax
from jax.experimental import pallas as pl
from jax.experimental.pallas import tpu as pltpu
from jax.sharding import PartitionSpec as P

HD = 128
LOG2E = 1.4426950408889634

dpo_beta = 0.5


def mask_bias(length, *, group, seq, prefix_rows):
    shape = (seq + prefix_rows, group * seq)
    key_index = lax.broadcasted_iota(jnp.int32, shape, 0)
    tok_index = lax.broadcasted_iota(jnp.int32, shape, 1) % seq
    in_suffix = key_index < seq
    allowed = (in_suffix & (key_index <= tok_index)) | (
        jnp.logical_not(in_suffix) & (key_index - seq < length))
    return jnp.where(allowed, 0.0, -1e30).astype(jnp.float32)


def attend_math(q_blk, og_blk, keys_pre, values_pre, keys_own, values_own, bias, coef, *, group, seq):
    scale = HD ** (-0.5)
    cot_blk = (coef * og_blk.astype(jnp.float32)).astype(jnp.bfloat16)
    q_rows = jnp.concatenate([q_blk[:, g * HD:(g + 1) * HD] for g in range(group)], 0)
    c_rows = jnp.concatenate([cot_blk[:, g * HD:(g + 1) * HD] for g in range(group)], 0)
    keys = jnp.concatenate([keys_own, keys_pre], 0)
    values = jnp.concatenate([values_own, values_pre], 0)

    nt = (((1,), (1,)), ((), ()))
    scores_t = lax.dot_general(keys, q_rows, nt, preferred_element_type=jnp.float32) * (scale * LOG2E)
    scores_t = scores_t + bias
    col_max = jnp.max(scores_t, 0, keepdims=True)
    raised = jnp.exp2(scores_t - col_max)
    inv_sum = 1.0 / jnp.sum(raised, 0, keepdims=True)
    prob_low_t = (raised * inv_sum).astype(jnp.bfloat16)
    output_t = jnp.dot(values.T, prob_low_t, preferred_element_type=jnp.float32)
    row_dot = jnp.sum(c_rows.T.astype(jnp.float32) * output_t, 0, keepdims=True)
    grad_prob_t = lax.dot_general(values, c_rows, nt, preferred_element_type=jnp.float32)
    grad_score_t = (raised * ((grad_prob_t - row_dot) * inv_sum)).astype(jnp.bfloat16)
    grad_q_t = jnp.dot(keys.T, grad_score_t, preferred_element_type=jnp.float32)
    grad_q = (scale * grad_q_t.T).astype(jnp.bfloat16)
    grad_k = scale * jnp.dot(grad_score_t, q_rows, preferred_element_type=jnp.float32)
    grad_v = jnp.dot(prob_low_t, c_rows, preferred_element_type=jnp.float32)
    return grad_q, grad_k, grad_v


def store_grads(grad_q, grad_k, grad_v, member, dq_ref, dkv_ref, dpre_ref, *, group, seq, prefix_rows, head=0):
    active = grad_k.shape[0] - seq
    kv_cols = pl.ds(pl.multiple_of(head * HD, HD), HD)
    for g in range(group):
        q_cols = pl.ds(pl.multiple_of((head * group + g) * HD, HD), HD)
        dq_ref[0, :, q_cols] = grad_q[g * seq:(g + 1) * seq]
    dkv_ref[0, 0, :, kv_cols] = grad_k[:seq].astype(jnp.bfloat16)
    dkv_ref[0, 1, :, kv_cols] = grad_v[:seq].astype(jnp.bfloat16)

    @pl.when(member == 0)
    def _():
        dpre_ref[0, 0, :active, kv_cols] = grad_k[seq:]
        dpre_ref[0, 1, :active, kv_cols] = grad_v[seq:]
        if active < prefix_rows:
            zeros = jnp.zeros((prefix_rows - active, HD), jnp.float32)
            dpre_ref[0, 0, active:, kv_cols] = zeros
            dpre_ref[0, 1, active:, kv_cols] = zeros

    @pl.when(member != 0)
    def _():
        dpre_ref[0, 0, :active, kv_cols] += grad_k[seq:]
        dpre_ref[0, 1, :active, kv_cols] += grad_v[seq:]


def attend_kernel(slots_ref, goal_ref, len_ref, coef_ref,
                  q_ref, og_ref, skv_ref, pkv_ref,
                  dq_ref, dkv_ref, dpre_ref, *, group, seq, prefix_rows):
    p = pl.program_id(0)
    member = pl.program_id(2)
    s = slots_ref[2 * p + member]
    length = len_ref[goal_ref[p]]
    bias = mask_bias(length, group=group, seq=seq, prefix_rows=prefix_rows)
    grads = attend_math(q_ref[0], og_ref[0], pkv_ref[0, 0], pkv_ref[0, 1], skv_ref[0, 0], skv_ref[0, 1],
                        bias, coef_ref[s], group=group, seq=seq)
    store_grads(*grads, member, dq_ref, dkv_ref, dpre_ref, group=group, seq=seq, prefix_rows=prefix_rows)


def pair_of(goal, goal_ref, pair_count):
    pair = 0
    for p in range(pair_count):
        pair = jnp.where(goal_ref[p] == goal, p, pair)
    return pair


def slot_kernel(me_ref, goal_ref, slots_ref, len_ref, lr_ref, q_ref, og_ref, skv_ref, pkv_ref, *rest,
                group, seq, prefix_rows, flip, pair_count, chained, seeded, low):
    if chained:
        rest = rest[2:]
    seed_ref = None
    if seeded:
        seed_ref, rest = rest[0], rest[1:]
    dq_ref, dkv_ref, dpre_ref, bias_ref = rest[:4]
    acc_ref = rest[4] if low else dpre_ref
    member = pl.program_id(0)
    goal = me_ref[0] ^ flip
    pair = pair_of(goal, goal_ref, pair_count)
    length = len_ref[goal]
    dims = dict(group=group, seq=seq, prefix_rows=prefix_rows)
    heads = skv_ref.shape[-1] // HD
    qb = group * HD

    @pl.when(member == 0)
    def _():
        bias_ref[...] = mask_bias(length, **dims)

    gap = lr_ref[slots_ref[0, pair]] - lr_ref[slots_ref[1, pair]]
    x = jnp.full((1, 128), -dpo_beta * gap, jnp.float32)
    weight = dpo_beta * (1.0 / (1.0 + jnp.exp(-x)))
    coef = jnp.where(member == 0, -weight, weight)[:, :1]
    blocks = (seq + length + 127) // 128

    def one_head(h, carry):
        q_cols = pl.ds(pl.multiple_of(h * qb, qb), qb)
        kv_cols = pl.ds(pl.multiple_of(h * HD, HD), HD)
        for used in range(1, (seq + prefix_rows + 127) // 128 + 1):
            @pl.when(blocks == used)
            def _():
                width = min(used * 128, seq + prefix_rows)
                grads = attend_math(q_ref[0, :, q_cols], og_ref[0, :, q_cols],
                                    pkv_ref[0, 0, :width - seq, kv_cols], pkv_ref[0, 1, :width - seq, kv_cols],
                                    skv_ref[0, 0, :, kv_cols], skv_ref[0, 1, :, kv_cols], bias_ref[:width], coef,
                                    group=group, seq=seq)
                store_grads(*grads, member, dq_ref, dkv_ref, acc_ref, head=h, **dims)
        return carry

    lax.fori_loop(0, heads, one_head, 0)

    if seeded:
        @pl.when(member == 1)
        def _():
            dpre_ref[...] += seed_ref[...].astype(jnp.float32)
    if low:
        @pl.when(member == 1)
        def _():
            dpre_ref[...] = acc_ref[...].astype(dpre_ref.dtype)


def attend_slot(flip, me, goals, slots, lengths, logratio, queries, out_grad, suffix_kv, prefix_one, chain,
                seed=None, low=False):
    suffix_count, seq, qwidth = queries.shape
    kv_width = suffix_kv.shape[-1]
    kv_local = kv_width // HD
    group = qwidth // kv_width
    prefix_rows = prefix_one.shape[2]
    pair_count = goals.shape[0]
    qb = group * HD

    def suffix_of(m, me_ref, goal_ref, slots_ref):
        pair = pair_of(me_ref[0] ^ flip, goal_ref, pair_count)
        return slots_ref[m, pair]

    def q_map(m, me_ref, goal_ref, slots_ref, len_ref):
        return (suffix_of(m, me_ref, goal_ref, slots_ref), 0, 0)

    def skv_map(m, me_ref, goal_ref, slots_ref, len_ref):
        return (suffix_of(m, me_ref, goal_ref, slots_ref), 0, 0, 0)

    def pkv_map(m, me_ref, goal_ref, slots_ref, len_ref):
        return (0, 0, 0, 0)

    out_shape = (
        jax.ShapeDtypeStruct((suffix_count, seq, qwidth), jnp.bfloat16),
        jax.ShapeDtypeStruct((suffix_count, 2, seq, kv_width), jnp.bfloat16),
        jax.ShapeDtypeStruct((1, 2, prefix_rows, kv_width), jnp.bfloat16 if low else jnp.float32),
    )
    in_specs = [
        pl.BlockSpec(memory_space=pltpu.SMEM),
        pl.BlockSpec((1, seq, qwidth), q_map),
        pl.BlockSpec((1, seq, qwidth), q_map),
        pl.BlockSpec((1, 2, seq, kv_width), skv_map),
        pl.BlockSpec((1, 2, prefix_rows, kv_width), pkv_map),
    ]
    operands = [logratio, queries, out_grad, suffix_kv, prefix_one]
    aliases = {}
    if chain is not None:
        in_specs += [pl.BlockSpec(memory_space=pl.ANY)] * 2
        operands += list(chain)
        aliases = {9: 0, 10: 1}
    if seed is not None:
        in_specs.append(pl.BlockSpec((1, 2, prefix_rows, kv_width), pkv_map))
        operands.append(seed)
    scratch = [pltpu.VMEM((prefix_rows + seq, group * seq), jnp.float32)]
    if low:
        scratch.append(pltpu.VMEM((1, 2, prefix_rows, kv_width), jnp.float32))
    kernel = functools.partial(slot_kernel, group=group, seq=seq, prefix_rows=prefix_rows, flip=flip,
                               pair_count=pair_count, chained=chain is not None, seeded=seed is not None,
                               low=low)
    grid_spec = pltpu.PrefetchScalarGridSpec(
        num_scalar_prefetch=4,
        grid=(2,),
        in_specs=in_specs,
        out_specs=[
            pl.BlockSpec((1, seq, qwidth), q_map),
            pl.BlockSpec((1, 2, seq, kv_width), skv_map),
            pl.BlockSpec((1, 2, prefix_rows, kv_width), pkv_map),
        ],
        scratch_shapes=scratch,
    )
    steps = 2 * kv_local
    cost = pl.CostEstimate(
        flops=steps * 2_200_000_000,
        transcendentals=steps * group * seq * (prefix_rows + seq),
        bytes_accessed=steps * (4 * seq * qb + 4 * seq * HD + 6 * prefix_rows * HD) * 2,
    )
    return pl.pallas_call(
        kernel,
        grid_spec=grid_spec,
        out_shape=out_shape,
        input_output_aliases=aliases,
        cost_estimate=cost,
        compiler_params=pltpu.CompilerParams(dimension_semantics=("arbitrary",)),
    )(me, goals, slots, lengths, *operands)


def attend_all(slots, goals, lengths, coef, queries, out_grad, suffix_kv, prefix_all):
    suffix_count, seq, qwidth = queries.shape
    kv_width = suffix_kv.shape[-1]
    kv_local = kv_width // HD
    group = qwidth // kv_width
    goal_count, _, prefix_rows, _ = prefix_all.shape
    pair_count = goals.shape[0]
    qb = group * HD

    def q_map(p, k, m, slots_ref, goal_ref, len_ref):
        return (slots_ref[2 * p + m], 0, k)

    def skv_map(p, k, m, slots_ref, goal_ref, len_ref):
        return (slots_ref[2 * p + m], 0, 0, k)

    def pkv_map(p, k, m, slots_ref, goal_ref, len_ref):
        return (goal_ref[p], 0, 0, k)

    kernel = functools.partial(attend_kernel, group=group, seq=seq, prefix_rows=prefix_rows)
    out_shape = (
        jax.ShapeDtypeStruct((suffix_count, seq, qwidth), jnp.bfloat16),
        jax.ShapeDtypeStruct((suffix_count, 2, seq, kv_width), jnp.bfloat16),
        jax.ShapeDtypeStruct((goal_count, 2, prefix_rows, kv_width), jnp.float32),
    )
    in_specs = [
        pl.BlockSpec(memory_space=pltpu.SMEM),
        pl.BlockSpec((1, seq, qb), q_map),
        pl.BlockSpec((1, seq, qb), q_map),
        pl.BlockSpec((1, 2, seq, HD), skv_map),
        pl.BlockSpec((1, 2, prefix_rows, HD), pkv_map),
    ]
    operands = [coef, queries, out_grad, suffix_kv, prefix_all]
    aliases = {}
    if pair_count < goal_count:
        in_specs.append(pl.BlockSpec(memory_space=pl.ANY))
        operands.append(jnp.zeros(out_shape[2].shape, jnp.float32))
        aliases = {3 + len(operands) - 1: 2}

        def kernel_with_zero(*refs):
            return kernel(*refs[:8], *refs[9:])
        body = kernel_with_zero
    else:
        body = kernel
    grid_spec = pltpu.PrefetchScalarGridSpec(
        num_scalar_prefetch=3,
        grid=(pair_count, kv_local, 2),
        in_specs=in_specs,
        out_specs=[
            pl.BlockSpec((1, seq, qb), q_map),
            pl.BlockSpec((1, 2, seq, HD), skv_map),
            pl.BlockSpec((1, 2, prefix_rows, HD), pkv_map),
        ],
    )
    return pl.pallas_call(
        body,
        grid_spec=grid_spec,
        out_shape=out_shape,
        input_output_aliases=aliases,
        compiler_params=pltpu.CompilerParams(
            dimension_semantics=("arbitrary", "arbitrary", "arbitrary")),
    )(slots, goals, lengths, *operands)


def shards(queries, suffix_kv, out_grad, prefix_kv, logratio, pair_slots, pair_goal, prefix_len):
    dp_size = lax.axis_size("dp")
    pair_count = pair_slots.shape[0]
    if dp_size == 4 and pair_count == dp_size:
        return pipelined(queries, suffix_kv, out_grad, prefix_kv, logratio,
                         pair_slots, pair_goal, prefix_len)
    suffix_count = queries.shape[0]
    chosen = pair_slots[:, 0]
    rejected = pair_slots[:, 1]
    positions = jnp.arange(suffix_count)
    pick_chosen = chosen[:, None] == positions[None, :]
    pick_rejected = rejected[:, None] == positions[None, :]
    ratio_chosen = jnp.sum(jnp.where(pick_chosen, logratio[None, :], 0.0), 1)
    ratio_rejected = jnp.sum(jnp.where(pick_rejected, logratio[None, :], 0.0), 1)
    weight = dpo_beta * jax.nn.sigmoid(-dpo_beta * (ratio_chosen - ratio_rejected))
    coefficient = jnp.sum(
        jnp.where(pick_rejected, weight[:, None], 0.0)
        - jnp.where(pick_chosen, weight[:, None], 0.0),
        0,
    )
    slots = pair_slots.reshape(-1).astype(jnp.int32)
    goals = pair_goal[:, 0].astype(jnp.int32)
    prefix_all = lax.all_gather(prefix_kv, "dp", axis=0, tiled=True)
    grad_q, grad_kv, partial = attend_all(
        slots, goals, prefix_len.astype(jnp.int32), coefficient,
        queries, out_grad, suffix_kv, prefix_all)
    prefix_grad = lax.psum_scatter(partial, "dp", scatter_dimension=0, tiled=True)
    return grad_q, grad_kv, prefix_grad.astype(jnp.bfloat16)


def pipelined(queries, suffix_kv, out_grad, prefix_kv, logratio, pair_slots, pair_goal, prefix_len):
    partner = [(i, i ^ 1) for i in range(4)]
    across = [(i, i ^ 2) for i in range(4)]
    pre_across = lax.ppermute(prefix_kv, "dp", across)
    pre_partner = lax.ppermute(prefix_kv, "dp", partner)
    me = lax.axis_index("dp").astype(jnp.int32).reshape(1)
    tables = (me, pair_goal.reshape(-1).astype(jnp.int32), pair_slots.T.astype(jnp.int32),
              prefix_len.astype(jnp.int32), logratio)

    def run(flip, prefix_one, chain, **extra):
        grad_q, grad_kv, partial = attend_slot(flip, *tables, queries, out_grad, suffix_kv, prefix_one, chain,
                                               **extra)
        return (grad_q, grad_kv), partial

    chain, near = run(1, pre_partner, None, low=True)
    pre_across, near = lax.optimization_barrier((pre_across, near))
    pre_relay = lax.ppermute(pre_across, "dp", partner)
    near_sent = lax.ppermute(near, "dp", partner)
    chain, cross = run(2, pre_across, chain, low=True)
    chain, relay = run(3, pre_relay, chain, low=True)
    forward = (cross.astype(jnp.float32)
               + lax.ppermute(relay, "dp", partner).astype(jnp.float32)).astype(jnp.bfloat16)
    forward, own_prefix = lax.optimization_barrier((forward, prefix_kv))
    chain, own = run(0, own_prefix, chain, seed=near_sent)
    total = own + lax.ppermute(forward, "dp", across).astype(jnp.float32)
    return chain[0], chain[1], total.astype(jnp.bfloat16)


def solution(mesh):
    return jax.shard_map(
        shards,
        mesh=mesh,
        in_specs=(
            P(("groups", "dp"), None, "tensor"),
            P(("groups", "dp"), None, None, "tensor"),
            P(("groups", "dp"), None, "tensor"),
            P(("groups", "dp"), None, None, "tensor"),
            P(("groups", "dp")),
            P(("groups", "dp"), None),
            P(("groups", "dp"), None),
            P("groups"),
        ),
        out_specs=(
            P(("groups", "dp"), None, "tensor"),
            P(("groups", "dp"), None, None, "tensor"),
            P(("groups", "dp"), None, None, "tensor"),
        ),
        check_vma=False,
    )
```

```python
import functools

import jax
import jax.numpy as jnp
from jax import lax
from jax.experimental import pallas as pl
from jax.experimental.pallas import tpu as pltpu
from jax.sharding import PartitionSpec as P

HD = 128
LOG2E = 1.4426950408889634

dpo_beta = 0.5


def mask_bias(length, *, group, seq, prefix_rows, rows=None):
    shape = (seq + prefix_rows if rows is None else rows, group * seq)
    key_index = lax.broadcasted_iota(jnp.int32, shape, 0)
    tok_index = lax.broadcasted_iota(jnp.int32, shape, 1) % seq
    in_suffix = key_index < seq
    allowed = (in_suffix & (key_index <= tok_index)) | (
        jnp.logical_not(in_suffix) & (key_index - seq < length))
    return jnp.where(allowed, 0.0, -1e30).astype(jnp.float32)


def attend_math(q_blk, og_blk, keys_pre, values_pre, keys_own, values_own, bias, coef, *, group, seq):
    scale = HD ** (-0.5)
    cot_blk = (coef * og_blk.astype(jnp.float32)).astype(jnp.bfloat16)
    q_rows = jnp.concatenate([q_blk[:, g * HD:(g + 1) * HD] for g in range(group)], 0)
    c_rows = jnp.concatenate([cot_blk[:, g * HD:(g + 1) * HD] for g in range(group)], 0)
    keys = jnp.concatenate([keys_own, keys_pre], 0)
    values = jnp.concatenate([values_own, values_pre], 0)

    nt = (((1,), (1,)), ((), ()))
    scores_t = lax.dot_general(keys, q_rows, nt, preferred_element_type=jnp.float32) * (scale * LOG2E)
    scores_t = scores_t + bias
    col_max = jnp.max(scores_t, 0, keepdims=True)
    raised = jnp.exp2(scores_t - col_max)
    inv_sum = 1.0 / jnp.sum(raised, 0, keepdims=True)
    prob_low_t = (raised * inv_sum).astype(jnp.bfloat16)
    output_t = jnp.dot(values.T, prob_low_t, preferred_element_type=jnp.float32)
    row_dot = jnp.sum(c_rows.T.astype(jnp.float32) * output_t, 0, keepdims=True)
    grad_prob_t = lax.dot_general(values, c_rows, nt, preferred_element_type=jnp.float32)
    grad_score_t = (raised * ((grad_prob_t - row_dot) * inv_sum)).astype(jnp.bfloat16)
    grad_q_t = jnp.dot(keys.T, grad_score_t, preferred_element_type=jnp.float32)
    grad_q = (scale * grad_q_t.T).astype(jnp.bfloat16)
    grad_k = scale * jnp.dot(grad_score_t, q_rows, preferred_element_type=jnp.float32)
    grad_v = jnp.dot(prob_low_t, c_rows, preferred_element_type=jnp.float32)
    return grad_q, grad_k, grad_v


def store_grads(grad_q, grad_k, grad_v, member, dq_ref, dkv_ref, dpre_ref, *, group, seq, prefix_rows, head=0):
    active = grad_k.shape[0] - seq
    kv_cols = pl.ds(pl.multiple_of(head * HD, HD), HD)
    for g in range(group):
        q_cols = pl.ds(pl.multiple_of((head * group + g) * HD, HD), HD)
        dq_ref[0, :, q_cols] = grad_q[g * seq:(g + 1) * seq]
    dkv_ref[0, 0, :, kv_cols] = grad_k[:seq].astype(jnp.bfloat16)
    dkv_ref[0, 1, :, kv_cols] = grad_v[:seq].astype(jnp.bfloat16)

    @pl.when(member == 0)
    def _():
        dpre_ref[0, 0, :active, kv_cols] = grad_k[seq:]
        dpre_ref[0, 1, :active, kv_cols] = grad_v[seq:]
        if active < prefix_rows:
            zeros = jnp.zeros((prefix_rows - active, HD), jnp.float32)
            dpre_ref[0, 0, active:, kv_cols] = zeros
            dpre_ref[0, 1, active:, kv_cols] = zeros

    @pl.when(member != 0)
    def _():
        dpre_ref[0, 0, :active, kv_cols] += grad_k[seq:]
        dpre_ref[0, 1, :active, kv_cols] += grad_v[seq:]


def attend_kernel(slots_ref, goal_ref, len_ref, coef_ref,
                  q_ref, og_ref, skv_ref, pkv_ref,
                  dq_ref, dkv_ref, dpre_ref, *, group, seq, prefix_rows):
    p = pl.program_id(0)
    member = pl.program_id(2)
    s = slots_ref[2 * p + member]
    length = len_ref[goal_ref[p]]
    bias = mask_bias(length, group=group, seq=seq, prefix_rows=prefix_rows)
    grads = attend_math(q_ref[0], og_ref[0], pkv_ref[0, 0], pkv_ref[0, 1], skv_ref[0, 0], skv_ref[0, 1],
                        bias, coef_ref[s], group=group, seq=seq)
    store_grads(*grads, member, dq_ref, dkv_ref, dpre_ref, group=group, seq=seq, prefix_rows=prefix_rows)


def pair_of(goal, goal_ref, pair_count):
    pair = 0
    for p in range(pair_count):
        pair = jnp.where(goal_ref[p] == goal, p, pair)
    return pair


def slot_kernel(me_ref, goal_ref, slots_ref, len_ref, lr_ref, q_ref, og_ref, skv_ref, pkv_ref, *rest,
                group, seq, prefix_rows, flip, pair_count, chained, seeded, low):
    if chained:
        rest = rest[2:]
    seed_ref = None
    if seeded:
        seed_ref, rest = rest[0], rest[1:]
    dq_ref, dkv_ref, dpre_ref, bias_ref = rest[:4]
    acc_ref = rest[4] if low else dpre_ref
    member = pl.program_id(0)
    goal = me_ref[0] ^ flip
    pair = pair_of(goal, goal_ref, pair_count)
    length = len_ref[goal]
    dims = dict(group=group, seq=seq, prefix_rows=prefix_rows)
    heads = skv_ref.shape[-1] // HD
    qb = group * HD

    gap = lr_ref[slots_ref[0, pair]] - lr_ref[slots_ref[1, pair]]
    x = jnp.full((1, 128), -dpo_beta * gap, jnp.float32)
    weight = dpo_beta * (1.0 / (1.0 + jnp.exp(-x)))
    coef = jnp.where(member == 0, -weight, weight)[:, :1]
    blocks = (seq + length + 127) // 128

    def one_head(h, carry):
        q_cols = pl.ds(pl.multiple_of(h * qb, qb), qb)
        kv_cols = pl.ds(pl.multiple_of(h * HD, HD), HD)
        for used in range(1, (seq + prefix_rows + 127) // 128 + 1):
            @pl.when(blocks == used)
            def _():
                width = min(used * 128, seq + prefix_rows)

                @pl.when((member == 0) & (h == 0))
                def _():
                    bias_ref[:width] = mask_bias(length, rows=width, **dims)

                grads = attend_math(q_ref[0, :, q_cols], og_ref[0, :, q_cols],
                                    pkv_ref[0, 0, :width - seq, kv_cols], pkv_ref[0, 1, :width - seq, kv_cols],
                                    skv_ref[0, 0, :, kv_cols], skv_ref[0, 1, :, kv_cols], bias_ref[:width], coef,
                                    group=group, seq=seq)
                store_grads(*grads, member, dq_ref, dkv_ref, acc_ref, head=h, **dims)
        return carry

    lax.fori_loop(0, heads, one_head, 0)

    if seeded:
        @pl.when(member == 1)
        def _():
            dpre_ref[...] += seed_ref[...]
    if low:
        @pl.when(member == 1)
        def _():
            dpre_ref[...] = acc_ref[...].astype(dpre_ref.dtype)


def attend_slot(flip, me, goals, slots, lengths, logratio, queries, out_grad, suffix_kv, prefix_one, chain,
                seed=None, low=False):
    suffix_count, seq, qwidth = queries.shape
    kv_width = suffix_kv.shape[-1]
    kv_local = kv_width // HD
    group = qwidth // kv_width
    prefix_rows = prefix_one.shape[2]
    pair_count = goals.shape[0]
    qb = group * HD

    def suffix_of(m, me_ref, goal_ref, slots_ref):
        pair = pair_of(me_ref[0] ^ flip, goal_ref, pair_count)
        return slots_ref[m, pair]

    def q_map(m, me_ref, goal_ref, slots_ref, len_ref):
        return (suffix_of(m, me_ref, goal_ref, slots_ref), 0, 0)

    def skv_map(m, me_ref, goal_ref, slots_ref, len_ref):
        return (suffix_of(m, me_ref, goal_ref, slots_ref), 0, 0, 0)

    def pkv_map(m, me_ref, goal_ref, slots_ref, len_ref):
        return (0, 0, 0, 0)

    out_shape = (
        jax.ShapeDtypeStruct((suffix_count, seq, qwidth), jnp.bfloat16),
        jax.ShapeDtypeStruct((suffix_count, 2, seq, kv_width), jnp.bfloat16),
        jax.ShapeDtypeStruct((1, 2, prefix_rows, kv_width), jnp.bfloat16 if low else jnp.float32),
    )
    in_specs = [
        pl.BlockSpec(memory_space=pltpu.SMEM),
        pl.BlockSpec((1, seq, qwidth), q_map),
        pl.BlockSpec((1, seq, qwidth), q_map),
        pl.BlockSpec((1, 2, seq, kv_width), skv_map),
        pl.BlockSpec((1, 2, prefix_rows, kv_width), pkv_map),
    ]
    operands = [logratio, queries, out_grad, suffix_kv, prefix_one]
    aliases = {}
    if chain is not None:
        in_specs += [pl.BlockSpec(memory_space=pl.ANY)] * 2
        operands += list(chain)
        aliases = {9: 0, 10: 1}
    if seed is not None:
        in_specs.append(pl.BlockSpec((1, 2, prefix_rows, kv_width), pkv_map))
        operands.append(seed)
    scratch = [pltpu.VMEM((prefix_rows + seq, group * seq), jnp.float32)]
    if low:
        scratch.append(pltpu.VMEM((1, 2, prefix_rows, kv_width), jnp.float32))
    kernel = functools.partial(slot_kernel, group=group, seq=seq, prefix_rows=prefix_rows, flip=flip,
                               pair_count=pair_count, chained=chain is not None, seeded=seed is not None,
                               low=low)
    grid_spec = pltpu.PrefetchScalarGridSpec(
        num_scalar_prefetch=4,
        grid=(2,),
        in_specs=in_specs,
        out_specs=[
            pl.BlockSpec((1, seq, qwidth), q_map),
            pl.BlockSpec((1, 2, seq, kv_width), skv_map),
            pl.BlockSpec((1, 2, prefix_rows, kv_width), pkv_map),
        ],
        scratch_shapes=scratch,
    )
    steps = 2 * kv_local
    cost = pl.CostEstimate(
        flops=steps * 2_200_000_000,
        transcendentals=steps * group * seq * (prefix_rows + seq),
        bytes_accessed=steps * (4 * seq * qb + 4 * seq * HD + 6 * prefix_rows * HD) * 2,
    )
    return pl.pallas_call(
        kernel,
        grid_spec=grid_spec,
        out_shape=out_shape,
        input_output_aliases=aliases,
        cost_estimate=cost,
        compiler_params=pltpu.CompilerParams(dimension_semantics=("arbitrary",)),
    )(me, goals, slots, lengths, *operands)


def attend_all(slots, goals, lengths, coef, queries, out_grad, suffix_kv, prefix_all):
    suffix_count, seq, qwidth = queries.shape
    kv_width = suffix_kv.shape[-1]
    kv_local = kv_width // HD
    group = qwidth // kv_width
    goal_count, _, prefix_rows, _ = prefix_all.shape
    pair_count = goals.shape[0]
    qb = group * HD

    def q_map(p, k, m, slots_ref, goal_ref, len_ref):
        return (slots_ref[2 * p + m], 0, k)

    def skv_map(p, k, m, slots_ref, goal_ref, len_ref):
        return (slots_ref[2 * p + m], 0, 0, k)

    def pkv_map(p, k, m, slots_ref, goal_ref, len_ref):
        return (goal_ref[p], 0, 0, k)

    kernel = functools.partial(attend_kernel, group=group, seq=seq, prefix_rows=prefix_rows)
    out_shape = (
        jax.ShapeDtypeStruct((suffix_count, seq, qwidth), jnp.bfloat16),
        jax.ShapeDtypeStruct((suffix_count, 2, seq, kv_width), jnp.bfloat16),
        jax.ShapeDtypeStruct((goal_count, 2, prefix_rows, kv_width), jnp.float32),
    )
    in_specs = [
        pl.BlockSpec(memory_space=pltpu.SMEM),
        pl.BlockSpec((1, seq, qb), q_map),
        pl.BlockSpec((1, seq, qb), q_map),
        pl.BlockSpec((1, 2, seq, HD), skv_map),
        pl.BlockSpec((1, 2, prefix_rows, HD), pkv_map),
    ]
    operands = [coef, queries, out_grad, suffix_kv, prefix_all]
    aliases = {}
    if pair_count < goal_count:
        in_specs.append(pl.BlockSpec(memory_space=pl.ANY))
        operands.append(jnp.zeros(out_shape[2].shape, jnp.float32))
        aliases = {3 + len(operands) - 1: 2}

        def kernel_with_zero(*refs):
            return kernel(*refs[:8], *refs[9:])
        body = kernel_with_zero
    else:
        body = kernel
    grid_spec = pltpu.PrefetchScalarGridSpec(
        num_scalar_prefetch=3,
        grid=(pair_count, kv_local, 2),
        in_specs=in_specs,
        out_specs=[
            pl.BlockSpec((1, seq, qb), q_map),
            pl.BlockSpec((1, 2, seq, HD), skv_map),
            pl.BlockSpec((1, 2, prefix_rows, HD), pkv_map),
        ],
    )
    return pl.pallas_call(
        body,
        grid_spec=grid_spec,
        out_shape=out_shape,
        input_output_aliases=aliases,
        compiler_params=pltpu.CompilerParams(
            dimension_semantics=("arbitrary", "arbitrary", "arbitrary")),
    )(slots, goals, lengths, *operands)


def shards(queries, suffix_kv, out_grad, prefix_kv, logratio, pair_slots, pair_goal, prefix_len):
    dp_size = lax.axis_size("dp")
    pair_count = pair_slots.shape[0]
    if dp_size == 4 and pair_count == dp_size:
        return pipelined(queries, suffix_kv, out_grad, prefix_kv, logratio,
                         pair_slots, pair_goal, prefix_len)
    suffix_count = queries.shape[0]
    chosen = pair_slots[:, 0]
    rejected = pair_slots[:, 1]
    positions = jnp.arange(suffix_count)
    pick_chosen = chosen[:, None] == positions[None, :]
    pick_rejected = rejected[:, None] == positions[None, :]
    ratio_chosen = jnp.sum(jnp.where(pick_chosen, logratio[None, :], 0.0), 1)
    ratio_rejected = jnp.sum(jnp.where(pick_rejected, logratio[None, :], 0.0), 1)
    weight = dpo_beta * jax.nn.sigmoid(-dpo_beta * (ratio_chosen - ratio_rejected))
    coefficient = jnp.sum(
        jnp.where(pick_rejected, weight[:, None], 0.0)
        - jnp.where(pick_chosen, weight[:, None], 0.0),
        0,
    )
    slots = pair_slots.reshape(-1).astype(jnp.int32)
    goals = pair_goal[:, 0].astype(jnp.int32)
    prefix_all = lax.all_gather(prefix_kv, "dp", axis=0, tiled=True)
    grad_q, grad_kv, partial = attend_all(
        slots, goals, prefix_len.astype(jnp.int32), coefficient,
        queries, out_grad, suffix_kv, prefix_all)
    prefix_grad = lax.psum_scatter(partial, "dp", scatter_dimension=0, tiled=True)
    return grad_q, grad_kv, prefix_grad.astype(jnp.bfloat16)


def pipelined(queries, suffix_kv, out_grad, prefix_kv, logratio, pair_slots, pair_goal, prefix_len):
    partner = [(i, i ^ 1) for i in range(4)]
    across = [(i, i ^ 2) for i in range(4)]
    pre_across = lax.ppermute(prefix_kv, "dp", across)
    pre_partner = lax.ppermute(prefix_kv, "dp", partner)
    me = lax.axis_index("dp").astype(jnp.int32).reshape(1)
    tables = (me, pair_goal.reshape(-1).astype(jnp.int32), pair_slots.T.astype(jnp.int32),
              prefix_len.astype(jnp.int32), logratio)

    def run(flip, prefix_one, chain, **extra):
        grad_q, grad_kv, partial = attend_slot(flip, *tables, queries, out_grad, suffix_kv, prefix_one, chain,
                                               **extra)
        return (grad_q, grad_kv), partial

    chain, near = run(1, pre_partner, None)
    pre_across, near = lax.optimization_barrier((pre_across, near))
    pre_relay = lax.ppermute(pre_across, "dp", partner)
    near_sent = lax.ppermute(near, "dp", partner)
    chain, cross = run(2, pre_across, chain)
    chain, relay = run(3, pre_relay, chain, low=True)
    forward = (cross + lax.ppermute(relay, "dp", partner).astype(jnp.float32)).astype(jnp.bfloat16)
    forward, own_prefix = lax.optimization_barrier((forward, prefix_kv))
    chain, own = run(0, own_prefix, chain, seed=near_sent)
    total = own + lax.ppermute(forward, "dp", across).astype(jnp.float32)
    return chain[0], chain[1], total.astype(jnp.bfloat16)


def solution(mesh):
    return jax.shard_map(
        shards,
        mesh=mesh,
        in_specs=(
            P(("groups", "dp"), None, "tensor"),
            P(("groups", "dp"), None, None, "tensor"),
            P(("groups", "dp"), None, "tensor"),
            P(("groups", "dp"), None, None, "tensor"),
            P(("groups", "dp")),
            P(("groups", "dp"), None),
            P(("groups", "dp"), None),
            P("groups"),
        ),
        out_specs=(
            P(("groups", "dp"), None, "tensor"),
            P(("groups", "dp"), None, None, "tensor"),
            P(("groups", "dp"), None, None, "tensor"),
        ),
        check_vma=False,
    )
```
